32 devices in a mesh: req: 8 (over z, y), tp: 4 (over x, core).
Axes of the slice: x: 2, y: 2, z: 4, core: 2. Of those that a mesh axis runs over, the one named last changes fastest.
Arguments:
- hidden_in: bfloat16 [192, 1536], P('req', 'tp'), may hold values from -12 to 12
- queries: bfloat16 [192, 1536], P('req', 'tp'), may hold values from -6 to 6
- fresh_key_value: bfloat16 [192, 2, 256], P('req'), may hold values from -120 to 120
- positions: int32 [192], P('req'), may hold values from 0 to 4095
- lengths: int32 [8, 24], P('req'), may hold values from 1 to 2048, 3072 in all within a row
- cache: bfloat16 [24576, 2, 2, 128], P(('req', 'tp')), may hold values from -160 to 160
- out_proj: bfloat16 [1536, 1536], P('tp'), may hold values from -0.59765625 to 0.59765625
- norm_gain: float32 [1536], replicated, may hold values from 0.1 to 1.9
- expert_ids: int32 [192, 4], P('req'), may hold values from 0 to 31, all different within a row; in each aligned block of 24 rows (0 to 23, 24 to 47, ...) at most 8 rows name the same one
- router_weights: float32 [192, 4], P('req'), may hold values from 0.05 to 0.5
- gate_up: bfloat16 [32, 2, 1536, 768], P('req', None, None, 'tp'), may hold values from -0.15625 to 0.15625
- down: bfloat16 [32, 768, 1536], P('req', 'tp'), may hold values from -0.21875 to 0.21875
Outputs:
- layer_out: bfloat16 [192, 1536], P('req', 'tp')
The draws below stay inside these ranges and needn't reach their ends.
Inputs may be any that keep to these rules, and one draw needn't show every extreme that they name: `lengths`: each row sums to 3072. `expert_ids`: each row names 4 different experts; among the 24 aligned rows of one request group no expert is named by more than 8 rows, a bound that some block reaches.
All inputs are finite; a program needn't handle non-finite values.
Results may differ from the reference program's by a relative error of at most 0.012.
The reference program's roundings to bfloat16 on the way count: a program that leaves them out, or rounds other values in their place, can miss the bound.
Values may be sent and summed in bfloat16 or wider, within the bound.
No kernel may reach another device: no remote copies, remote signals or barrier semaphores. Data moves between devices by JAX's collectives and lax.ppermute only.
A program may use at most 64 MiB of HBM per device.

```python
import math
import jax
import jax.numpy as jnp
import numpy as np
from jax import lax

D = 1536
QUERY_HEAD_COUNT = 12
KEY_VALUE_HEADS = 2
HEAD_WIDTH = 128
EXPERTS = 32
FFE = 768
TOPK = 4
REQUESTS_IN_GROUP = 24
LONG = 2048
CACHE_PER_GROUP = 3072
CAP = 8
SPLIT = 1
REQUEST_TOTAL = 192
CACHE_TOTAL = 24576
N_REQ = 8
N_TP = 4


def draw_hidden_in(key, part):
    random_subkey = jax.random.fold_in(key, 23)
    column_share = jnp.arange(D, dtype=jnp.float32) / (D - 1)
    column_scale = 0.5 * jnp.exp(jnp.log(4.0) * column_share)
    entries = jnp.clip(jax.random.normal(random_subkey, (REQUEST_TOTAL, D), jnp.float32), -6.0, 6.0)
    return (entries * column_scale[None, :]).astype(jnp.bfloat16)


def query_values(key):
    random_subkey = jax.random.fold_in(key, 11)
    return jnp.clip(jax.random.normal(random_subkey, (REQUEST_TOTAL, QUERY_HEAD_COUNT * HEAD_WIDTH), jnp.float32), -6.0, 6.0)


def draw_queries(key, part):
    return query_values(key).astype(jnp.bfloat16)


def draw_positions(key, part):
    return jax.random.randint(jax.random.fold_in(key, 13), (REQUEST_TOTAL,), 0, 4096, dtype=jnp.int32)


def draw_fresh_key_value(key, part):
    random_subkey = jax.random.fold_in(key, 17)
    return jnp.clip(jax.random.normal(random_subkey, (REQUEST_TOTAL, 2, KEY_VALUE_HEADS * HEAD_WIDTH), jnp.float32), -6.0, 6.0).astype(jnp.bfloat16)


def draw_cache(key, part):
    random_subkey = jax.random.fold_in(key, 19)
    full_shape = (CACHE_TOTAL, 2, KEY_VALUE_HEADS, HEAD_WIDTH)
    return jnp.clip(jax.random.normal(random_subkey, full_shape, jnp.float32), -6.0, 6.0).astype(jnp.bfloat16)


def block_levels(rng, dims, cuts, low, high):
    factor_of = 1.0
    for dim, blocks in cuts:
        steps = jax.random.uniform(jax.random.fold_in(jax.random.fold_in(rng, 6), dim), (blocks,), jnp.float32, low / len(cuts), high / len(cuts))
        factor_of = factor_of * jnp.repeat(jnp.exp(steps), dims[dim] // blocks).reshape((-1,) + (1,) * (len(dims) - 1 - dim))
    return factor_of


def profile(count, total, limit, skew):
    loads = [(1 << 20) // math.isqrt(standing ** skew) + 1 for standing in range(2, count + 1)]
    surplus, holding = total - limit - (count - 1), [1] * (count - 1)
    while surplus > 0:
        candidates = [i for i in range(count - 1) if holding[i] < limit]
        whole, remaining = sum([loads[i] for i in candidates]), surplus
        for i in candidates:
            extra = min(limit - holding[i], max(1, remaining * loads[i] // whole), surplus)
            holding[i] = holding[i] + extra
            surplus = surplus - extra
    return np.array([limit] + holding)


def ragged(own_key, amount, total, limit, lean):
    if amount == 2:
        one = jax.random.randint(own_key, (), max(1, total - limit), min(limit, total - 1) + 1)
        return jnp.stack([one, total - one])
    tallies = jnp.asarray(profile(amount, total, limit, lean), jnp.int32)
    couples = (amount - 1) // 2
    donor, taker = tallies[1:1 + 2 * couples:2], tallies[2:2 + 2 * couples:2]
    slack = jnp.minimum(donor - 1, limit - taker)
    shifted = jax.random.randint(jax.random.fold_in(own_key, 1), (couples,), 0, 1 << 20) % (slack + 1)
    tallies = tallies.at[1:1 + 2 * couples:2].set(donor - shifted).at[2:2 + 2 * couples:2].set(taker + shifted)
    return tallies[jax.random.permutation(jax.random.fold_in(own_key, 2), amount)]


def assign_block(stream_key, own, number, rows, amount, top, reach, slope):
    sequence = jax.random.permutation(stream_key, amount)
    packed, usual = load_shares(amount, rows * top, reach, slope, True), load_shares(amount, rows * top, reach, slope, False)
    places = jnp.arange(amount)

    def named(tallies, offset_by):
        used = int((tallies > 0).sum())
        fixed = max(1, used // 4)
        shifted = fixed + (places - fixed + offset_by * (used - fixed)) % max(1, amount - fixed)
        return jnp.zeros((amount,), jnp.int32).at[sequence[jnp.where(places < fixed, places, shifted)]].set(jnp.asarray(tallies, jnp.int32))

    tallies = jnp.where(number % 4 == 0, named(packed, number // 4), named(usual, number - number // 4 - 1))
    mixed = jax.random.permutation(jax.random.fold_in(own, 3), amount)
    donor, sink = mixed[0:amount // 2 * 2:2], mixed[1:amount // 2 * 2:2]
    room = jnp.minimum(tallies[donor] - 1, reach - tallies[sink]) // 2
    room = jnp.where((donor == sequence[0]) | (sink == sequence[0]) | (tallies[sink] == 0), 0, jnp.maximum(room, 0))
    shifted = jax.random.randint(jax.random.fold_in(own, 4), (amount // 2,), 0, 1 << 20) % (room + 1)
    tallies = tallies.at[donor].add(-shifted).at[sink].add(shifted)
    members = jnp.searchsorted(jnp.cumsum(tallies), jnp.arange(rows * top), side="right").astype(jnp.int32)
    grid = members.reshape(top, rows).T
    grid = grid[jax.random.permutation(jax.random.fold_in(own, 1), rows)]
    offset_by = jax.random.randint(jax.random.fold_in(own, 2), (rows, 1), 0, top)
    return jnp.take_along_axis(grid, (jnp.arange(top)[None, :] + offset_by) % top, axis=1)


def load_shares(amount, total, bound, lean, full):
    weights = [(1 << 20) // math.isqrt(standing ** lean) + 1 for standing in range(1, amount + 1)]
    largest = bound if full else min(bound, max(-(-total // amount), total * weights[0] // sum(weights)))
    least = 1 if total - largest >= amount - 1 else 0
    holding, spare = [largest] + [least] * (amount - 1), total - largest - least * (amount - 1)
    while spare > 0:
        free = [i for i in range(1, amount) if holding[i] < largest] or [i for i in range(1, amount) if holding[i] < bound]
        mass, remaining = sum([weights[i] for i in free]), spare
        for i in free:
            more = min(bound - holding[i], max(1, remaining * weights[i] // mass), spare)
            holding[i] = holding[i] + more
            spare = spare - more
    return np.array(holding)


def normal_values(stream_key, dims, deviation, bound, split=(), held_as=jnp.bfloat16):
    values = jax.random.normal(stream_key, dims, jnp.float32) * deviation
    if len(split) > 0:
        values = block_levels(stream_key, dims, split, -0.22, 0.18) * values
    return jnp.clip(values, min=-bound, max=bound).astype(held_as)


def setup_inputs(seed: int = 0) -> dict:
    key_of = jax.random.split(jax.random.key(seed), 13)
    hidden_in = draw_hidden_in(jax.random.fold_in(key_of[12], 71), 0)
    queries = draw_queries(jax.random.fold_in(key_of[12], 71), 0)
    fresh_key_value = draw_fresh_key_value(jax.random.fold_in(key_of[12], 71), 0)
    positions = draw_positions(jax.random.fold_in(key_of[12], 71), 0)
    lengths = jax.vmap(lambda own: ragged(own, REQUESTS_IN_GROUP, CACHE_PER_GROUP, LONG, 2))(jax.random.split(key_of[4], N_REQ)).reshape((N_REQ, REQUESTS_IN_GROUP)).astype(jnp.int32)
    cache = draw_cache(jax.random.fold_in(key_of[12], 71), 0)
    out_proj = normal_values(key_of[6], (QUERY_HEAD_COUNT * HEAD_WIDTH, D), 0.1, 0.59765625, ((0, 4),))
    norm_gain = jnp.clip(1.0 + 0.18 * jax.random.normal(key_of[7], (D,), jnp.float32), 0.1, 1.9)
    expert_ids_keys = jax.random.split(jax.random.fold_in(key_of[8], 1), REQUEST_TOTAL // REQUESTS_IN_GROUP)
    expert_ids_turns = jax.random.permutation(jax.random.fold_in(key_of[8], 3), REQUEST_TOTAL // REQUESTS_IN_GROUP)
    expert_ids = jax.vmap(lambda own, number: assign_block(jax.random.fold_in(key_of[8], 2), own, number, REQUESTS_IN_GROUP, EXPERTS, TOPK, CAP, 1))(expert_ids_keys, expert_ids_turns).reshape((REQUEST_TOTAL, TOPK))
    router_weights = jnp.clip(0.05 + 0.45 * jax.random.uniform(key_of[9], (REQUEST_TOTAL, TOPK), jnp.float32) ** block_levels(key_of[9], (REQUEST_TOTAL, TOPK), ((0, 8),), -0.2, 0.2), 0.05, 0.5)
    gate_up = normal_values(key_of[10], (SPLIT * EXPERTS, 2, D, FFE), D ** -0.5, 0.15625, ((0, 8), (3, 4)))
    down = normal_values(key_of[11], (SPLIT * EXPERTS, FFE, D), FFE ** -0.5, 0.21875, ((0, 8), (1, 4)))
    return dict(hidden_in=hidden_in, queries=queries, fresh_key_value=fresh_key_value, positions=positions, lengths=lengths, cache=cache, out_proj=out_proj, norm_gain=norm_gain, expert_ids=expert_ids, router_weights=router_weights, gate_up=gate_up, down=down)


rope_base = 1000000.0
norm_eps = 1e-06

def apply_rotary_heads(values, positions, head_size):
    half_size = head_size // 2
    exponents = jnp.arange(half_size, dtype=jnp.float32) * (2.0 / head_size)
    inverse_freq = jnp.power(jnp.float32(rope_base), -exponents)
    angles = positions.astype(jnp.float32)[:, None] * inverse_freq[None, :]
    cosine = jnp.cos(angles)[:, None, :]
    sine = jnp.sin(angles)[:, None, :]
    first_half = values[..., :half_size]
    second_half = values[..., half_size:]
    return jnp.concatenate([first_half * cosine - second_half * sine, second_half * cosine + first_half * sine], axis=-1)

def attend_request_group(arguments):
    q_group, length_row, cache_group, own_group, value_new = arguments
    request_count = q_group.shape[0]
    head_count = q_group.shape[1]
    head_size = q_group.shape[2]
    kv_count = cache_group.shape[2]
    request_group_size = head_count // kv_count
    segment_ends = jnp.cumsum(length_row, dtype=jnp.int32)
    cache_spots = jnp.arange(cache_group.shape[0], dtype=jnp.int32)
    owners = lax.optimization_barrier(jnp.sum((cache_spots[:, None] >= segment_ends[None, :]).astype(jnp.int32), axis=1))
    spread = q_group[owners].astype(jnp.float32).reshape(-1, kv_count, request_group_size, head_size)
    scores = jnp.einsum('pkgd,pkd->pkg', spread, cache_group[:, 0].astype(jnp.float32)).reshape(-1, head_count) * head_size ** (-0.5)
    highest = jnp.maximum(jax.ops.segment_max(scores, owners, request_count), own_group)
    cache_weights = jnp.exp(scores - highest[owners])
    own_weight = jnp.exp(own_group - highest)
    totals = jax.ops.segment_sum(cache_weights, owners, request_count) + own_weight
    weighted = cache_weights.reshape(-1, kv_count, request_group_size, 1) * cache_group[:, 1].astype(jnp.float32)[:, :, None, :]
    summed = jax.ops.segment_sum(weighted.reshape(-1, head_count * head_size), owners, request_count)
    own_term = own_weight.reshape(request_count, kv_count, request_group_size, 1) * value_new.astype(jnp.float32)[:, :, None, :]
    summed = summed.reshape(request_count, head_count, head_size) + own_term.reshape(request_count, head_count, head_size)
    return (summed / totals[:, :, None]).astype(jnp.bfloat16)

def reference(hidden_in, queries, fresh_key_value, positions, lengths, cache, out_proj, norm_gain, expert_ids, router_weights, gate_up, down):
    request_group_size = QUERY_HEAD_COUNT // KEY_VALUE_HEADS
    score_scaling = HEAD_WIDTH ** (-0.5)
    request_group_count = REQUEST_TOTAL // REQUESTS_IN_GROUP
    query_rotated = apply_rotary_heads(queries.reshape(REQUEST_TOTAL, QUERY_HEAD_COUNT, HEAD_WIDTH).astype(jnp.float32), positions, HEAD_WIDTH).astype(jnp.bfloat16)
    key_rotated = apply_rotary_heads(fresh_key_value[:, 0].reshape(REQUEST_TOTAL, KEY_VALUE_HEADS, HEAD_WIDTH).astype(jnp.float32), positions, HEAD_WIDTH).astype(jnp.bfloat16)
    value_fresh = fresh_key_value[:, 1].reshape(REQUEST_TOTAL, KEY_VALUE_HEADS, HEAD_WIDTH)
    self_token_scores = jnp.einsum('tsjp,tsp->tsj', query_rotated.reshape(REQUEST_TOTAL, KEY_VALUE_HEADS, request_group_size, HEAD_WIDTH).astype(jnp.float32), key_rotated.astype(jnp.float32)).reshape(REQUEST_TOTAL, QUERY_HEAD_COUNT) * score_scaling
    attention_output = lax.map(attend_request_group, (query_rotated.reshape(request_group_count, REQUESTS_IN_GROUP, QUERY_HEAD_COUNT, HEAD_WIDTH), lengths, cache.reshape(request_group_count, CACHE_PER_GROUP, 2, KEY_VALUE_HEADS, HEAD_WIDTH), self_token_scores.reshape(request_group_count, REQUESTS_IN_GROUP, QUERY_HEAD_COUNT), value_fresh.reshape(request_group_count, REQUESTS_IN_GROUP, KEY_VALUE_HEADS, HEAD_WIDTH)))
    attention_output = attention_output.reshape(REQUEST_TOTAL, QUERY_HEAD_COUNT * HEAD_WIDTH)
    residual = hidden_in.astype(jnp.float32) + jnp.dot(attention_output, out_proj, preferred_element_type=jnp.float32)
    mean_square = lax.optimization_barrier(jnp.mean(residual * residual, axis=1, keepdims=True))
    normed = (residual * lax.rsqrt(mean_square + norm_eps) * norm_gain[None, :]).astype(jnp.bfloat16)
    slots_all = request_group_count * CAP
    unit_groups = FFE // N_TP

    def expert_pass(accumulated, block):
        replica = block // EXPERTS
        expert = block % EXPERTS
        gate_whole = lax.dynamic_index_in_dim(gate_up, block, 0, keepdims=False)
        down_whole = lax.dynamic_index_in_dim(down, block, 0, keepdims=False)
        chosen = lax.optimization_barrier(jnp.sum(jnp.where(expert_ids == expert, router_weights, 0.0), axis=1))
        named = jnp.any(expert_ids == expert, axis=1)
        named_group = named.astype(jnp.int32).reshape(request_group_count, REQUESTS_IN_GROUP)
        slot_in_group = (jnp.cumsum(named_group, axis=1, dtype=jnp.int32) - named_group).reshape(REQUEST_TOTAL)
        used = named & (slot_in_group % SPLIT == replica)
        picks = jnp.nonzero(used, size=slots_all, fill_value=0)[0].astype(jnp.int32)
        live = jnp.arange(slots_all, dtype=jnp.int32) < jnp.sum(used.astype(jnp.int32))
        inputs = normed[picks]
        gate_part = jnp.dot(inputs, gate_whole[0], preferred_element_type=jnp.float32)
        up_part = jnp.dot(inputs, gate_whole[1], preferred_element_type=jnp.float32)
        activation = (jnp.maximum(gate_part, 0.0) * up_part).astype(jnp.bfloat16)
        grouped = jnp.einsum('cgf,gfd->cgd', activation.reshape(slots_all, N_TP, unit_groups).astype(jnp.float32), down_whole.reshape(N_TP, unit_groups, D).astype(jnp.float32))
        rounded_down = lax.optimization_barrier(grouped.astype(jnp.bfloat16)).astype(jnp.float32)
        contribution = lax.optimization_barrier(jnp.sum(rounded_down, axis=1)) * jnp.where(live, chosen[picks], 0.0)[:, None]
        return (accumulated.at[picks].add(contribution), None)
    moe_total, unused = lax.scan(expert_pass, jnp.zeros((REQUEST_TOTAL, D), jnp.float32), jnp.arange(SPLIT * EXPERTS, dtype=jnp.int32))
    return (residual + moe_total).astype(jnp.bfloat16)
```

```python
import jax
import jax.numpy as jnp
from jax import lax
from jax.sharding import PartitionSpec as P

EXPERTS = 32


rope_base = 1000000.0
norm_eps = 1e-06
neg_floor = -1e30


def apply_rotary_heads(values, positions, head_size):
    half_size = head_size // 2
    exponents = jnp.arange(half_size, dtype=jnp.float32) * (2.0 / head_size)
    inverse_freq = jnp.power(jnp.float32(rope_base), -exponents)
    angles = positions.astype(jnp.float32)[:, None] * inverse_freq[None, :]
    cosine = jnp.cos(angles)[:, None, :]
    sine = jnp.sin(angles)[:, None, :]
    first_half = values[..., :half_size]
    second_half = values[..., half_size:]
    return jnp.concatenate(
        [first_half * cosine - second_half * sine, second_half * cosine + first_half * sine],
        axis=-1,
    )


def per_device(
    hidden_in,
    queries,
    fresh_key_value,
    positions,
    lengths,
    cache,
    out_proj,
    norm_gain,
    expert_ids,
    router_weights,
    gate_up,
    down,
):
    tp_count = lax.axis_size("tp")
    req_count = lax.axis_size("req")
    tp_index = lax.axis_index("tp")
    req_index = lax.axis_index("req")
    row_count = hidden_in.shape[0]
    head_size = cache.shape[3]
    kv_count = cache.shape[2]
    own_heads = queries.shape[1] // head_size
    head_count = own_heads * tp_count
    request_group_size = head_count // kv_count
    score_scaling = head_size ** (-0.5)
    model_width = norm_gain.shape[0]
    own_width = hidden_in.shape[1]
    first_head = tp_index * own_heads
    span_rows = cache.shape[0]

    q_local = apply_rotary_heads(
        queries.reshape(row_count, own_heads, head_size).astype(jnp.float32), positions, head_size
    ).astype(jnp.bfloat16)
    packed = jnp.stack([q_local.reshape(row_count, own_width), hidden_in], axis=0)
    gathered = lax.all_gather(packed, "tp", axis=0)
    q_all = jnp.transpose(gathered[:, 0], (1, 0, 2)).reshape(
        row_count, kv_count, request_group_size, head_size
    )
    hidden_full = jnp.transpose(gathered[:, 1], (1, 0, 2)).reshape(row_count, model_width)

    k_new = apply_rotary_heads(
        fresh_key_value[:, 0].reshape(row_count, kv_count, head_size).astype(jnp.float32),
        positions,
        head_size,
    ).astype(jnp.bfloat16)
    value_fresh = fresh_key_value[:, 1].reshape(row_count, kv_count, head_size)
    own_score = (
        jnp.einsum("rcgd,rcd->rcg", q_all, k_new, preferred_element_type=jnp.float32)
        * score_scaling
    )

    segment_ends = jnp.cumsum(lengths[0], dtype=jnp.int32)
    segment_starts = segment_ends - lengths[0]
    cache_spots = tp_index * span_rows + jnp.arange(span_rows, dtype=jnp.int32)
    mask = (cache_spots[None, :] >= segment_starts[:, None]) & (
        cache_spots[None, :] < segment_ends[:, None]
    )
    mask = mask[:, None, None, :]
    keys = cache[:, 0]
    values = cache[:, 1]
    scores = (
        jnp.einsum("rcgd,jcd->rcgj", q_all, keys, preferred_element_type=jnp.float32)
        * score_scaling
    )
    scores = jnp.where(mask, scores, neg_floor)
    highest_local = jnp.max(scores, axis=3)
    weights = jnp.where(mask, jnp.exp(scores - highest_local[..., None]), 0.0)
    totals_local = jnp.sum(weights, axis=3)
    sums_local = jnp.einsum(
        "rcgj,jcd->rcgd",
        weights,
        values.astype(jnp.float32),
        precision=lax.Precision.HIGHEST,
        preferred_element_type=jnp.float32,
    )
    states = jnp.concatenate(
        [highest_local[..., None], totals_local[..., None], sums_local], axis=3
    ).reshape(row_count, head_count, head_size + 2)
    all_states = lax.all_gather(states, "tp", axis=0)
    all_states = lax.dynamic_slice_in_dim(all_states, first_head, own_heads, 2)
    parts_highest = all_states[..., 0]
    parts_totals = all_states[..., 1]
    parts_sums = all_states[..., 2:]
    own_slice = lax.dynamic_slice_in_dim(own_score.reshape(row_count, head_count), first_head, own_heads, 1)
    top_score = jnp.maximum(jnp.max(parts_highest, axis=0), own_slice)
    factors = jnp.exp(parts_highest - top_score[None])
    own_part = jnp.exp(own_slice - top_score)
    head_kv = (first_head + jnp.arange(own_heads, dtype=jnp.int32)) // request_group_size
    own_values = jnp.take(value_fresh, head_kv, axis=1).astype(jnp.float32)
    totals = jnp.sum(parts_totals * factors, axis=0) + own_part
    summed = jnp.sum(parts_sums * factors[..., None], axis=0) + own_values * own_part[..., None]
    attention_output = (summed / totals[..., None]).astype(jnp.bfloat16).reshape(
        row_count, own_heads * head_size
    )

    partial_proj = jnp.dot(attention_output, out_proj, preferred_element_type=jnp.float32)
    projected = lax.psum(partial_proj, "tp")
    residual = hidden_full.astype(jnp.float32) + projected
    mean_square = jnp.mean(residual * residual, axis=1, keepdims=True)
    normed = (residual * lax.rsqrt(mean_square + norm_eps) * norm_gain[None, :]).astype(jnp.bfloat16)

    local_count = gate_up.shape[0]
    block_total = local_count * req_count
    split_count = max(1, block_total // EXPERTS)
    expert_range = jnp.arange(EXPERTS, dtype=jnp.int32)
    member = jnp.any(expert_ids[:, :, None] == expert_range[None, None, :], axis=1)
    member_int = member.astype(jnp.int32)
    slot_of = jnp.cumsum(member_int, axis=0, dtype=jnp.int32) - member_int
    slot_taken = jnp.take_along_axis(slot_of, expert_ids, axis=1)
    block_taken = (slot_taken % split_count) * EXPERTS + expert_ids
    block_range = jnp.arange(block_total, dtype=jnp.int32)
    block_weights = jnp.sum(
        jnp.where(block_taken[:, :, None] == block_range[None, None, :], router_weights[:, :, None], 0.0),
        axis=1,
    )

    rows_all = lax.all_gather(normed, "req", axis=0, tiled=True)
    weights_all = lax.all_gather(block_weights, "req", axis=0, tiled=True)
    weights_own = lax.dynamic_slice_in_dim(weights_all, req_index * local_count, local_count, 1)

    mixed = jnp.zeros((rows_all.shape[0], model_width), jnp.float32)
    for local_block in range(local_count):
        gate_part = jnp.dot(rows_all, gate_up[local_block, 0], preferred_element_type=jnp.float32)
        up_part = jnp.dot(rows_all, gate_up[local_block, 1], preferred_element_type=jnp.float32)
        activation = (jnp.maximum(gate_part, 0.0) * up_part).astype(jnp.bfloat16)
        produced = jnp.dot(activation, down[local_block], preferred_element_type=jnp.float32)
        produced = produced.astype(jnp.bfloat16).astype(jnp.float32)
        mixed = mixed + weights_own[:, local_block : local_block + 1] * produced

    mixed = mixed.reshape(req_count, row_count, tp_count, own_width)
    mixed = jnp.transpose(mixed, (0, 2, 1, 3)).reshape(req_count * tp_count, row_count, own_width)
    mixed = lax.psum_scatter(mixed, ("req", "tp"), scatter_dimension=0, tiled=True)
    mixed = mixed.reshape(row_count, own_width)
    residual_own = lax.dynamic_slice_in_dim(residual, tp_index * own_width, own_width, 1)
    return (residual_own + mixed).astype(jnp.bfloat16)


def solution(mesh):
    placed = (
        P("req", "tp"),
        P("req", "tp"),
        P("req", None, None),
        P("req"),
        P("req", None),
        P(("req", "tp"), None, None, None),
        P("tp", None),
        P(),
        P("req", None),
        P("req", None),
        P("req", None, None, "tp"),
        P("req", "tp", None),
    )
    return jax.shard_map(
        per_device, mesh=mesh, in_specs=placed, out_specs=P("req", "tp"), check_vma=False
    )
```

```python
import jax
import jax.numpy as jnp
from jax import lax
from jax.sharding import PartitionSpec as P

EXPERTS = 32


rope_base = 1000000.0
norm_eps = 1e-06
neg_floor = -1e30


def apply_rotary_heads(values, positions, head_size):
    half_size = head_size // 2
    exponents = jnp.arange(half_size, dtype=jnp.float32) * (2.0 / head_size)
    inverse_freq = jnp.power(jnp.float32(rope_base), -exponents)
    angles = positions.astype(jnp.float32)[:, None] * inverse_freq[None, :]
    cosine = jnp.cos(angles)[:, None, :]
    sine = jnp.sin(angles)[:, None, :]
    first_half = values[..., :half_size]
    second_half = values[..., half_size:]
    return jnp.concatenate(
        [first_half * cosine - second_half * sine, second_half * cosine + first_half * sine],
        axis=-1,
    )


def per_device(
    hidden_in,
    queries,
    fresh_key_value,
    positions,
    lengths,
    cache,
    out_proj,
    norm_gain,
    expert_ids,
    router_weights,
    gate_up,
    down,
):
    tp_count = lax.axis_size("tp")
    req_count = lax.axis_size("req")
    tp_index = lax.axis_index("tp")
    req_index = lax.axis_index("req")
    row_count = hidden_in.shape[0]
    head_size = cache.shape[3]
    kv_count = cache.shape[2]
    own_heads = queries.shape[1] // head_size
    head_count = own_heads * tp_count
    request_group_size = head_count // kv_count
    score_scaling = head_size ** (-0.5)
    model_width = norm_gain.shape[0]
    own_width = hidden_in.shape[1]
    first_head = tp_index * own_heads
    span_rows = cache.shape[0]

    q_local = apply_rotary_heads(
        queries.reshape(row_count, own_heads, head_size).astype(jnp.float32), positions, head_size
    ).astype(jnp.bfloat16)
    gathered = lax.all_gather(q_local.reshape(row_count, own_width), "tp", axis=0)
    q_all = jnp.transpose(gathered, (1, 0, 2)).reshape(
        row_count, kv_count, request_group_size, head_size
    )

    k_new = apply_rotary_heads(
        fresh_key_value[:, 0].reshape(row_count, kv_count, head_size).astype(jnp.float32),
        positions,
        head_size,
    ).astype(jnp.bfloat16)
    value_fresh = fresh_key_value[:, 1].reshape(row_count, kv_count, head_size)
    own_score = (
        jnp.einsum("rcgd,rcd->rcg", q_all, k_new, preferred_element_type=jnp.float32)
        * score_scaling
    )

    segment_ends = jnp.cumsum(lengths[0], dtype=jnp.int32)
    segment_starts = segment_ends - lengths[0]
    cache_spots = tp_index * span_rows + jnp.arange(span_rows, dtype=jnp.int32)
    mask = (cache_spots[None, :] >= segment_starts[:, None]) & (
        cache_spots[None, :] < segment_ends[:, None]
    )
    mask = mask[:, None, None, :]
    keys = cache[:, 0]
    values = cache[:, 1]
    scores = (
        jnp.einsum("rcgd,jcd->rcgj", q_all, keys, preferred_element_type=jnp.float32)
        * score_scaling
    )
    scores = jnp.where(mask, scores, neg_floor)
    highest_local = jnp.max(scores, axis=3)
    weights = jnp.where(mask, jnp.exp(scores - highest_local[..., None]), 0.0)
    totals_local = jnp.sum(weights, axis=3)
    sums_local = jnp.einsum(
        "rcgj,jcd->rcgd",
        weights,
        values.astype(jnp.float32),
        precision=lax.Precision.HIGHEST,
        preferred_element_type=jnp.float32,
    )
    states = jnp.concatenate(
        [highest_local[..., None], totals_local[..., None], sums_local], axis=3
    ).reshape(row_count, tp_count, own_heads, head_size + 2)
    all_states = lax.all_to_all(
        jnp.transpose(states, (1, 0, 2, 3)), "tp", 0, 0, tiled=True
    )
    parts_highest = all_states[..., 0]
    parts_totals = all_states[..., 1]
    parts_sums = all_states[..., 2:]
    own_slice = lax.dynamic_slice_in_dim(own_score.reshape(row_count, head_count), first_head, own_heads, 1)
    top_score = jnp.maximum(jnp.max(parts_highest, axis=0), own_slice)
    factors = jnp.exp(parts_highest - top_score[None])
    own_part = jnp.exp(own_slice - top_score)
    head_kv = (first_head + jnp.arange(own_heads, dtype=jnp.int32)) // request_group_size
    own_values = jnp.take(value_fresh, head_kv, axis=1).astype(jnp.float32)
    totals = jnp.sum(parts_totals * factors, axis=0) + own_part
    summed = jnp.sum(parts_sums * factors[..., None], axis=0) + own_values * own_part[..., None]
    attention_output = (summed / totals[..., None]).astype(jnp.bfloat16).reshape(
        row_count, own_heads * head_size
    )

    partial_proj = jnp.dot(attention_output, out_proj, preferred_element_type=jnp.float32)
    partial_proj = jnp.transpose(partial_proj.reshape(row_count, tp_count, own_width), (1, 0, 2))
    projected = jnp.sum(lax.all_to_all(partial_proj, "tp", 0, 0, tiled=True), axis=0)
    residual_own = hidden_in.astype(jnp.float32) + projected
    residual = lax.all_gather(residual_own, "tp", axis=1, tiled=True)
    mean_square = jnp.mean(residual * residual, axis=1, keepdims=True)
    normed = (residual * lax.rsqrt(mean_square + norm_eps) * norm_gain[None, :]).astype(jnp.bfloat16)

    local_count = gate_up.shape[0]
    block_total = local_count * req_count
    split_count = max(1, block_total // EXPERTS)
    expert_range = jnp.arange(EXPERTS, dtype=jnp.int32)
    member = jnp.any(expert_ids[:, :, None] == expert_range[None, None, :], axis=1)
    member_int = member.astype(jnp.int32)
    slot_of = jnp.cumsum(member_int, axis=0, dtype=jnp.int32) - member_int
    slot_taken = jnp.take_along_axis(slot_of, expert_ids, axis=1)
    block_taken = (slot_taken % split_count) * EXPERTS + expert_ids
    block_range = jnp.arange(block_total, dtype=jnp.int32)
    block_weights = jnp.sum(
        jnp.where(block_taken[:, :, None] == block_range[None, None, :], router_weights[:, :, None], 0.0),
        axis=1,
    )

    weights_all = lax.all_gather(block_weights, "req", axis=0, tiled=True)
    weights_own = lax.dynamic_slice_in_dim(weights_all, req_index * local_count, local_count, 1)
    if req_count <= 16:
        arrived = [normed] + [
            lax.ppermute(normed, "req", [(i, (i + shift) % req_count) for i in range(req_count)])
            for shift in range(1, req_count)
        ]
        arrived = jnp.stack(arrived, axis=0)
        order = (req_index - jnp.arange(req_count, dtype=jnp.int32)) % req_count
        rows_all = jnp.take(arrived, order, axis=0).reshape(req_count * row_count, model_width)
    else:
        rows_all = lax.all_gather(normed, "req", axis=0, tiled=True)

    mixed = jnp.zeros((rows_all.shape[0], model_width), jnp.float32)
    for local_block in range(local_count):
        gate_part = jnp.dot(rows_all, gate_up[local_block, 0], preferred_element_type=jnp.float32)
        up_part = jnp.dot(rows_all, gate_up[local_block, 1], preferred_element_type=jnp.float32)
        activation = (jnp.maximum(gate_part, 0.0) * up_part).astype(jnp.bfloat16)
        produced = jnp.dot(activation, down[local_block], preferred_element_type=jnp.float32)
        produced = produced.astype(jnp.bfloat16).astype(jnp.float32)
        mixed = mixed + weights_own[:, local_block : local_block + 1] * produced

    mixed = mixed.astype(jnp.bfloat16).reshape(req_count, row_count, tp_count, own_width)
    mixed = jnp.transpose(mixed, (0, 2, 1, 3)).reshape(req_count * tp_count, row_count, own_width)
    mixed = lax.all_to_all(mixed, ("req", "tp"), 0, 0, tiled=True)
    mixed = jnp.sum(mixed.astype(jnp.float32), axis=0)
    return (residual_own + mixed).astype(jnp.bfloat16)


def solution(mesh):
    placed = (
        P("req", "tp"),
        P("req", "tp"),
        P("req", None, None),
        P("req"),
        P("req", None),
        P(("req", "tp"), None, None, None),
        P("tp", None),
        P(),
        P("req", None),
        P("req", None),
        P("req", None, None, "tp"),
        P("req", "tp", None),
    )
    return jax.shard_map(
        per_device, mesh=mesh, in_specs=placed, out_specs=P("req", "tp"), check_vma=False
    )
```

```python
import jax
import jax.numpy as jnp
from jax import lax
from jax.sharding import PartitionSpec as P

EXPERTS = 32


rope_base = 1000000.0
norm_eps = 1e-06
neg_floor = -1e30


def apply_rotary_heads(values, positions, head_size):
    half_size = head_size // 2
    exponents = jnp.arange(half_size, dtype=jnp.float32) * (2.0 / head_size)
    inverse_freq = jnp.power(jnp.float32(rope_base), -exponents)
    angles = positions.astype(jnp.float32)[:, None] * inverse_freq[None, :]
    cosine = jnp.cos(angles)[:, None, :]
    sine = jnp.sin(angles)[:, None, :]
    first_half = values[..., :half_size]
    second_half = values[..., half_size:]
    return jnp.concatenate(
        [first_half * cosine - second_half * sine, second_half * cosine + first_half * sine],
        axis=-1,
    )


def per_device(
    hidden_in,
    queries,
    fresh_key_value,
    positions,
    lengths,
    cache,
    out_proj,
    norm_gain,
    expert_ids,
    router_weights,
    gate_up,
    down,
):
    tp_count = lax.axis_size("tp")
    req_count = lax.axis_size("req")
    tp_index = lax.axis_index("tp")
    req_index = lax.axis_index("req")
    row_count = hidden_in.shape[0]
    head_size = cache.shape[3]
    kv_count = cache.shape[2]
    own_heads = queries.shape[1] // head_size
    head_count = own_heads * tp_count
    request_group_size = head_count // kv_count
    score_scaling = head_size ** (-0.5)
    model_width = norm_gain.shape[0]
    own_width = hidden_in.shape[1]
    first_head = tp_index * own_heads
    span_rows = cache.shape[0]

    q_local = apply_rotary_heads(
        queries.reshape(row_count, own_heads, head_size).astype(jnp.float32), positions, head_size
    ).astype(jnp.bfloat16)
    packed = jnp.stack([q_local.reshape(row_count, own_width), hidden_in], axis=0)
    gathered = lax.all_gather(packed, "tp", axis=0)
    q_all = jnp.transpose(gathered[:, 0], (1, 0, 2)).reshape(
        row_count, kv_count, request_group_size, head_size
    )
    hidden_full = jnp.transpose(gathered[:, 1], (1, 0, 2)).reshape(row_count, model_width)

    k_new = apply_rotary_heads(
        fresh_key_value[:, 0].reshape(row_count, kv_count, head_size).astype(jnp.float32),
        positions,
        head_size,
    ).astype(jnp.bfloat16)
    value_fresh = fresh_key_value[:, 1].reshape(row_count, kv_count, head_size)
    own_score = (
        jnp.einsum("rcgd,rcd->rcg", q_all, k_new, preferred_element_type=jnp.float32)
        * score_scaling
    )

    segment_ends = jnp.cumsum(lengths[0], dtype=jnp.int32)
    segment_starts = segment_ends - lengths[0]
    cache_spots = tp_index * span_rows + jnp.arange(span_rows, dtype=jnp.int32)
    mask = (cache_spots[None, :] >= segment_starts[:, None]) & (
        cache_spots[None, :] < segment_ends[:, None]
    )
    mask = mask[:, None, None, :]
    keys = cache[:, 0]
    values = cache[:, 1]
    scores = (
        jnp.einsum("rcgd,jcd->rcgj", q_all, keys, preferred_element_type=jnp.float32)
        * score_scaling
    )
    scores = jnp.where(mask, scores, neg_floor)
    highest_local = jnp.max(scores, axis=3)
    weights = jnp.where(mask, jnp.exp(scores - highest_local[..., None]), 0.0)
    totals_local = jnp.sum(weights, axis=3)
    sums_local = jnp.einsum(
        "rcgj,jcd->rcgd",
        weights,
        values.astype(jnp.float32),
        precision=lax.Precision.HIGHEST,
        preferred_element_type=jnp.float32,
    )
    states = jnp.concatenate(
        [highest_local[..., None], totals_local[..., None], sums_local], axis=3
    ).reshape(row_count, tp_count, own_heads, head_size + 2)
    all_states = lax.all_to_all(
        jnp.transpose(states, (1, 0, 2, 3)), "tp", 0, 0, tiled=True
    )
    parts_highest = all_states[..., 0]
    parts_totals = all_states[..., 1]
    parts_sums = all_states[..., 2:]
    own_slice = lax.dynamic_slice_in_dim(own_score.reshape(row_count, head_count), first_head, own_heads, 1)
    top_score = jnp.maximum(jnp.max(parts_highest, axis=0), own_slice)
    factors = jnp.exp(parts_highest - top_score[None])
    own_part = jnp.exp(own_slice - top_score)
    head_kv = (first_head + jnp.arange(own_heads, dtype=jnp.int32)) // request_group_size
    own_values = jnp.take(value_fresh, head_kv, axis=1).astype(jnp.float32)
    totals = jnp.sum(parts_totals * factors, axis=0) + own_part
    summed = jnp.sum(parts_sums * factors[..., None], axis=0) + own_values * own_part[..., None]
    attention_output = (summed / totals[..., None]).astype(jnp.bfloat16).reshape(
        row_count, own_heads * head_size
    )

    partial_proj = jnp.dot(attention_output, out_proj, preferred_element_type=jnp.float32)
    projected = jnp.sum(lax.all_gather(partial_proj, "tp", axis=0), axis=0)
    residual = hidden_full.astype(jnp.float32) + projected
    mean_square = jnp.mean(residual * residual, axis=1, keepdims=True)
    normed = (residual * lax.rsqrt(mean_square + norm_eps) * norm_gain[None, :]).astype(jnp.bfloat16)
    residual_own = lax.dynamic_slice_in_dim(residual, tp_index * own_width, own_width, 1)

    local_count = gate_up.shape[0]
    block_total = local_count * req_count
    split_count = max(1, block_total // EXPERTS)
    expert_range = jnp.arange(EXPERTS, dtype=jnp.int32)
    member = jnp.any(expert_ids[:, :, None] == expert_range[None, None, :], axis=1)
    member_int = member.astype(jnp.int32)
    slot_of = jnp.cumsum(member_int, axis=0, dtype=jnp.int32) - member_int
    slot_taken = jnp.take_along_axis(slot_of, expert_ids, axis=1)
    block_taken = (slot_taken % split_count) * EXPERTS + expert_ids
    block_range = jnp.arange(block_total, dtype=jnp.int32)
    block_weights = jnp.sum(
        jnp.where(block_taken[:, :, None] == block_range[None, None, :], router_weights[:, :, None], 0.0),
        axis=1,
    )

    if req_count <= 16:
        def gather_req(value):
            arrived = [value] + [
                lax.ppermute(value, "req", [(i, (i + shift) % req_count) for i in range(req_count)])
                for shift in range(1, req_count)
            ]
            order = (req_index - jnp.arange(req_count, dtype=jnp.int32)) % req_count
            arrived = jnp.take(jnp.stack(arrived, axis=0), order, axis=0)
            return arrived.reshape((req_count * value.shape[0],) + value.shape[1:])
    else:
        def gather_req(value):
            return lax.all_gather(value, "req", axis=0, tiled=True)
    rows_all = gather_req(normed)
    weights_all = gather_req(block_weights)
    weights_own = lax.dynamic_slice_in_dim(weights_all, req_index * local_count, local_count, 1)

    mixed = jnp.zeros((rows_all.shape[0], model_width), jnp.float32)
    for local_block in range(local_count):
        gate_part = jnp.dot(rows_all, gate_up[local_block, 0], preferred_element_type=jnp.float32)
        up_part = jnp.dot(rows_all, gate_up[local_block, 1], preferred_element_type=jnp.float32)
        activation = (jnp.maximum(gate_part, 0.0) * up_part).astype(jnp.bfloat16)
        produced = jnp.dot(activation, down[local_block], preferred_element_type=jnp.float32)
        produced = produced.astype(jnp.bfloat16).astype(jnp.float32)
        mixed = mixed + weights_own[:, local_block : local_block + 1] * produced

    mixed = mixed.astype(jnp.bfloat16).reshape(req_count, row_count, tp_count, own_width)
    mixed = jnp.transpose(mixed, (0, 2, 1, 3)).reshape(req_count * tp_count, row_count, own_width)
    mixed = lax.all_to_all(mixed, ("req", "tp"), 0, 0, tiled=True)
    mixed = jnp.sum(mixed.astype(jnp.float32), axis=0)
    return (residual_own + mixed).astype(jnp.bfloat16)


def solution(mesh):
    placed = (
        P("req", "tp"),
        P("req", "tp"),
        P("req", None, None),
        P("req"),
        P("req", None),
        P(("req", "tp"), None, None, None),
        P("tp", None),
        P(),
        P("req", None),
        P("req", None),
        P("req", None, None, "tp"),
        P("req", "tp", None),
    )
    return jax.shard_map(
        per_device, mesh=mesh, in_specs=placed, out_specs=P("req", "tp"), check_vma=False
    )
```

```python
import math

import jax
import jax.numpy as jnp
from jax import lax
from jax.experimental import pallas as pl
from jax.experimental.pallas import tpu as pltpu
from jax.sharding import PartitionSpec as P

EXPERTS = 32


rope_base = 1000000.0
norm_eps = 1e-06
neg_floor = -1e30


def apply_rotary_heads(values, positions, head_size):
    half_size = head_size // 2
    exponents = jnp.arange(half_size, dtype=jnp.float32) * (2.0 / head_size)
    inverse_freq = jnp.power(jnp.float32(rope_base), -exponents)
    angles = positions.astype(jnp.float32)[:, None] * inverse_freq[None, :]
    cosine = jnp.cos(angles)[:, None, :]
    sine = jnp.sin(angles)[:, None, :]
    first_half = values[..., :half_size]
    second_half = values[..., half_size:]
    return jnp.concatenate(
        [first_half * cosine - second_half * sine, second_half * cosine + first_half * sine],
        axis=-1,
    )


def _expert_body(x_ref, gu_ref, dn_ref, w_ref, o_ref, acc_ref):
    block = pl.program_id(1)

    @pl.when(block == 0)
    def _():
        acc_ref[...] = jnp.zeros_like(acc_ref)

    x = x_ref[...]
    gate_part = jnp.dot(x, gu_ref[0, 0], preferred_element_type=jnp.float32)
    up_part = jnp.dot(x, gu_ref[0, 1], preferred_element_type=jnp.float32)
    activation = (jnp.maximum(gate_part, 0.0) * up_part).astype(jnp.bfloat16)
    produced = jnp.dot(activation, dn_ref[0], preferred_element_type=jnp.float32)
    produced = produced.astype(jnp.bfloat16).astype(jnp.float32)
    acc_ref[...] += w_ref[0] * produced

    @pl.when(block == pl.num_programs(1) - 1)
    def _():
        o_ref[...] = acc_ref[...].astype(o_ref.dtype)


def expert_mix(rows, gate_up, down, weights):
    row_total, width = rows.shape
    local_count, _, _, hidden = gate_up.shape
    tile = math.gcd(row_total, 192)
    weights_t = jnp.transpose(weights)[:, :, None]
    return pl.pallas_call(
        _expert_body,
        grid=(row_total // tile, local_count),
        in_specs=[
            pl.BlockSpec((tile, width), lambda i, b: (i, 0)),
            pl.BlockSpec((1, 2, width, hidden), lambda i, b: (b, 0, 0, 0)),
            pl.BlockSpec((1, hidden, width), lambda i, b: (b, 0, 0)),
            pl.BlockSpec((1, tile, 1), lambda i, b: (b, i, 0)),
        ],
        out_specs=pl.BlockSpec((tile, width), lambda i, b: (i, 0)),
        out_shape=jax.ShapeDtypeStruct((row_total, width), jnp.bfloat16),
        scratch_shapes=[pltpu.VMEM((tile, width), jnp.float32)],
        compiler_params=pltpu.CompilerParams(dimension_semantics=("parallel", "arbitrary")),
    )(rows, gate_up, down, weights_t)


def per_device(
    hidden_in,
    queries,
    fresh_key_value,
    positions,
    lengths,
    cache,
    out_proj,
    norm_gain,
    expert_ids,
    router_weights,
    gate_up,
    down,
):
    tp_count = lax.axis_size("tp")
    req_count = lax.axis_size("req")
    tp_index = lax.axis_index("tp")
    req_index = lax.axis_index("req")
    row_count = hidden_in.shape[0]
    head_size = cache.shape[3]
    kv_count = cache.shape[2]
    own_heads = queries.shape[1] // head_size
    head_count = own_heads * tp_count
    request_group_size = head_count // kv_count
    score_scaling = head_size ** (-0.5)
    model_width = norm_gain.shape[0]
    own_width = hidden_in.shape[1]
    first_head = tp_index * own_heads
    span_rows = cache.shape[0]

    q_local = apply_rotary_heads(
        queries.reshape(row_count, own_heads, head_size).astype(jnp.float32), positions, head_size
    ).astype(jnp.bfloat16)
    packed = jnp.stack([q_local.reshape(row_count, own_width), hidden_in], axis=0)
    gathered = lax.all_gather(packed, "tp", axis=0)
    q_all = jnp.transpose(gathered[:, 0], (1, 0, 2)).reshape(
        row_count, kv_count, request_group_size, head_size
    )
    hidden_full = jnp.transpose(gathered[:, 1], (1, 0, 2)).reshape(row_count, model_width)

    k_new = apply_rotary_heads(
        fresh_key_value[:, 0].reshape(row_count, kv_count, head_size).astype(jnp.float32),
        positions,
        head_size,
    ).astype(jnp.bfloat16)
    value_fresh = fresh_key_value[:, 1].reshape(row_count, kv_count, head_size)
    own_score = (
        jnp.einsum("rcgd,rcd->rcg", q_all, k_new, preferred_element_type=jnp.float32)
        * score_scaling
    )

    segment_ends = jnp.cumsum(lengths[0], dtype=jnp.int32)
    segment_starts = segment_ends - lengths[0]
    cache_spots = tp_index * span_rows + jnp.arange(span_rows, dtype=jnp.int32)
    mask = (cache_spots[None, :] >= segment_starts[:, None]) & (
        cache_spots[None, :] < segment_ends[:, None]
    )
    mask = mask[:, None, None, :]
    keys = cache[:, 0]
    values = cache[:, 1]
    scores = (
        jnp.einsum("rcgd,jcd->rcgj", q_all, keys, preferred_element_type=jnp.float32)
        * score_scaling
    )
    scores = jnp.where(mask, scores, neg_floor)
    highest_local = jnp.max(scores, axis=3)
    weights = jnp.where(mask, jnp.exp(scores - highest_local[..., None]), 0.0)
    totals_local = jnp.sum(weights, axis=3)
    sums_local = jnp.einsum(
        "rcgj,jcd->rcgd",
        weights,
        values.astype(jnp.float32),
        precision=lax.Precision.HIGHEST,
        preferred_element_type=jnp.float32,
    )
    states = jnp.concatenate(
        [highest_local[..., None], totals_local[..., None], sums_local], axis=3
    ).reshape(row_count, tp_count, own_heads, head_size + 2)
    all_states = lax.all_to_all(
        jnp.transpose(states, (1, 0, 2, 3)), "tp", 0, 0, tiled=True
    )
    parts_highest = all_states[..., 0]
    parts_totals = all_states[..., 1]
    parts_sums = all_states[..., 2:]
    own_slice = lax.dynamic_slice_in_dim(own_score.reshape(row_count, head_count), first_head, own_heads, 1)
    top_score = jnp.maximum(jnp.max(parts_highest, axis=0), own_slice)
    factors = jnp.exp(parts_highest - top_score[None])
    own_part = jnp.exp(own_slice - top_score)
    head_kv = (first_head + jnp.arange(own_heads, dtype=jnp.int32)) // request_group_size
    own_values = jnp.take(value_fresh, head_kv, axis=1).astype(jnp.float32)
    totals = jnp.sum(parts_totals * factors, axis=0) + own_part
    summed = jnp.sum(parts_sums * factors[..., None], axis=0) + own_values * own_part[..., None]
    attention_output = (summed / totals[..., None]).astype(jnp.bfloat16).reshape(
        row_count, own_heads * head_size
    )

    partial_proj = jnp.dot(attention_output, out_proj, preferred_element_type=jnp.float32)
    projected = jnp.sum(lax.all_gather(partial_proj, "tp", axis=0), axis=0)
    residual = hidden_full.astype(jnp.float32) + projected
    mean_square = jnp.mean(residual * residual, axis=1, keepdims=True)
    normed = (residual * lax.rsqrt(mean_square + norm_eps) * norm_gain[None, :]).astype(jnp.bfloat16)
    residual_own = lax.dynamic_slice_in_dim(residual, tp_index * own_width, own_width, 1)

    local_count = gate_up.shape[0]
    block_total = local_count * req_count
    split_count = max(1, block_total // EXPERTS)
    expert_range = jnp.arange(EXPERTS, dtype=jnp.int32)
    member = jnp.any(expert_ids[:, :, None] == expert_range[None, None, :], axis=1)
    member_int = member.astype(jnp.int32)
    slot_of = jnp.cumsum(member_int, axis=0, dtype=jnp.int32) - member_int
    slot_taken = jnp.take_along_axis(slot_of, expert_ids, axis=1)
    block_taken = (slot_taken % split_count) * EXPERTS + expert_ids
    block_range = jnp.arange(block_total, dtype=jnp.int32)
    block_weights = jnp.sum(
        jnp.where(block_taken[:, :, None] == block_range[None, None, :], router_weights[:, :, None], 0.0),
        axis=1,
    )

    if req_count <= 16:
        def gather_req(value):
            arrived = [value] + [
                lax.ppermute(value, "req", [(i, (i + shift) % req_count) for i in range(req_count)])
                for shift in range(1, req_count)
            ]
            order = (req_index - jnp.arange(req_count, dtype=jnp.int32)) % req_count
            arrived = jnp.take(jnp.stack(arrived, axis=0), order, axis=0)
            return arrived.reshape((req_count * value.shape[0],) + value.shape[1:])
    else:
        def gather_req(value):
            return lax.all_gather(value, "req", axis=0, tiled=True)
    weight_high = lax.reduce_precision(block_weights, exponent_bits=8, mantissa_bits=7)
    weight_rest = block_weights - weight_high
    weight_mid = lax.reduce_precision(weight_rest, exponent_bits=8, mantissa_bits=7)
    weight_low = weight_rest - weight_mid
    message = jnp.concatenate(
        [normed, weight_high.astype(jnp.bfloat16), weight_mid.astype(jnp.bfloat16), weight_low.astype(jnp.bfloat16)],
        axis=1,
    )
    message_all = gather_req(message)
    rows_all = message_all[:, :model_width]
    pieces = message_all[:, model_width:].astype(jnp.float32).reshape(-1, 3, block_total)
    weights_all = (pieces[:, 0] + pieces[:, 1]) + pieces[:, 2]
    weights_own = lax.dynamic_slice_in_dim(weights_all, req_index * local_count, local_count, 1)

    mixed = expert_mix(rows_all, gate_up, down, weights_own)
    mixed = mixed.reshape(req_count, row_count, tp_count, own_width)
    mixed = jnp.transpose(mixed, (0, 2, 1, 3)).reshape(req_count * tp_count, row_count, own_width)
    mixed = lax.all_to_all(mixed, ("req", "tp"), 0, 0, tiled=True)
    mixed = jnp.sum(mixed.astype(jnp.float32), axis=0)
    return (residual_own + mixed).astype(jnp.bfloat16)


def solution(mesh):
    placed = (
        P("req", "tp"),
        P("req", "tp"),
        P("req", None, None),
        P("req"),
        P("req", None),
        P(("req", "tp"), None, None, None),
        P("tp", None),
        P(),
        P("req", None),
        P("req", None),
        P("req", None, None, "tp"),
        P("req", "tp", None),
    )
    return jax.shard_map(
        per_device, mesh=mesh, in_specs=placed, out_specs=P("req", "tp"), check_vma=False
    )
```

```python
import math

import jax
import jax.numpy as jnp
from jax import lax
from jax.experimental import pallas as pl
from jax.experimental.pallas import tpu as pltpu
from jax.sharding import PartitionSpec as P

EXPERTS = 32


rope_base = 1000000.0
norm_eps = 1e-06
neg_floor = -1e30


def apply_rotary_heads(values, positions, head_size):
    half_size = head_size // 2
    exponents = jnp.arange(half_size, dtype=jnp.float32) * (2.0 / head_size)
    inverse_freq = jnp.power(jnp.float32(rope_base), -exponents)
    angles = positions.astype(jnp.float32)[:, None] * inverse_freq[None, :]
    cosine = jnp.cos(angles)[:, None, :]
    sine = jnp.sin(angles)[:, None, :]
    first_half = values[..., :half_size]
    second_half = values[..., half_size:]
    return jnp.concatenate(
        [first_half * cosine - second_half * sine, second_half * cosine + first_half * sine],
        axis=-1,
    )


def _expert_body(x_ref, gu_ref, dn_ref, w_ref, o_ref, acc_ref):
    block = pl.program_id(1)

    @pl.when(block == 0)
    def _():
        acc_ref[...] = jnp.zeros_like(acc_ref)

    x = x_ref[...]
    contract_rows = (((1,), (1,)), ((), ()))
    gate_part = lax.dot_general(x, gu_ref[0, 0], contract_rows, preferred_element_type=jnp.float32)
    up_part = lax.dot_general(x, gu_ref[0, 1], contract_rows, preferred_element_type=jnp.float32)
    activation = (jnp.maximum(gate_part, 0.0) * up_part).astype(jnp.bfloat16)
    produced = jnp.dot(activation, dn_ref[0], preferred_element_type=jnp.float32)
    produced = produced.astype(jnp.bfloat16).astype(jnp.float32)
    weights = w_ref[...]
    lanes = lax.broadcasted_iota(jnp.int32, weights.shape, 1)
    chosen = jnp.sum(jnp.where(lanes == block, weights, 0.0), axis=1, keepdims=True)
    acc_ref[...] += chosen * produced

    @pl.when(block == pl.num_programs(1) - 1)
    def _():
        o_ref[...] = acc_ref[...].astype(o_ref.dtype)


def expert_mix(rows, gate_up, down, weights):
    row_total, width = rows.shape
    local_count, _, _, hidden = gate_up.shape
    tile = math.gcd(row_total, 192)
    gate_up_t = jnp.swapaxes(gate_up, 2, 3)
    return pl.pallas_call(
        _expert_body,
        grid=(row_total // tile, local_count),
        in_specs=[
            pl.BlockSpec((tile, width), lambda i, b: (i, 0)),
            pl.BlockSpec((1, 2, hidden, width), lambda i, b: (b, 0, 0, 0)),
            pl.BlockSpec((1, hidden, width), lambda i, b: (b, 0, 0)),
            pl.BlockSpec((tile, local_count), lambda i, b: (i, 0)),
        ],
        out_specs=pl.BlockSpec((tile, width), lambda i, b: (i, 0)),
        out_shape=jax.ShapeDtypeStruct((row_total, width), jnp.bfloat16),
        scratch_shapes=[pltpu.VMEM((tile, width), jnp.float32)],
        compiler_params=pltpu.CompilerParams(dimension_semantics=("parallel", "arbitrary")),
    )(rows, gate_up_t, down, weights)


def per_device(
    hidden_in,
    queries,
    fresh_key_value,
    positions,
    lengths,
    cache,
    out_proj,
    norm_gain,
    expert_ids,
    router_weights,
    gate_up,
    down,
):
    tp_count = lax.axis_size("tp")
    req_count = lax.axis_size("req")
    tp_index = lax.axis_index("tp")
    req_index = lax.axis_index("req")
    row_count = hidden_in.shape[0]
    head_size = cache.shape[3]
    kv_count = cache.shape[2]
    own_heads = queries.shape[1] // head_size
    head_count = own_heads * tp_count
    request_group_size = head_count // kv_count
    score_scaling = head_size ** (-0.5)
    model_width = norm_gain.shape[0]
    own_width = hidden_in.shape[1]
    first_head = tp_index * own_heads
    span_rows = cache.shape[0]

    q_local = apply_rotary_heads(
        queries.reshape(row_count, own_heads, head_size).astype(jnp.float32), positions, head_size
    ).astype(jnp.bfloat16)
    packed = jnp.stack([q_local.reshape(row_count, own_width), hidden_in], axis=0)
    gathered = lax.all_gather(packed, "tp", axis=0)
    q_all = jnp.transpose(gathered[:, 0], (1, 0, 2)).reshape(
        row_count, kv_count, request_group_size, head_size
    )
    hidden_full = jnp.transpose(gathered[:, 1], (1, 0, 2)).reshape(row_count, model_width)

    k_new = apply_rotary_heads(
        fresh_key_value[:, 0].reshape(row_count, kv_count, head_size).astype(jnp.float32),
        positions,
        head_size,
    ).astype(jnp.bfloat16)
    value_fresh = fresh_key_value[:, 1].reshape(row_count, kv_count, head_size)
    own_score = (
        jnp.einsum("rcgd,rcd->rcg", q_all, k_new, preferred_element_type=jnp.float32)
        * score_scaling
    )

    segment_ends = jnp.cumsum(lengths[0], dtype=jnp.int32)
    segment_starts = segment_ends - lengths[0]
    cache_spots = tp_index * span_rows + jnp.arange(span_rows, dtype=jnp.int32)
    mask = (cache_spots[None, :] >= segment_starts[:, None]) & (
        cache_spots[None, :] < segment_ends[:, None]
    )
    mask = mask[:, None, None, :]
    keys = cache[:, 0]
    values = cache[:, 1]
    scores = (
        jnp.einsum("rcgd,jcd->rcgj", q_all, keys, preferred_element_type=jnp.float32)
        * score_scaling
    )
    scores = jnp.where(mask, scores, neg_floor)
    highest_local = jnp.max(scores, axis=3)
    weights = jnp.where(mask, jnp.exp(scores - highest_local[..., None]), 0.0)
    totals_local = jnp.sum(weights, axis=3)
    sums_local = jnp.einsum(
        "rcgj,jcd->rcgd",
        weights,
        values.astype(jnp.float32),
        precision=lax.Precision.HIGHEST,
        preferred_element_type=jnp.float32,
    )
    states = jnp.concatenate(
        [highest_local[..., None], totals_local[..., None], sums_local], axis=3
    ).reshape(row_count, tp_count, own_heads, head_size + 2)
    all_states = lax.all_to_all(
        jnp.transpose(states, (1, 0, 2, 3)), "tp", 0, 0, tiled=True
    )
    parts_highest = all_states[..., 0]
    parts_totals = all_states[..., 1]
    parts_sums = all_states[..., 2:]
    own_slice = lax.dynamic_slice_in_dim(own_score.reshape(row_count, head_count), first_head, own_heads, 1)
    top_score = jnp.maximum(jnp.max(parts_highest, axis=0), own_slice)
    factors = jnp.exp(parts_highest - top_score[None])
    own_part = jnp.exp(own_slice - top_score)
    head_kv = (first_head + jnp.arange(own_heads, dtype=jnp.int32)) // request_group_size
    own_values = jnp.take(value_fresh, head_kv, axis=1).astype(jnp.float32)
    totals = jnp.sum(parts_totals * factors, axis=0) + own_part
    summed = jnp.sum(parts_sums * factors[..., None], axis=0) + own_values * own_part[..., None]
    attention_output = (summed / totals[..., None]).astype(jnp.bfloat16).reshape(
        row_count, own_heads * head_size
    )

    partial_proj = jnp.dot(attention_output, out_proj, preferred_element_type=jnp.float32)
    projected = jnp.sum(lax.all_gather(partial_proj, "tp", axis=0), axis=0)
    residual = hidden_full.astype(jnp.float32) + projected
    mean_square = jnp.mean(residual * residual, axis=1, keepdims=True)
    normed = (residual * lax.rsqrt(mean_square + norm_eps) * norm_gain[None, :]).astype(jnp.bfloat16)
    residual_own = lax.dynamic_slice_in_dim(residual, tp_index * own_width, own_width, 1)

    local_count = gate_up.shape[0]
    block_total = local_count * req_count
    split_count = max(1, block_total // EXPERTS)
    expert_range = jnp.arange(EXPERTS, dtype=jnp.int32)
    member = jnp.any(expert_ids[:, :, None] == expert_range[None, None, :], axis=1)
    member_int = member.astype(jnp.int32)
    slot_of = jnp.cumsum(member_int, axis=0, dtype=jnp.int32) - member_int
    slot_taken = jnp.take_along_axis(slot_of, expert_ids, axis=1)
    block_taken = (slot_taken % split_count) * EXPERTS + expert_ids
    block_range = jnp.arange(block_total, dtype=jnp.int32)
    block_weights = jnp.sum(
        jnp.where(block_taken[:, :, None] == block_range[None, None, :], router_weights[:, :, None], 0.0),
        axis=1,
    )

    if req_count <= 16:
        def gather_req(value):
            arrived = [value] + [
                lax.ppermute(value, "req", [(i, (i + shift) % req_count) for i in range(req_count)])
                for shift in range(1, req_count)
            ]
            order = (req_index - jnp.arange(req_count, dtype=jnp.int32)) % req_count
            arrived = jnp.take(jnp.stack(arrived, axis=0), order, axis=0)
            return arrived.reshape((req_count * value.shape[0],) + value.shape[1:])
    else:
        def gather_req(value):
            return lax.all_gather(value, "req", axis=0, tiled=True)
    weight_high = lax.reduce_precision(block_weights, exponent_bits=8, mantissa_bits=7)
    weight_rest = block_weights - weight_high
    weight_mid = lax.reduce_precision(weight_rest, exponent_bits=8, mantissa_bits=7)
    weight_low = weight_rest - weight_mid
    code = jnp.stack(
        [weight_high.astype(jnp.bfloat16), weight_mid.astype(jnp.bfloat16), weight_low.astype(jnp.bfloat16)],
        axis=1,
    ).reshape(-1)
    code_rows = -(-code.shape[0] // model_width)
    code = jnp.pad(code, (0, code_rows * model_width - code.shape[0])).reshape(code_rows, model_width)
    message = jnp.concatenate([normed, code], axis=0)
    message_all = gather_req(message).reshape(req_count, row_count + code_rows, model_width)
    rows_all = message_all[:, :row_count].reshape(req_count * row_count, model_width)
    pieces = message_all[:, row_count:].reshape(req_count, code_rows * model_width)
    pieces = pieces[:, : row_count * 3 * block_total].astype(jnp.float32)
    pieces = pieces.reshape(req_count * row_count, 3, block_total)
    weights_all = (pieces[:, 0] + pieces[:, 1]) + pieces[:, 2]
    weights_own = lax.dynamic_slice_in_dim(weights_all, req_index * local_count, local_count, 1)

    mixed = expert_mix(rows_all, gate_up, down, weights_own)
    mixed = mixed.reshape(req_count, row_count, tp_count, own_width)
    mixed = jnp.transpose(mixed, (0, 2, 1, 3)).reshape(req_count * tp_count, row_count, own_width)
    mixed = lax.all_to_all(mixed, ("req", "tp"), 0, 0, tiled=True)
    mixed = jnp.sum(mixed.astype(jnp.float32), axis=0)
    return (residual_own + mixed).astype(jnp.bfloat16)


def solution(mesh):
    placed = (
        P("req", "tp"),
        P("req", "tp"),
        P("req", None, None),
        P("req"),
        P("req", None),
        P(("req", "tp"), None, None, None),
        P("tp", None),
        P(),
        P("req", None),
        P("req", None),
        P("req", None, None, "tp"),
        P("req", "tp", None),
    )
    return jax.shard_map(
        per_device, mesh=mesh, in_specs=placed, out_specs=P("req", "tp"), check_vma=False
    )
```

```python
import functools
import math

import jax
import jax.numpy as jnp
from jax import lax
from jax.experimental import pallas as pl
from jax.experimental.pallas import tpu as pltpu
from jax.sharding import PartitionSpec as P

EXPERTS = 32


rope_base = 1000000.0
norm_eps = 1e-06
neg_floor = -1e30


def apply_rotary_heads(values, positions, head_size):
    half_size = head_size // 2
    exponents = jnp.arange(half_size, dtype=jnp.float32) * (2.0 / head_size)
    inverse_freq = jnp.power(jnp.float32(rope_base), -exponents)
    angles = positions.astype(jnp.float32)[:, None] * inverse_freq[None, :]
    cosine = jnp.cos(angles)[:, None, :]
    sine = jnp.sin(angles)[:, None, :]
    first_half = values[..., :half_size]
    second_half = values[..., half_size:]
    return jnp.concatenate(
        [first_half * cosine - second_half * sine, second_half * cosine + first_half * sine],
        axis=-1,
    )


def _expert_body(x_ref, gu_ref, dn_ref, w_ref, o_ref, acc_ref, *, group_rows, row_count, tp_count):
    block = pl.program_id(1)

    @pl.when(block == 0)
    def _():
        acc_ref[...] = jnp.zeros_like(acc_ref)

    x = x_ref[...]
    contract_rows = (((1,), (1,)), ((), ()))
    gate_part = lax.dot_general(x, gu_ref[0, 0], contract_rows, preferred_element_type=jnp.float32)
    up_part = lax.dot_general(x, gu_ref[0, 1], contract_rows, preferred_element_type=jnp.float32)
    activation = (jnp.maximum(gate_part, 0.0) * up_part).astype(jnp.bfloat16)
    produced = jnp.dot(activation, dn_ref[0], preferred_element_type=jnp.float32)
    produced = produced.astype(jnp.bfloat16).astype(jnp.float32)
    weights = w_ref[...]
    lanes = lax.broadcasted_iota(jnp.int32, weights.shape, 1)
    chosen = jnp.sum(jnp.where(lanes == block, weights, 0.0), axis=1, keepdims=True)
    acc_ref[...] += chosen * produced

    @pl.when(block == pl.num_programs(1) - 1)
    def _():
        own_width = o_ref.shape[2]
        for group in range(x_ref.shape[0] // group_rows):
            for part in range(tp_count):
                o_ref[group * tp_count + part] = acc_ref[
                    group * group_rows : group * group_rows + row_count,
                    part * own_width : (part + 1) * own_width,
                ].astype(o_ref.dtype)


def expert_mix(rows, gate_up, down, weights, group_rows, row_count, tp_count):
    row_total, width = rows.shape
    local_count, _, _, hidden = gate_up.shape
    group_total = row_total // group_rows
    tile_groups = math.gcd(group_total, 8)
    tile = tile_groups * group_rows
    own_width = width // tp_count
    gate_up_t = jnp.swapaxes(gate_up, 2, 3)
    body = functools.partial(
        _expert_body, group_rows=group_rows, row_count=row_count, tp_count=tp_count
    )
    return pl.pallas_call(
        body,
        grid=(group_total // tile_groups, local_count),
        in_specs=[
            pl.BlockSpec((tile, width), lambda i, b: (i, 0)),
            pl.BlockSpec((1, 2, hidden, width), lambda i, b: (b, 0, 0, 0)),
            pl.BlockSpec((1, hidden, width), lambda i, b: (b, 0, 0)),
            pl.BlockSpec((tile, local_count), lambda i, b: (i, 0)),
        ],
        out_specs=pl.BlockSpec((tile_groups * tp_count, row_count, own_width), lambda i, b: (i, 0, 0)),
        out_shape=jax.ShapeDtypeStruct((group_total * tp_count, row_count, own_width), jnp.bfloat16),
        scratch_shapes=[pltpu.VMEM((tile, width), jnp.float32)],
        compiler_params=pltpu.CompilerParams(dimension_semantics=("parallel", "arbitrary")),
    )(rows, gate_up_t, down, weights)


def per_device(
    hidden_in,
    queries,
    fresh_key_value,
    positions,
    lengths,
    cache,
    out_proj,
    norm_gain,
    expert_ids,
    router_weights,
    gate_up,
    down,
):
    tp_count = lax.axis_size("tp")
    req_count = lax.axis_size("req")
    tp_index = lax.axis_index("tp")
    req_index = lax.axis_index("req")
    row_count = hidden_in.shape[0]
    head_size = cache.shape[3]
    kv_count = cache.shape[2]
    own_heads = queries.shape[1] // head_size
    head_count = own_heads * tp_count
    request_group_size = head_count // kv_count
    score_scaling = head_size ** (-0.5)
    model_width = norm_gain.shape[0]
    own_width = hidden_in.shape[1]
    first_head = tp_index * own_heads
    span_rows = cache.shape[0]

    q_local = apply_rotary_heads(
        queries.reshape(row_count, own_heads, head_size).astype(jnp.float32), positions, head_size
    ).astype(jnp.bfloat16)
    packed = jnp.stack([q_local.reshape(row_count, own_width), hidden_in], axis=0)
    gathered = lax.all_gather(packed, "tp", axis=0)
    q_all = jnp.transpose(gathered[:, 0], (1, 0, 2)).reshape(
        row_count, kv_count, request_group_size, head_size
    )
    hidden_full = jnp.transpose(gathered[:, 1], (1, 0, 2)).reshape(row_count, model_width)

    k_new = apply_rotary_heads(
        fresh_key_value[:, 0].reshape(row_count, kv_count, head_size).astype(jnp.float32),
        positions,
        head_size,
    ).astype(jnp.bfloat16)
    value_fresh = fresh_key_value[:, 1].reshape(row_count, kv_count, head_size)
    own_score = (
        jnp.einsum("rcgd,rcd->rcg", q_all, k_new, preferred_element_type=jnp.float32)
        * score_scaling
    )

    segment_ends = jnp.cumsum(lengths[0], dtype=jnp.int32)
    segment_starts = segment_ends - lengths[0]
    cache_spots = tp_index * span_rows + jnp.arange(span_rows, dtype=jnp.int32)
    mask = (cache_spots[None, :] >= segment_starts[:, None]) & (
        cache_spots[None, :] < segment_ends[:, None]
    )
    mask = mask[:, None, None, :]
    keys = cache[:, 0]
    values = cache[:, 1]
    scores = (
        jnp.einsum("rcgd,jcd->rcgj", q_all, keys, preferred_element_type=jnp.float32)
        * score_scaling
    )
    scores = jnp.where(mask, scores, neg_floor)
    highest_local = jnp.max(scores, axis=3)
    weights = jnp.where(mask, jnp.exp(scores - highest_local[..., None]), 0.0)
    totals_local = jnp.sum(weights, axis=3)
    sums_local = jnp.einsum(
        "rcgj,jcd->rcgd",
        weights,
        values.astype(jnp.float32),
        precision=lax.Precision.HIGHEST,
        preferred_element_type=jnp.float32,
    )
    states = jnp.concatenate(
        [highest_local[..., None], totals_local[..., None], sums_local], axis=3
    ).reshape(row_count, tp_count, own_heads, head_size + 2)
    all_states = lax.all_to_all(
        jnp.transpose(states, (1, 0, 2, 3)), "tp", 0, 0, tiled=True
    )
    parts_highest = all_states[..., 0]
    parts_totals = all_states[..., 1]
    parts_sums = all_states[..., 2:]
    own_slice = lax.dynamic_slice_in_dim(own_score.reshape(row_count, head_count), first_head, own_heads, 1)
    top_score = jnp.maximum(jnp.max(parts_highest, axis=0), own_slice)
    factors = jnp.exp(parts_highest - top_score[None])
    own_part = jnp.exp(own_slice - top_score)
    head_kv = (first_head + jnp.arange(own_heads, dtype=jnp.int32)) // request_group_size
    own_values = jnp.take(value_fresh, head_kv, axis=1).astype(jnp.float32)
    totals = jnp.sum(parts_totals * factors, axis=0) + own_part
    summed = jnp.sum(parts_sums * factors[..., None], axis=0) + own_values * own_part[..., None]
    attention_output = (summed / totals[..., None]).astype(jnp.bfloat16).reshape(
        row_count, own_heads * head_size
    )

    partial_proj = jnp.dot(attention_output, out_proj, preferred_element_type=jnp.float32)
    projected = jnp.sum(lax.all_gather(partial_proj, "tp", axis=0), axis=0)
    residual = hidden_full.astype(jnp.float32) + projected
    mean_square = jnp.mean(residual * residual, axis=1, keepdims=True)
    normed = (residual * lax.rsqrt(mean_square + norm_eps) * norm_gain[None, :]).astype(jnp.bfloat16)
    residual_own = lax.dynamic_slice_in_dim(residual, tp_index * own_width, own_width, 1)

    local_count = gate_up.shape[0]
    block_total = local_count * req_count
    split_count = max(1, block_total // EXPERTS)
    expert_range = jnp.arange(EXPERTS, dtype=jnp.int32)
    member = jnp.any(expert_ids[:, :, None] == expert_range[None, None, :], axis=1)
    member_int = member.astype(jnp.int32)
    slot_of = jnp.cumsum(member_int, axis=0, dtype=jnp.int32) - member_int
    slot_taken = jnp.take_along_axis(slot_of, expert_ids, axis=1)
    block_taken = (slot_taken % split_count) * EXPERTS + expert_ids
    block_range = jnp.arange(block_total, dtype=jnp.int32)
    block_weights = jnp.sum(
        jnp.where(block_taken[:, :, None] == block_range[None, None, :], router_weights[:, :, None], 0.0),
        axis=1,
    )

    if req_count <= 16:
        def gather_req(value):
            arrived = [value] + [
                lax.ppermute(value, "req", [(i, (i + shift) % req_count) for i in range(req_count)])
                for shift in range(1, req_count)
            ]
            order = (req_index - jnp.arange(req_count, dtype=jnp.int32)) % req_count
            arrived = jnp.take(jnp.stack(arrived, axis=0), order, axis=0)
            return arrived.reshape((req_count * value.shape[0],) + value.shape[1:])
    else:
        def gather_req(value):
            return lax.all_gather(value, "req", axis=0, tiled=True)
    weight_high = lax.reduce_precision(block_weights, exponent_bits=8, mantissa_bits=7)
    weight_rest = block_weights - weight_high
    weight_mid = lax.reduce_precision(weight_rest, exponent_bits=8, mantissa_bits=7)
    weight_low = weight_rest - weight_mid
    code = jnp.stack(
        [weight_high.astype(jnp.bfloat16), weight_mid.astype(jnp.bfloat16), weight_low.astype(jnp.bfloat16)],
        axis=0,
    ).reshape(-1)
    group_rows = -(-(row_count + -(-code.shape[0] // model_width)) // 16) * 16
    code_rows = group_rows - row_count
    code = jnp.pad(code, (0, code_rows * model_width - code.shape[0])).reshape(code_rows, model_width)
    message = jnp.concatenate([normed, code], axis=0)
    message_all = gather_req(message).reshape(req_count, group_rows, model_width)
    pieces = message_all[:, row_count:].reshape(req_count, code_rows * model_width)
    pieces = pieces[:, : 3 * row_count * block_total].astype(jnp.float32)
    pieces = pieces.reshape(req_count, 3, row_count, block_total)
    weights_all = (pieces[:, 0] + pieces[:, 1]) + pieces[:, 2]
    weights_own = lax.dynamic_slice_in_dim(weights_all, req_index * local_count, local_count, 2)
    weights_own = jnp.pad(weights_own, ((0, 0), (0, code_rows), (0, 0)))
    weights_own = weights_own.reshape(req_count * group_rows, local_count)

    mixed = expert_mix(
        message_all.reshape(req_count * group_rows, model_width),
        gate_up,
        down,
        weights_own,
        group_rows,
        row_count,
        tp_count,
    )
    mixed = lax.all_to_all(mixed, ("req", "tp"), 0, 0, tiled=True)
    mixed = jnp.sum(mixed.astype(jnp.float32), axis=0)
    return (residual_own + mixed).astype(jnp.bfloat16)


def solution(mesh):
    placed = (
        P("req", "tp"),
        P("req", "tp"),
        P("req", None, None),
        P("req"),
        P("req", None),
        P(("req", "tp"), None, None, None),
        P("tp", None),
        P(),
        P("req", None),
        P("req", None),
        P("req", None, None, "tp"),
        P("req", "tp", None),
    )
    return jax.shard_map(
        per_device, mesh=mesh, in_specs=placed, out_specs=P("req", "tp"), check_vma=False
    )
```

```python
import functools
import math

import jax
import jax.numpy as jnp
from jax import lax
from jax.experimental import pallas as pl
from jax.experimental.pallas import tpu as pltpu
from jax.sharding import PartitionSpec as P

EXPERTS = 32


rope_base = 1000000.0
norm_eps = 1e-06
neg_floor = -1e30


def apply_rotary_heads(values, positions, head_size):
    half_size = head_size // 2
    exponents = jnp.arange(half_size, dtype=jnp.float32) * (2.0 / head_size)
    inverse_freq = jnp.power(jnp.float32(rope_base), -exponents)
    angles = positions.astype(jnp.float32)[:, None] * inverse_freq[None, :]
    cosine = jnp.cos(angles)[:, None, :]
    sine = jnp.sin(angles)[:, None, :]
    first_half = values[..., :half_size]
    second_half = values[..., half_size:]
    return jnp.concatenate(
        [first_half * cosine - second_half * sine, second_half * cosine + first_half * sine],
        axis=-1,
    )


def _expert_body(x_ref, gu_ref, dn_ref, w_ref, o_ref, acc_ref, *, group_rows, row_count, tp_count):
    block = pl.program_id(1)

    @pl.when(block == 0)
    def _():
        acc_ref[...] = jnp.zeros_like(acc_ref)

    x = x_ref[...]
    contract_rows = (((1,), (1,)), ((), ()))
    gate_part = lax.dot_general(x, gu_ref[0, 0], contract_rows, preferred_element_type=jnp.float32)
    up_part = lax.dot_general(x, gu_ref[0, 1], contract_rows, preferred_element_type=jnp.float32)
    activation = (jnp.maximum(gate_part, 0.0) * up_part).astype(jnp.bfloat16)
    produced = jnp.dot(activation, dn_ref[0], preferred_element_type=jnp.float32)
    produced = produced.astype(jnp.bfloat16).astype(jnp.float32)
    weights = w_ref[...]
    lanes = lax.broadcasted_iota(jnp.int32, weights.shape, 1)
    chosen = jnp.sum(jnp.where(lanes == block, weights, 0.0), axis=1, keepdims=True)
    acc_ref[...] += chosen * produced

    @pl.when(block == pl.num_programs(1) - 1)
    def _():
        own_width = o_ref.shape[2]
        for group in range(x_ref.shape[0] // group_rows):
            for part in range(tp_count):
                o_ref[group * tp_count + part] = acc_ref[
                    group * group_rows : group * group_rows + row_count,
                    part * own_width : (part + 1) * own_width,
                ].astype(o_ref.dtype)


def expert_mix(rows, gate_up, down, weights, group_rows, row_count, tp_count):
    row_total, width = rows.shape
    local_count, _, _, hidden = gate_up.shape
    group_total = row_total // group_rows
    tile_groups = math.gcd(group_total, 8)
    tile = tile_groups * group_rows
    own_width = width // tp_count
    gate_up_t = jnp.swapaxes(gate_up, 2, 3)
    body = functools.partial(
        _expert_body, group_rows=group_rows, row_count=row_count, tp_count=tp_count
    )
    return pl.pallas_call(
        body,
        grid=(group_total // tile_groups, local_count),
        in_specs=[
            pl.BlockSpec((tile, width), lambda i, b: (i, 0)),
            pl.BlockSpec((1, 2, hidden, width), lambda i, b: (b, 0, 0, 0)),
            pl.BlockSpec((1, hidden, width), lambda i, b: (b, 0, 0)),
            pl.BlockSpec((tile, local_count), lambda i, b: (i, 0)),
        ],
        out_specs=pl.BlockSpec((tile_groups * tp_count, row_count, own_width), lambda i, b: (i, 0, 0)),
        out_shape=jax.ShapeDtypeStruct((group_total * tp_count, row_count, own_width), jnp.bfloat16),
        scratch_shapes=[pltpu.VMEM((tile, width), jnp.float32)],
        compiler_params=pltpu.CompilerParams(dimension_semantics=("parallel", "arbitrary")),
    )(rows, gate_up_t, down, weights)


def per_device(
    hidden_in,
    queries,
    fresh_key_value,
    positions,
    lengths,
    cache,
    out_proj,
    norm_gain,
    expert_ids,
    router_weights,
    gate_up,
    down,
):
    tp_count = lax.axis_size("tp")
    req_count = lax.axis_size("req")
    tp_index = lax.axis_index("tp")
    req_index = lax.axis_index("req")
    row_count = hidden_in.shape[0]
    head_size = cache.shape[3]
    kv_count = cache.shape[2]
    own_heads = queries.shape[1] // head_size
    head_count = own_heads * tp_count
    request_group_size = head_count // kv_count
    score_scaling = head_size ** (-0.5)
    model_width = norm_gain.shape[0]
    own_width = hidden_in.shape[1]
    first_head = tp_index * own_heads
    span_rows = cache.shape[0]

    q_local = apply_rotary_heads(
        queries.reshape(row_count, own_heads, head_size).astype(jnp.float32), positions, head_size
    ).astype(jnp.bfloat16)
    packed = jnp.stack([q_local.reshape(row_count, own_width), hidden_in], axis=0)
    gathered = lax.all_gather(packed, "tp", axis=0)
    q_all = jnp.transpose(gathered[:, 0], (1, 0, 2)).reshape(
        row_count, kv_count, request_group_size, head_size
    )
    hidden_full = jnp.transpose(gathered[:, 1], (1, 0, 2)).reshape(row_count, model_width)

    k_new = apply_rotary_heads(
        fresh_key_value[:, 0].reshape(row_count, kv_count, head_size).astype(jnp.float32),
        positions,
        head_size,
    ).astype(jnp.bfloat16)
    value_fresh = fresh_key_value[:, 1].reshape(row_count, kv_count, head_size)
    own_score = (
        jnp.einsum("rcgd,rcd->rcg", q_all, k_new, preferred_element_type=jnp.float32)
        * score_scaling
    )

    segment_ends = jnp.cumsum(lengths[0], dtype=jnp.int32)
    segment_starts = segment_ends - lengths[0]
    cache_spots = tp_index * span_rows + jnp.arange(span_rows, dtype=jnp.int32)
    mask = (cache_spots[None, :] >= segment_starts[:, None]) & (
        cache_spots[None, :] < segment_ends[:, None]
    )
    mask = mask[:, None, None, :]
    keys = cache[:, 0]
    values = cache[:, 1]
    scores = (
        jnp.einsum("rcgd,jcd->rcgj", q_all, keys, preferred_element_type=jnp.float32)
        * score_scaling
    )
    scores = jnp.where(mask, scores, neg_floor)
    highest_local = jnp.max(scores, axis=3)
    weights = jnp.where(mask, jnp.exp(scores - highest_local[..., None]), 0.0)
    totals_local = jnp.sum(weights, axis=3)
    sums_local = jnp.einsum(
        "rcgj,jcd->rcgd",
        weights,
        values.astype(jnp.float32),
        precision=lax.Precision.HIGHEST,
        preferred_element_type=jnp.float32,
    )
    states = jnp.concatenate(
        [highest_local[..., None], totals_local[..., None], sums_local], axis=3
    ).reshape(row_count, tp_count, own_heads, head_size + 2)
    all_states = lax.all_to_all(
        jnp.transpose(states, (1, 0, 2, 3)), "tp", 0, 0, tiled=True
    )
    parts_highest = all_states[..., 0]
    parts_totals = all_states[..., 1]
    parts_sums = all_states[..., 2:]
    own_slice = lax.dynamic_slice_in_dim(own_score.reshape(row_count, head_count), first_head, own_heads, 1)
    top_score = jnp.maximum(jnp.max(parts_highest, axis=0), own_slice)
    factors = jnp.exp(parts_highest - top_score[None])
    own_part = jnp.exp(own_slice - top_score)
    head_kv = (first_head + jnp.arange(own_heads, dtype=jnp.int32)) // request_group_size
    own_values = jnp.take(value_fresh, head_kv, axis=1).astype(jnp.float32)
    totals = jnp.sum(parts_totals * factors, axis=0) + own_part
    summed = jnp.sum(parts_sums * factors[..., None], axis=0) + own_values * own_part[..., None]
    attention_output = (summed / totals[..., None]).astype(jnp.bfloat16).reshape(
        row_count, own_heads * head_size
    )

    partial_proj = jnp.dot(attention_output, out_proj, preferred_element_type=jnp.float32)
    projected = jnp.sum(lax.all_gather(partial_proj, "tp", axis=0), axis=0)
    residual = hidden_full.astype(jnp.float32) + projected
    mean_square = jnp.mean(residual * residual, axis=1, keepdims=True)
    normed = (residual * lax.rsqrt(mean_square + norm_eps) * norm_gain[None, :]).astype(jnp.bfloat16)
    residual_own = lax.dynamic_slice_in_dim(residual, tp_index * own_width, own_width, 1)

    local_count = gate_up.shape[0]
    block_total = local_count * req_count
    split_count = max(1, block_total // EXPERTS)
    expert_range = jnp.arange(EXPERTS, dtype=jnp.int32)
    member = jnp.any(expert_ids[:, :, None] == expert_range[None, None, :], axis=1)
    member_int = member.astype(jnp.int32)
    slot_of = jnp.cumsum(member_int, axis=0, dtype=jnp.int32) - member_int
    slot_taken = jnp.take_along_axis(slot_of, expert_ids, axis=1)
    block_taken = (slot_taken % split_count) * EXPERTS + expert_ids
    block_range = jnp.arange(block_total, dtype=jnp.int32)
    block_weights = jnp.sum(
        jnp.where(block_taken[:, :, None] == block_range[None, None, :], router_weights[:, :, None], 0.0),
        axis=1,
    )

    def gather_req(value):
        if req_count > 16 or (req_count - 1) % tp_count != tp_count - 1 or req_count < tp_count:
            return lax.all_gather(value, "req", axis=0, tiled=True)
        per_tp = (req_count + tp_count - 1) // tp_count
        fetched = []
        for slot in range(per_tp):
            pairs = []
            for group in range(req_count):
                for part in range(tp_count):
                    shift = per_tp * part + slot + 1
                    if shift < req_count:
                        source = ((group - shift) % req_count) * tp_count + part
                        pairs.append((source, group * tp_count + part))
            moved = lax.ppermute(value, ("req", "tp"), pairs)
            shift_here = per_tp * tp_index + slot + 1
            fetched.append(jnp.where(shift_here < req_count, moved, value))
        shared = lax.all_gather(jnp.stack(fetched, axis=0), "tp", axis=0)
        shifts = (per_tp * jnp.arange(tp_count, dtype=jnp.int32)[:, None] + jnp.arange(per_tp, dtype=jnp.int32)[None, :] + 1) % req_count
        shared = shared.reshape((tp_count * per_tp,) + value.shape)
        groups = ((req_index - shifts.reshape(-1)) % req_count).astype(jnp.int32)
        order = jnp.argsort(groups)
        arrived = jnp.take(shared, order, axis=0)
        return arrived.reshape((req_count * value.shape[0],) + value.shape[1:])

    weight_high = lax.reduce_precision(block_weights, exponent_bits=8, mantissa_bits=7)
    weight_rest = block_weights - weight_high
    weight_mid = lax.reduce_precision(weight_rest, exponent_bits=8, mantissa_bits=7)
    weight_low = weight_rest - weight_mid
    code = jnp.stack(
        [weight_high.astype(jnp.bfloat16), weight_mid.astype(jnp.bfloat16), weight_low.astype(jnp.bfloat16)],
        axis=0,
    ).reshape(-1)
    group_rows = -(-(row_count + -(-code.shape[0] // model_width)) // 16) * 16
    code_rows = group_rows - row_count
    code = jnp.pad(code, (0, code_rows * model_width - code.shape[0])).reshape(code_rows, model_width)
    message = jnp.concatenate([normed, code], axis=0)
    message_all = gather_req(message).reshape(req_count, group_rows, model_width)
    pieces = message_all[:, row_count:].reshape(req_count, code_rows * model_width)
    pieces = pieces[:, : 3 * row_count * block_total].astype(jnp.float32)
    pieces = pieces.reshape(req_count, 3, row_count, block_total)
    weights_all = (pieces[:, 0] + pieces[:, 1]) + pieces[:, 2]
    weights_own = lax.dynamic_slice_in_dim(weights_all, req_index * local_count, local_count, 2)
    weights_own = jnp.pad(weights_own, ((0, 0), (0, code_rows), (0, 0)))
    weights_own = weights_own.reshape(req_count * group_rows, local_count)

    mixed = expert_mix(
        message_all.reshape(req_count * group_rows, model_width),
        gate_up,
        down,
        weights_own,
        group_rows,
        row_count,
        tp_count,
    )
    mixed = lax.all_to_all(mixed, ("req", "tp"), 0, 0, tiled=True)
    mixed = jnp.sum(mixed.astype(jnp.float32), axis=0)
    return (residual_own + mixed).astype(jnp.bfloat16)


def solution(mesh):
    placed = (
        P("req", "tp"),
        P("req", "tp"),
        P("req", None, None),
        P("req"),
        P("req", None),
        P(("req", "tp"), None, None, None),
        P("tp", None),
        P(),
        P("req", None),
        P("req", None),
        P("req", None, None, "tp"),
        P("req", "tp", None),
    )
    return jax.shard_map(
        per_device, mesh=mesh, in_specs=placed, out_specs=P("req", "tp"), check_vma=False
    )
```

```python
import functools
import math

import jax
import jax.numpy as jnp
from jax import lax
from jax.experimental import pallas as pl
from jax.experimental.pallas import tpu as pltpu
from jax.sharding import PartitionSpec as P

EXPERTS = 32


rope_base = 1000000.0
norm_eps = 1e-06
neg_floor = -1e30


def apply_rotary_flat(values, positions, head_size):
    half_size = head_size // 2
    head_total = values.shape[1] // head_size
    exponents = jnp.arange(half_size, dtype=jnp.float32) * (2.0 / head_size)
    inverse_freq = jnp.power(jnp.float32(rope_base), -exponents)
    angles = positions.astype(jnp.float32)[:, None] * inverse_freq[None, :]
    cosine = jnp.cos(angles)
    sine = jnp.sin(angles)
    cosine_full = jnp.tile(jnp.concatenate([cosine, cosine], axis=1), (1, head_total))
    sine_full = jnp.tile(jnp.concatenate([-sine, sine], axis=1), (1, head_total))
    values = values.astype(jnp.float32)
    swapped = jnp.concatenate(
        [
            piece
            for head in range(head_total)
            for piece in (
                values[:, head * head_size + half_size : (head + 1) * head_size],
                values[:, head * head_size : head * head_size + half_size],
            )
        ],
        axis=1,
    )
    return values * cosine_full + swapped * sine_full


def _expert_body(x_ref, gu_ref, dn_ref, w_ref, o_ref, acc_ref, *, group_rows, row_count, tp_count):
    block = pl.program_id(1)

    @pl.when(block == 0)
    def _():
        acc_ref[...] = jnp.zeros_like(acc_ref)

    x = x_ref[...]
    contract_rows = (((1,), (1,)), ((), ()))
    gate_part = lax.dot_general(x, gu_ref[0, 0], contract_rows, preferred_element_type=jnp.float32)
    up_part = lax.dot_general(x, gu_ref[0, 1], contract_rows, preferred_element_type=jnp.float32)
    activation = (jnp.maximum(gate_part, 0.0) * up_part).astype(jnp.bfloat16)
    produced = jnp.dot(activation, dn_ref[0], preferred_element_type=jnp.float32)
    produced = produced.astype(jnp.bfloat16).astype(jnp.float32)
    weights = w_ref[...]
    lanes = lax.broadcasted_iota(jnp.int32, weights.shape, 1)
    chosen = jnp.sum(jnp.where(lanes == block, weights, 0.0), axis=1, keepdims=True)
    acc_ref[...] += chosen * produced

    @pl.when(block == pl.num_programs(1) - 1)
    def _():
        own_width = o_ref.shape[2]
        for group in range(x_ref.shape[0] // group_rows):
            for part in range(tp_count):
                o_ref[group * tp_count + part] = acc_ref[
                    group * group_rows : group * group_rows + row_count,
                    part * own_width : (part + 1) * own_width,
                ].astype(o_ref.dtype)


def expert_mix(rows, gate_up, down, weights, group_rows, row_count, tp_count):
    row_total, width = rows.shape
    local_count, _, _, hidden = gate_up.shape
    group_total = row_total // group_rows
    tile_groups = math.gcd(group_total, 8)
    tile = tile_groups * group_rows
    own_width = width // tp_count
    gate_up_t = jnp.swapaxes(gate_up, 2, 3)
    body = functools.partial(
        _expert_body, group_rows=group_rows, row_count=row_count, tp_count=tp_count
    )
    return pl.pallas_call(
        body,
        grid=(group_total // tile_groups, local_count),
        in_specs=[
            pl.BlockSpec((tile, width), lambda i, b: (i, 0)),
            pl.BlockSpec((1, 2, hidden, width), lambda i, b: (b, 0, 0, 0)),
            pl.BlockSpec((1, hidden, width), lambda i, b: (b, 0, 0)),
            pl.BlockSpec((tile, local_count), lambda i, b: (i, 0)),
        ],
        out_specs=pl.BlockSpec((tile_groups * tp_count, row_count, own_width), lambda i, b: (i, 0, 0)),
        out_shape=jax.ShapeDtypeStruct((group_total * tp_count, row_count, own_width), jnp.bfloat16),
        scratch_shapes=[pltpu.VMEM((tile, width), jnp.float32)],
        compiler_params=pltpu.CompilerParams(dimension_semantics=("parallel", "arbitrary")),
    )(rows, gate_up_t, down, weights)


def per_device(
    hidden_in,
    queries,
    fresh_key_value,
    positions,
    lengths,
    cache,
    out_proj,
    norm_gain,
    expert_ids,
    router_weights,
    gate_up,
    down,
):
    tp_count = lax.axis_size("tp")
    req_count = lax.axis_size("req")
    tp_index = lax.axis_index("tp")
    req_index = lax.axis_index("req")
    row_count = hidden_in.shape[0]
    head_size = cache.shape[3]
    kv_count = cache.shape[2]
    own_heads = queries.shape[1] // head_size
    head_count = own_heads * tp_count
    request_group_size = head_count // kv_count
    score_scaling = head_size ** (-0.5)
    model_width = norm_gain.shape[0]
    own_width = hidden_in.shape[1]
    first_head = tp_index * own_heads
    span_rows = cache.shape[0]

    q_local = apply_rotary_flat(queries, positions, head_size).astype(jnp.bfloat16)
    packed = jnp.stack([q_local, hidden_in], axis=0)
    gathered = lax.all_gather(packed, "tp", axis=0)
    q_all = jnp.transpose(gathered[:, 0], (1, 0, 2)).reshape(
        row_count, kv_count, request_group_size, head_size
    )
    hidden_full = jnp.transpose(gathered[:, 1], (1, 0, 2)).reshape(row_count, model_width)

    k_new = apply_rotary_flat(fresh_key_value[:, 0], positions, head_size).astype(jnp.bfloat16)
    k_new = k_new.reshape(row_count, kv_count, head_size)
    value_fresh = fresh_key_value[:, 1].reshape(row_count, kv_count, head_size)
    own_score = (
        jnp.einsum("rcgd,rcd->rcg", q_all, k_new, preferred_element_type=jnp.float32)
        * score_scaling
    )

    segment_ends = jnp.cumsum(lengths[0], dtype=jnp.int32)
    segment_starts = segment_ends - lengths[0]
    cache_spots = tp_index * span_rows + jnp.arange(span_rows, dtype=jnp.int32)
    mask = (cache_spots[None, :] >= segment_starts[:, None]) & (
        cache_spots[None, :] < segment_ends[:, None]
    )
    mask = mask[:, None, None, :]
    keys = cache[:, 0]
    values = cache[:, 1]
    scores = (
        jnp.einsum("rcgd,jcd->rcgj", q_all, keys, preferred_element_type=jnp.float32)
        * score_scaling
    )
    scores = jnp.where(mask, scores, neg_floor)
    highest_local = jnp.max(scores, axis=3)
    weights = jnp.where(mask, jnp.exp(scores - highest_local[..., None]), 0.0)
    totals_local = jnp.sum(weights, axis=3)
    sums_local = jnp.einsum(
        "rcgj,jcd->rcgd",
        weights,
        values.astype(jnp.float32),
        precision=lax.Precision.HIGHEST,
        preferred_element_type=jnp.float32,
    )
    states = jnp.concatenate(
        [highest_local[..., None], totals_local[..., None], sums_local], axis=3
    ).reshape(row_count, tp_count, own_heads, head_size + 2)
    all_states = lax.all_to_all(
        jnp.transpose(states, (1, 0, 2, 3)), "tp", 0, 0, tiled=True
    )
    parts_highest = all_states[..., 0]
    parts_totals = all_states[..., 1]
    parts_sums = all_states[..., 2:]
    own_slice = lax.dynamic_slice_in_dim(own_score.reshape(row_count, head_count), first_head, own_heads, 1)
    top_score = jnp.maximum(jnp.max(parts_highest, axis=0), own_slice)
    factors = jnp.exp(parts_highest - top_score[None])
    own_part = jnp.exp(own_slice - top_score)
    head_kv = (first_head + jnp.arange(own_heads, dtype=jnp.int32)) // request_group_size
    own_values = jnp.take(value_fresh, head_kv, axis=1).astype(jnp.float32)
    totals = jnp.sum(parts_totals * factors, axis=0) + own_part
    summed = jnp.sum(parts_sums * factors[..., None], axis=0) + own_values * own_part[..., None]
    attention_output = (summed / totals[..., None]).astype(jnp.bfloat16).reshape(
        row_count, own_heads * head_size
    )

    partial_proj = jnp.dot(attention_output, out_proj, preferred_element_type=jnp.float32)
    projected = jnp.sum(lax.all_gather(partial_proj, "tp", axis=0), axis=0)
    residual = hidden_full.astype(jnp.float32) + projected
    mean_square = jnp.mean(residual * residual, axis=1, keepdims=True)
    normed = (residual * lax.rsqrt(mean_square + norm_eps) * norm_gain[None, :]).astype(jnp.bfloat16)
    residual_own = lax.dynamic_slice_in_dim(residual, tp_index * own_width, own_width, 1)

    local_count = gate_up.shape[0]
    block_total = local_count * req_count
    split_count = max(1, block_total // EXPERTS)
    expert_range = jnp.arange(EXPERTS, dtype=jnp.int32)
    member = jnp.any(expert_ids[:, :, None] == expert_range[None, None, :], axis=1)
    member_int = member.astype(jnp.int32)
    slot_of = jnp.cumsum(member_int, axis=0, dtype=jnp.int32) - member_int
    slot_taken = jnp.take_along_axis(slot_of, expert_ids, axis=1)
    block_taken = (slot_taken % split_count) * EXPERTS + expert_ids
    block_range = jnp.arange(block_total, dtype=jnp.int32)
    block_weights = jnp.sum(
        jnp.where(block_taken[:, :, None] == block_range[None, None, :], router_weights[:, :, None], 0.0),
        axis=1,
    )

    def gather_req(value):
        if req_count > 16 or (req_count - 1) % tp_count != tp_count - 1 or req_count < tp_count:
            return lax.all_gather(value, "req", axis=0, tiled=True)
        per_tp = (req_count + tp_count - 1) // tp_count
        fetched = []
        for slot in range(per_tp):
            pairs = []
            for group in range(req_count):
                for part in range(tp_count):
                    shift = per_tp * part + slot + 1
                    source = ((group - shift) % req_count) * tp_count + part
                    pairs.append((source, group * tp_count + part))
            moved = lax.ppermute(value, ("req", "tp"), pairs)
            fetched.append(lax.ppermute(value, ("req", "tp"), pairs))
        shared = lax.all_gather(jnp.stack(fetched, axis=0), "tp", axis=0)
        shared = shared.reshape((tp_count * per_tp,) + value.shape)
        order = (req_index - jnp.arange(req_count, dtype=jnp.int32) - 1) % req_count
        arrived = jnp.take(shared, order, axis=0)
        return arrived.reshape((req_count * value.shape[0],) + value.shape[1:])

    weight_high = lax.reduce_precision(block_weights, exponent_bits=8, mantissa_bits=7)
    weight_rest = block_weights - weight_high
    weight_mid = lax.reduce_precision(weight_rest, exponent_bits=8, mantissa_bits=7)
    weight_low = weight_rest - weight_mid
    code = jnp.stack(
        [weight_high.astype(jnp.bfloat16), weight_mid.astype(jnp.bfloat16), weight_low.astype(jnp.bfloat16)],
        axis=0,
    ).reshape(-1)
    group_rows = -(-(row_count + -(-code.shape[0] // model_width)) // 16) * 16
    code_rows = group_rows - row_count
    code = jnp.pad(code, (0, code_rows * model_width - code.shape[0])).reshape(code_rows, model_width)
    message = jnp.concatenate([normed, code], axis=0)
    message_all = gather_req(message).reshape(req_count, group_rows, model_width)
    pieces = message_all[:, row_count:].reshape(req_count, code_rows * model_width)
    pieces = pieces[:, : 3 * row_count * block_total].astype(jnp.float32)
    pieces = pieces.reshape(req_count, 3, row_count, block_total)
    weights_all = (pieces[:, 0] + pieces[:, 1]) + pieces[:, 2]
    weights_own = lax.dynamic_slice_in_dim(weights_all, req_index * local_count, local_count, 2)
    weights_own = jnp.pad(weights_own, ((0, 0), (0, code_rows), (0, 0)))
    weights_own = weights_own.reshape(req_count * group_rows, local_count)

    mixed = expert_mix(
        message_all.reshape(req_count * group_rows, model_width),
        gate_up,
        down,
        weights_own,
        group_rows,
        row_count,
        tp_count,
    )
    mixed = lax.all_to_all(mixed, ("req", "tp"), 0, 0, tiled=True)
    mixed = jnp.sum(mixed.astype(jnp.float32), axis=0)
    return (residual_own + mixed).astype(jnp.bfloat16)


def solution(mesh):
    placed = (
        P("req", "tp"),
        P("req", "tp"),
        P("req", None, None),
        P("req"),
        P("req", None),
        P(("req", "tp"), None, None, None),
        P("tp", None),
        P(),
        P("req", None),
        P("req", None),
        P("req", None, None, "tp"),
        P("req", "tp", None),
    )
    return jax.shard_map(
        per_device, mesh=mesh, in_specs=placed, out_specs=P("req", "tp"), check_vma=False
    )
```

```python
import functools
import math

import jax
import jax.numpy as jnp
from jax import lax
from jax.experimental import pallas as pl
from jax.experimental.pallas import tpu as pltpu
from jax.sharding import PartitionSpec as P

EXPERTS = 32


rope_base = 1000000.0
norm_eps = 1e-06
neg_floor = -1e30


def apply_rotary_heads(values, positions, head_size):
    half_size = head_size // 2
    exponents = jnp.arange(half_size, dtype=jnp.float32) * (2.0 / head_size)
    inverse_freq = jnp.power(jnp.float32(rope_base), -exponents)
    angles = positions.astype(jnp.float32)[:, None] * inverse_freq[None, :]
    cosine = jnp.cos(angles)[:, None, :]
    sine = jnp.sin(angles)[:, None, :]
    first_half = values[..., :half_size]
    second_half = values[..., half_size:]
    return jnp.concatenate(
        [first_half * cosine - second_half * sine, second_half * cosine + first_half * sine],
        axis=-1,
    )


def _expert_body(
    offset_ref, x_ref, gu_ref, dn_ref, o_ref, acc_ref, *, width, block_total, row_count, tp_count
):
    block = pl.program_id(1)

    @pl.when(block == 0)
    def _():
        acc_ref[...] = jnp.zeros_like(acc_ref)

    x = x_ref[:, :width]
    contract_rows = (((1,), (1,)), ((), ()))
    gate_part = lax.dot_general(x, gu_ref[0, 0], contract_rows, preferred_element_type=jnp.float32)
    up_part = lax.dot_general(x, gu_ref[0, 1], contract_rows, preferred_element_type=jnp.float32)
    activation = (jnp.maximum(gate_part, 0.0) * up_part).astype(jnp.bfloat16)
    produced = jnp.dot(activation, dn_ref[0], preferred_element_type=jnp.float32)
    produced = produced.astype(jnp.bfloat16).astype(jnp.float32)
    code = x_ref[:, width:].astype(jnp.float32)
    lanes = lax.broadcasted_iota(jnp.int32, code.shape, 1)
    column = offset_ref[0] + block
    chosen = jnp.sum(jnp.where(lanes == column, code, 0.0), axis=1, keepdims=True)
    chosen = chosen + jnp.sum(jnp.where(lanes == column + block_total, code, 0.0), axis=1, keepdims=True)
    chosen = chosen + jnp.sum(jnp.where(lanes == column + 2 * block_total, code, 0.0), axis=1, keepdims=True)
    acc_ref[...] += chosen * produced

    @pl.when(block == pl.num_programs(1) - 1)
    def _():
        own_width = o_ref.shape[2]
        for group in range(x_ref.shape[0] // row_count):
            for part in range(tp_count):
                o_ref[group * tp_count + part] = acc_ref[
                    group * row_count : (group + 1) * row_count,
                    part * own_width : (part + 1) * own_width,
                ].astype(o_ref.dtype)


def expert_mix(rows, gate_up, down, offset, width, block_total, row_count, tp_count):
    row_total, message_width = rows.shape
    local_count, _, _, hidden = gate_up.shape
    group_total = row_total // row_count
    tile_groups = math.gcd(group_total, 8)
    tile = tile_groups * row_count
    own_width = width // tp_count
    gate_up_t = jnp.swapaxes(gate_up, 2, 3)
    body = functools.partial(
        _expert_body, width=width, block_total=block_total, row_count=row_count, tp_count=tp_count
    )
    return pl.pallas_call(
        body,
        grid=(group_total // tile_groups, local_count),
        in_specs=[
            pl.BlockSpec(memory_space=pltpu.SMEM),
            pl.BlockSpec((tile, message_width), lambda i, b: (i, 0)),
            pl.BlockSpec((1, 2, hidden, width), lambda i, b: (b, 0, 0, 0)),
            pl.BlockSpec((1, hidden, width), lambda i, b: (b, 0, 0)),
        ],
        out_specs=pl.BlockSpec((tile_groups * tp_count, row_count, own_width), lambda i, b: (i, 0, 0)),
        out_shape=jax.ShapeDtypeStruct((group_total * tp_count, row_count, own_width), jnp.bfloat16),
        scratch_shapes=[pltpu.VMEM((tile, width), jnp.float32)],
        compiler_params=pltpu.CompilerParams(dimension_semantics=("parallel", "arbitrary")),
    )(offset, rows, gate_up_t, down)


def per_device(
    hidden_in,
    queries,
    fresh_key_value,
    positions,
    lengths,
    cache,
    out_proj,
    norm_gain,
    expert_ids,
    router_weights,
    gate_up,
    down,
):
    tp_count = lax.axis_size("tp")
    req_count = lax.axis_size("req")
    tp_index = lax.axis_index("tp")
    req_index = lax.axis_index("req")
    row_count = hidden_in.shape[0]
    head_size = cache.shape[3]
    kv_count = cache.shape[2]
    own_heads = queries.shape[1] // head_size
    head_count = own_heads * tp_count
    request_group_size = head_count // kv_count
    score_scaling = head_size ** (-0.5)
    model_width = norm_gain.shape[0]
    own_width = hidden_in.shape[1]
    first_head = tp_index * own_heads
    span_rows = cache.shape[0]

    q_local = apply_rotary_heads(
        queries.reshape(row_count, own_heads, head_size).astype(jnp.float32), positions, head_size
    ).astype(jnp.bfloat16)
    packed = jnp.stack([q_local.reshape(row_count, own_width), hidden_in], axis=0)
    gathered = lax.all_gather(packed, "tp", axis=0)
    q_all = jnp.transpose(gathered[:, 0], (1, 0, 2)).reshape(
        row_count, kv_count, request_group_size, head_size
    )
    hidden_full = jnp.transpose(gathered[:, 1], (1, 0, 2)).reshape(row_count, model_width)

    k_new = apply_rotary_heads(
        fresh_key_value[:, 0].reshape(row_count, kv_count, head_size).astype(jnp.float32),
        positions,
        head_size,
    ).astype(jnp.bfloat16)
    value_fresh = fresh_key_value[:, 1].reshape(row_count, kv_count, head_size)
    own_score = (
        jnp.einsum("rcgd,rcd->rcg", q_all, k_new, preferred_element_type=jnp.float32)
        * score_scaling
    )

    segment_ends = jnp.cumsum(lengths[0], dtype=jnp.int32)
    segment_starts = segment_ends - lengths[0]
    cache_spots = tp_index * span_rows + jnp.arange(span_rows, dtype=jnp.int32)
    mask = (cache_spots[None, :] >= segment_starts[:, None]) & (
        cache_spots[None, :] < segment_ends[:, None]
    )
    mask = mask[:, None, None, :]
    keys = cache[:, 0]
    values = cache[:, 1]
    scores = (
        jnp.einsum("rcgd,jcd->rcgj", q_all, keys, preferred_element_type=jnp.float32)
        * score_scaling
    )
    scores = jnp.where(mask, scores, neg_floor)
    highest_local = jnp.max(scores, axis=3)
    weights = jnp.where(mask, jnp.exp(scores - highest_local[..., None]), 0.0)
    totals_local = jnp.sum(weights, axis=3)
    sums_local = jnp.einsum(
        "rcgj,jcd->rcgd",
        weights,
        values.astype(jnp.float32),
        precision=lax.Precision.HIGHEST,
        preferred_element_type=jnp.float32,
    )
    states = jnp.concatenate(
        [highest_local[..., None], totals_local[..., None], sums_local], axis=3
    ).reshape(row_count, tp_count, own_heads, head_size + 2)
    all_states = lax.all_to_all(
        jnp.transpose(states, (1, 0, 2, 3)), "tp", 0, 0, tiled=True
    )
    parts_highest = all_states[..., 0]
    parts_totals = all_states[..., 1]
    parts_sums = all_states[..., 2:]
    own_slice = lax.dynamic_slice_in_dim(own_score.reshape(row_count, head_count), first_head, own_heads, 1)
    top_score = jnp.maximum(jnp.max(parts_highest, axis=0), own_slice)
    factors = jnp.exp(parts_highest - top_score[None])
    own_part = jnp.exp(own_slice - top_score)
    if request_group_size % own_heads == 0:
        own_values = lax.dynamic_slice_in_dim(value_fresh, first_head // request_group_size, 1, 1)
        own_values = own_values.astype(jnp.float32)
    else:
        head_kv = (first_head + jnp.arange(own_heads, dtype=jnp.int32)) // request_group_size
        own_values = jnp.take(value_fresh, head_kv, axis=1).astype(jnp.float32)
    totals = jnp.sum(parts_totals * factors, axis=0) + own_part
    summed = jnp.sum(parts_sums * factors[..., None], axis=0) + own_values * own_part[..., None]
    attention_output = (summed / totals[..., None]).astype(jnp.bfloat16).reshape(
        row_count, own_heads * head_size
    )

    partial_proj = jnp.dot(attention_output, out_proj, preferred_element_type=jnp.float32)
    projected = jnp.sum(lax.all_gather(partial_proj, "tp", axis=0), axis=0)
    residual = hidden_full.astype(jnp.float32) + projected
    mean_square = jnp.mean(residual * residual, axis=1, keepdims=True)
    normed = (residual * lax.rsqrt(mean_square + norm_eps) * norm_gain[None, :]).astype(jnp.bfloat16)
    residual_own = lax.dynamic_slice_in_dim(residual, tp_index * own_width, own_width, 1)

    local_count = gate_up.shape[0]
    block_total = local_count * req_count
    split_count = max(1, block_total // EXPERTS)
    expert_range = jnp.arange(EXPERTS, dtype=jnp.int32)
    member = jnp.any(expert_ids[:, :, None] == expert_range[None, None, :], axis=1)
    member_int = member.astype(jnp.int32)
    slot_of = jnp.cumsum(member_int, axis=0, dtype=jnp.int32) - member_int
    slot_taken = jnp.take_along_axis(slot_of, expert_ids, axis=1)
    block_taken = (slot_taken % split_count) * EXPERTS + expert_ids
    block_range = jnp.arange(block_total, dtype=jnp.int32)
    block_weights = jnp.sum(
        jnp.where(block_taken[:, :, None] == block_range[None, None, :], router_weights[:, :, None], 0.0),
        axis=1,
    )

    def gather_req(value):
        if req_count > 16 or (req_count - 1) % tp_count != tp_count - 1 or req_count < tp_count:
            return lax.all_gather(value, "req", axis=0, tiled=True)
        per_tp = (req_count + tp_count - 1) // tp_count
        fetched = []
        for slot in range(per_tp):
            pairs = []
            for group in range(req_count):
                for part in range(tp_count):
                    shift = per_tp * part + slot + 1
                    source = ((group - shift) % req_count) * tp_count + part
                    pairs.append((source, group * tp_count + part))
            moved = lax.ppermute(value, ("req", "tp"), pairs)
            fetched.append(lax.ppermute(value, ("req", "tp"), pairs))
        shared = lax.all_gather(jnp.stack(fetched, axis=0), "tp", axis=0)
        shared = shared.reshape((tp_count * per_tp,) + value.shape)
        order = (req_index - jnp.arange(req_count, dtype=jnp.int32) - 1) % req_count
        arrived = jnp.take(shared, order, axis=0)
        return arrived.reshape((req_count * value.shape[0],) + value.shape[1:])

    weight_high = lax.reduce_precision(block_weights, exponent_bits=8, mantissa_bits=7)
    weight_rest = block_weights - weight_high
    weight_mid = lax.reduce_precision(weight_rest, exponent_bits=8, mantissa_bits=7)
    weight_low = weight_rest - weight_mid
    code = jnp.concatenate([weight_high, weight_mid, weight_low], axis=1).astype(jnp.bfloat16)
    code_lanes = -(-code.shape[1] // 128) * 128
    code = jnp.pad(code, ((0, 0), (0, code_lanes - code.shape[1])))
    message = jnp.concatenate([normed, code], axis=1)
    message_all = gather_req(message)
    offset = (req_index * local_count).astype(jnp.int32).reshape(1)
    mixed = expert_mix(
        message_all, gate_up, down, offset, model_width, block_total, row_count, tp_count
    )
    mixed = lax.all_to_all(mixed, ("req", "tp"), 0, 0, tiled=True)
    mixed = jnp.sum(mixed.astype(jnp.float32), axis=0)
    return (residual_own + mixed).astype(jnp.bfloat16)


def solution(mesh):
    placed = (
        P("req", "tp"),
        P("req", "tp"),
        P("req", None, None),
        P("req"),
        P("req", None),
        P(("req", "tp"), None, None, None),
        P("tp", None),
        P(),
        P("req", None),
        P("req", None),
        P("req", None, None, "tp"),
        P("req", "tp", None),
    )
    return jax.shard_map(
        per_device, mesh=mesh, in_specs=placed, out_specs=P("req", "tp"), check_vma=False
    )
```

```python
import functools
import math

import jax
import jax.numpy as jnp
from jax import lax
from jax.experimental import pallas as pl
from jax.experimental.pallas import tpu as pltpu
from jax.sharding import PartitionSpec as P

EXPERTS = 32


rope_base = 1000000.0
norm_eps = 1e-06
neg_floor = -1e30


def apply_rotary_heads(values, positions, head_size):
    half_size = head_size // 2
    exponents = jnp.arange(half_size, dtype=jnp.float32) * (2.0 / head_size)
    inverse_freq = jnp.power(jnp.float32(rope_base), -exponents)
    angles = positions.astype(jnp.float32)[:, None] * inverse_freq[None, :]
    cosine = jnp.cos(angles)[:, None, :]
    sine = jnp.sin(angles)[:, None, :]
    first_half = values[..., :half_size]
    second_half = values[..., half_size:]
    return jnp.concatenate(
        [first_half * cosine - second_half * sine, second_half * cosine + first_half * sine],
        axis=-1,
    )


def _expert_body(
    offset_ref, dest_ref, x_ref, gu_ref, dn_ref, o_ref, acc_ref, *, width, block_total, row_count, tp_count
):
    block = pl.program_id(1)

    @pl.when(block == 0)
    def _():
        acc_ref[...] = jnp.zeros_like(acc_ref)

    x = x_ref[:, :width]
    contract_rows = (((1,), (1,)), ((), ()))
    gate_part = lax.dot_general(x, gu_ref[0, 0], contract_rows, preferred_element_type=jnp.float32)
    up_part = lax.dot_general(x, gu_ref[0, 1], contract_rows, preferred_element_type=jnp.float32)
    activation = (jnp.maximum(gate_part, 0.0) * up_part).astype(jnp.bfloat16)
    produced = jnp.dot(activation, dn_ref[0], preferred_element_type=jnp.float32)
    produced = produced.astype(jnp.bfloat16).astype(jnp.float32)
    code = x_ref[:, width:].astype(jnp.float32)
    lanes = lax.broadcasted_iota(jnp.int32, code.shape, 1)
    column = offset_ref[0] + block
    chosen = jnp.sum(jnp.where(lanes == column, code, 0.0), axis=1, keepdims=True)
    chosen = chosen + jnp.sum(jnp.where(lanes == column + block_total, code, 0.0), axis=1, keepdims=True)
    chosen = chosen + jnp.sum(jnp.where(lanes == column + 2 * block_total, code, 0.0), axis=1, keepdims=True)
    acc_ref[...] += chosen * produced

    @pl.when(block == pl.num_programs(1) - 1)
    def _():
        own_width = o_ref.shape[2]
        tile_groups = x_ref.shape[0] // row_count
        for group in range(tile_groups):
            dest = dest_ref[pl.program_id(0) * tile_groups + group] - pl.program_id(0) * tile_groups
            for part in range(tp_count):
                o_ref[dest * tp_count + part] = acc_ref[
                    group * row_count : (group + 1) * row_count,
                    part * own_width : (part + 1) * own_width,
                ].astype(o_ref.dtype)


def expert_mix(rows, gate_up, down, offset, dest, width, block_total, row_count, tp_count):
    row_total, message_width = rows.shape
    local_count, _, _, hidden = gate_up.shape
    group_total = row_total // row_count
    tile_groups = math.gcd(group_total, 8)
    tile = tile_groups * row_count
    own_width = width // tp_count
    gate_up_t = jnp.swapaxes(gate_up, 2, 3)
    body = functools.partial(
        _expert_body, width=width, block_total=block_total, row_count=row_count, tp_count=tp_count
    )
    return pl.pallas_call(
        body,
        grid=(group_total // tile_groups, local_count),
        in_specs=[
            pl.BlockSpec(memory_space=pltpu.SMEM),
            pl.BlockSpec(memory_space=pltpu.SMEM),
            pl.BlockSpec((tile, message_width), lambda i, b: (i, 0)),
            pl.BlockSpec((1, 2, hidden, width), lambda i, b: (b, 0, 0, 0)),
            pl.BlockSpec((1, hidden, width), lambda i, b: (b, 0, 0)),
        ],
        out_specs=pl.BlockSpec((tile_groups * tp_count, row_count, own_width), lambda i, b: (i, 0, 0)),
        out_shape=jax.ShapeDtypeStruct((group_total * tp_count, row_count, own_width), jnp.bfloat16),
        scratch_shapes=[pltpu.VMEM((tile, width), jnp.float32)],
        compiler_params=pltpu.CompilerParams(dimension_semantics=("parallel", "arbitrary")),
    )(offset, dest, rows, gate_up_t, down)


def per_device(
    hidden_in,
    queries,
    fresh_key_value,
    positions,
    lengths,
    cache,
    out_proj,
    norm_gain,
    expert_ids,
    router_weights,
    gate_up,
    down,
):
    tp_count = lax.axis_size("tp")
    req_count = lax.axis_size("req")
    tp_index = lax.axis_index("tp")
    req_index = lax.axis_index("req")
    row_count = hidden_in.shape[0]
    head_size = cache.shape[3]
    kv_count = cache.shape[2]
    own_heads = queries.shape[1] // head_size
    head_count = own_heads * tp_count
    request_group_size = head_count // kv_count
    score_scaling = head_size ** (-0.5)
    model_width = norm_gain.shape[0]
    own_width = hidden_in.shape[1]
    first_head = tp_index * own_heads
    span_rows = cache.shape[0]

    q_local = apply_rotary_heads(
        queries.reshape(row_count, own_heads, head_size).astype(jnp.float32), positions, head_size
    ).astype(jnp.bfloat16)
    packed = jnp.stack([q_local.reshape(row_count, own_width), hidden_in], axis=0)
    gathered = lax.all_gather(packed, "tp", axis=0)
    q_all = jnp.transpose(gathered[:, 0], (1, 0, 2)).reshape(
        row_count, kv_count, request_group_size, head_size
    )
    hidden_full = jnp.transpose(gathered[:, 1], (1, 0, 2)).reshape(row_count, model_width)

    k_new = apply_rotary_heads(
        fresh_key_value[:, 0].reshape(row_count, kv_count, head_size).astype(jnp.float32),
        positions,
        head_size,
    ).astype(jnp.bfloat16)
    value_fresh = fresh_key_value[:, 1].reshape(row_count, kv_count, head_size)
    own_score = (
        jnp.einsum("rcgd,rcd->rcg", q_all, k_new, preferred_element_type=jnp.float32)
        * score_scaling
    )

    segment_ends = jnp.cumsum(lengths[0], dtype=jnp.int32)
    segment_starts = segment_ends - lengths[0]
    cache_spots = tp_index * span_rows + jnp.arange(span_rows, dtype=jnp.int32)
    mask = (cache_spots[None, :] >= segment_starts[:, None]) & (
        cache_spots[None, :] < segment_ends[:, None]
    )
    mask = mask[:, None, None, :]
    keys = cache[:, 0]
    values = cache[:, 1]
    scores = (
        jnp.einsum("rcgd,jcd->rcgj", q_all, keys, preferred_element_type=jnp.float32)
        * score_scaling
    )
    scores = jnp.where(mask, scores, neg_floor)
    highest_local = jnp.max(scores, axis=3)
    weights = jnp.where(mask, jnp.exp(scores - highest_local[..., None]), 0.0)
    totals_local = jnp.sum(weights, axis=3)
    sums_local = jnp.einsum(
        "rcgj,jcd->rcgd",
        weights,
        values.astype(jnp.float32),
        precision=lax.Precision.HIGHEST,
        preferred_element_type=jnp.float32,
    )
    states = jnp.concatenate(
        [highest_local[..., None], totals_local[..., None], sums_local], axis=3
    ).reshape(row_count, tp_count, own_heads, head_size + 2)
    all_states = lax.all_to_all(
        jnp.transpose(states, (1, 0, 2, 3)), "tp", 0, 0, tiled=True
    )
    parts_highest = all_states[..., 0]
    parts_totals = all_states[..., 1]
    parts_sums = all_states[..., 2:]
    own_slice = lax.dynamic_slice_in_dim(own_score.reshape(row_count, head_count), first_head, own_heads, 1)
    top_score = jnp.maximum(jnp.max(parts_highest, axis=0), own_slice)
    factors = jnp.exp(parts_highest - top_score[None])
    own_part = jnp.exp(own_slice - top_score)
    if request_group_size % own_heads == 0:
        own_values = lax.dynamic_slice_in_dim(value_fresh, first_head // request_group_size, 1, 1)
        own_values = own_values.astype(jnp.float32)
    else:
        head_kv = (first_head + jnp.arange(own_heads, dtype=jnp.int32)) // request_group_size
        own_values = jnp.take(value_fresh, head_kv, axis=1).astype(jnp.float32)
    totals = jnp.sum(parts_totals * factors, axis=0) + own_part
    summed = jnp.sum(parts_sums * factors[..., None], axis=0) + own_values * own_part[..., None]
    attention_output = (summed / totals[..., None]).astype(jnp.bfloat16).reshape(
        row_count, own_heads * head_size
    )

    partial_proj = jnp.dot(attention_output, out_proj, preferred_element_type=jnp.float32)
    projected = jnp.sum(lax.all_gather(partial_proj, "tp", axis=0), axis=0)
    residual = hidden_full.astype(jnp.float32) + projected
    mean_square = jnp.mean(residual * residual, axis=1, keepdims=True)
    normed = (residual * lax.rsqrt(mean_square + norm_eps) * norm_gain[None, :]).astype(jnp.bfloat16)
    residual_own = lax.dynamic_slice_in_dim(residual, tp_index * own_width, own_width, 1)

    local_count = gate_up.shape[0]
    block_total = local_count * req_count
    split_count = max(1, block_total // EXPERTS)
    expert_range = jnp.arange(EXPERTS, dtype=jnp.int32)
    member = jnp.any(expert_ids[:, :, None] == expert_range[None, None, :], axis=1)
    member_int = member.astype(jnp.int32)
    slot_of = jnp.cumsum(member_int, axis=0, dtype=jnp.int32) - member_int
    slot_taken = jnp.take_along_axis(slot_of, expert_ids, axis=1)
    block_taken = (slot_taken % split_count) * EXPERTS + expert_ids
    block_range = jnp.arange(block_total, dtype=jnp.int32)
    block_weights = jnp.sum(
        jnp.where(block_taken[:, :, None] == block_range[None, None, :], router_weights[:, :, None], 0.0),
        axis=1,
    )

    def gather_req(value):
        if req_count > 8 or req_count % tp_count != 0:
            gathered = lax.all_gather(value, "req", axis=0, tiled=True)
            return gathered, jnp.arange(req_count, dtype=jnp.int32)
        per_tp = req_count // tp_count
        fetched = []
        for slot in range(per_tp):
            pairs = []
            for group in range(req_count):
                for part in range(tp_count):
                    shift = per_tp * part + slot + 1
                    source = ((group - shift) % req_count) * tp_count + part
                    pairs.append((source, group * tp_count + part))
            fetched.append(lax.ppermute(value, ("req", "tp"), pairs))
        shared = lax.all_gather(jnp.stack(fetched, axis=0), "tp", axis=0)
        shared = shared.reshape((req_count * value.shape[0],) + value.shape[1:])
        groups = (req_index - jnp.arange(req_count, dtype=jnp.int32) - 1) % req_count
        return shared, groups.astype(jnp.int32)

    weight_high = lax.reduce_precision(block_weights, exponent_bits=8, mantissa_bits=7)
    weight_rest = block_weights - weight_high
    weight_mid = lax.reduce_precision(weight_rest, exponent_bits=8, mantissa_bits=7)
    weight_low = weight_rest - weight_mid
    code = jnp.concatenate([weight_high, weight_mid, weight_low], axis=1).astype(jnp.bfloat16)
    code_lanes = -(-code.shape[1] // 128) * 128
    code = jnp.pad(code, ((0, 0), (0, code_lanes - code.shape[1])))
    message = jnp.concatenate([normed, code], axis=1)
    message_all, message_groups = gather_req(message)
    offset = (req_index * local_count).astype(jnp.int32).reshape(1)
    mixed = expert_mix(
        message_all, gate_up, down, offset, message_groups, model_width, block_total, row_count, tp_count
    )
    mixed = lax.all_to_all(mixed, ("req", "tp"), 0, 0, tiled=True)
    mixed = jnp.sum(mixed.astype(jnp.float32), axis=0)
    return (residual_own + mixed).astype(jnp.bfloat16)


def solution(mesh):
    placed = (
        P("req", "tp"),
        P("req", "tp"),
        P("req", None, None),
        P("req"),
        P("req", None),
        P(("req", "tp"), None, None, None),
        P("tp", None),
        P(),
        P("req", None),
        P("req", None),
        P("req", None, None, "tp"),
        P("req", "tp", None),
    )
    return jax.shard_map(
        per_device, mesh=mesh, in_specs=placed, out_specs=P("req", "tp"), check_vma=False
    )
```

```python
import functools
import math

import jax
import jax.numpy as jnp
from jax import lax
from jax.experimental import pallas as pl
from jax.experimental.pallas import tpu as pltpu
from jax.sharding import PartitionSpec as P

EXPERTS = 32


rope_base = 1000000.0
norm_eps = 1e-06
neg_floor = -1e30


def apply_rotary_heads(values, positions, head_size):
    half_size = head_size // 2
    exponents = jnp.arange(half_size, dtype=jnp.float32) * (2.0 / head_size)
    inverse_freq = jnp.power(jnp.float32(rope_base), -exponents)
    angles = positions.astype(jnp.float32)[:, None] * inverse_freq[None, :]
    cosine = jnp.cos(angles)[:, None, :]
    sine = jnp.sin(angles)[:, None, :]
    first_half = values[..., :half_size]
    second_half = values[..., half_size:]
    return jnp.concatenate(
        [first_half * cosine - second_half * sine, second_half * cosine + first_half * sine],
        axis=-1,
    )


def _expert_body(
    offset_ref, dest_ref, x_ref, gu_ref, dn_ref, o_ref, acc_ref, *, width, block_total, row_count, tp_count
):
    block = pl.program_id(1)

    @pl.when(block == 0)
    def _():
        acc_ref[...] = jnp.zeros_like(acc_ref)

    x = x_ref[:, :width]
    contract_rows = (((1,), (1,)), ((), ()))
    gate_part = lax.dot_general(x, gu_ref[0, 0], contract_rows, preferred_element_type=jnp.float32)
    up_part = lax.dot_general(x, gu_ref[0, 1], contract_rows, preferred_element_type=jnp.float32)
    activation = (jnp.maximum(gate_part, 0.0) * up_part).astype(jnp.bfloat16)
    produced = jnp.dot(activation, dn_ref[0], preferred_element_type=jnp.float32)
    produced = produced.astype(jnp.bfloat16).astype(jnp.float32)
    code = x_ref[:, width:].astype(jnp.float32)
    lanes = lax.broadcasted_iota(jnp.int32, code.shape, 1)
    column = offset_ref[0] + block
    chosen = jnp.sum(jnp.where(lanes == column, code, 0.0), axis=1, keepdims=True)
    chosen = chosen + jnp.sum(jnp.where(lanes == column + block_total, code, 0.0), axis=1, keepdims=True)
    chosen = chosen + jnp.sum(jnp.where(lanes == column + 2 * block_total, code, 0.0), axis=1, keepdims=True)
    acc_ref[...] += chosen * produced

    @pl.when(block == pl.num_programs(1) - 1)
    def _():
        own_width = o_ref.shape[2]
        tile_groups = x_ref.shape[0] // row_count
        for group in range(tile_groups):
            dest = dest_ref[pl.program_id(0) * tile_groups + group] - pl.program_id(0) * tile_groups
            for part in range(tp_count):
                o_ref[dest * tp_count + part] = acc_ref[
                    group * row_count : (group + 1) * row_count,
                    part * own_width : (part + 1) * own_width,
                ].astype(o_ref.dtype)


def expert_mix(rows, gate_up, down, offset, dest, width, block_total, row_count, tp_count):
    row_total, message_width = rows.shape
    local_count, _, _, hidden = gate_up.shape
    group_total = row_total // row_count
    tile_groups = math.gcd(group_total, 8)
    tile = tile_groups * row_count
    own_width = width // tp_count
    gate_up_t = jnp.swapaxes(gate_up, 2, 3)
    body = functools.partial(
        _expert_body, width=width, block_total=block_total, row_count=row_count, tp_count=tp_count
    )
    return pl.pallas_call(
        body,
        grid=(group_total // tile_groups, local_count),
        in_specs=[
            pl.BlockSpec(memory_space=pltpu.SMEM),
            pl.BlockSpec(memory_space=pltpu.SMEM),
            pl.BlockSpec((tile, message_width), lambda i, b: (i, 0)),
            pl.BlockSpec((1, 2, hidden, width), lambda i, b: (b, 0, 0, 0)),
            pl.BlockSpec((1, hidden, width), lambda i, b: (b, 0, 0)),
        ],
        out_specs=pl.BlockSpec((tile_groups * tp_count, row_count, own_width), lambda i, b: (i, 0, 0)),
        out_shape=jax.ShapeDtypeStruct((group_total * tp_count, row_count, own_width), jnp.bfloat16),
        scratch_shapes=[pltpu.VMEM((tile, width), jnp.float32)],
        compiler_params=pltpu.CompilerParams(dimension_semantics=("parallel", "arbitrary")),
    )(offset, dest, rows, gate_up_t, down)


def per_device(
    hidden_in,
    queries,
    fresh_key_value,
    positions,
    lengths,
    cache,
    out_proj,
    norm_gain,
    expert_ids,
    router_weights,
    gate_up,
    down,
):
    tp_count = lax.axis_size("tp")
    req_count = lax.axis_size("req")
    tp_index = lax.axis_index("tp")
    req_index = lax.axis_index("req")
    row_count = hidden_in.shape[0]
    head_size = cache.shape[3]
    kv_count = cache.shape[2]
    own_heads = queries.shape[1] // head_size
    head_count = own_heads * tp_count
    request_group_size = head_count // kv_count
    score_scaling = head_size ** (-0.5)
    model_width = norm_gain.shape[0]
    own_width = hidden_in.shape[1]
    first_head = tp_index * own_heads
    span_rows = cache.shape[0]

    q_local = apply_rotary_heads(
        queries.reshape(row_count, own_heads, head_size).astype(jnp.float32), positions, head_size
    ).astype(jnp.bfloat16)
    packed = jnp.stack([q_local.reshape(row_count, own_width), hidden_in], axis=0)
    gathered = lax.all_gather(packed, "tp", axis=0)
    q_all = jnp.transpose(gathered[:, 0], (1, 0, 2)).reshape(
        row_count, kv_count, request_group_size, head_size
    )
    hidden_full = jnp.transpose(gathered[:, 1], (1, 0, 2)).reshape(row_count, model_width)

    k_new = apply_rotary_heads(
        fresh_key_value[:, 0].reshape(row_count, kv_count, head_size).astype(jnp.float32),
        positions,
        head_size,
    ).astype(jnp.bfloat16)
    value_fresh = fresh_key_value[:, 1].reshape(row_count, kv_count, head_size)
    own_score = (
        jnp.einsum("rcgd,rcd->rcg", q_all, k_new, preferred_element_type=jnp.float32)
        * score_scaling
    )

    segment_ends = jnp.cumsum(lengths[0], dtype=jnp.int32)
    segment_starts = segment_ends - lengths[0]
    cache_spots = tp_index * span_rows + jnp.arange(span_rows, dtype=jnp.int32)
    mask = (cache_spots[None, :] >= segment_starts[:, None]) & (
        cache_spots[None, :] < segment_ends[:, None]
    )
    mask = mask[:, None, None, :]
    keys = cache[:, 0]
    values = cache[:, 1]
    scores = (
        jnp.einsum("rcgd,jcd->rcgj", q_all, keys, preferred_element_type=jnp.float32)
        * score_scaling
    )
    scores = jnp.where(mask, scores, neg_floor)
    highest_local = jnp.max(scores, axis=3)
    weights = jnp.where(mask, jnp.exp(scores - highest_local[..., None]), 0.0)
    totals_local = jnp.sum(weights, axis=3)
    sums_local = jnp.einsum(
        "rcgj,jcd->rcgd",
        weights,
        values.astype(jnp.float32),
        precision=lax.Precision.HIGHEST,
        preferred_element_type=jnp.float32,
    )
    states = jnp.concatenate(
        [highest_local[..., None], totals_local[..., None], sums_local], axis=3
    ).reshape(row_count, tp_count, own_heads, head_size + 2)
    states = jnp.transpose(states, (1, 0, 2, 3))
    own_part_states = lax.dynamic_index_in_dim(states, tp_index, 0, keepdims=False)
    all_states = [own_part_states]
    for shift in range(1, tp_count):
        outgoing = lax.dynamic_index_in_dim(states, (tp_index + shift) % tp_count, 0, keepdims=False)
        all_states.append(
            lax.ppermute(outgoing, "tp", [(i, (i + shift) % tp_count) for i in range(tp_count)])
        )
    all_states = jnp.stack(all_states, axis=0)
    parts_highest = all_states[..., 0]
    parts_totals = all_states[..., 1]
    parts_sums = all_states[..., 2:]
    own_slice = lax.dynamic_slice_in_dim(own_score.reshape(row_count, head_count), first_head, own_heads, 1)
    top_score = jnp.maximum(jnp.max(parts_highest, axis=0), own_slice)
    factors = jnp.exp(parts_highest - top_score[None])
    own_part = jnp.exp(own_slice - top_score)
    if request_group_size % own_heads == 0:
        own_values = lax.dynamic_slice_in_dim(value_fresh, first_head // request_group_size, 1, 1)
        own_values = own_values.astype(jnp.float32)
    else:
        head_kv = (first_head + jnp.arange(own_heads, dtype=jnp.int32)) // request_group_size
        own_values = jnp.take(value_fresh, head_kv, axis=1).astype(jnp.float32)
    totals = jnp.sum(parts_totals * factors, axis=0) + own_part
    summed = jnp.sum(parts_sums * factors[..., None], axis=0) + own_values * own_part[..., None]
    attention_output = (summed / totals[..., None]).astype(jnp.bfloat16).reshape(
        row_count, own_heads * head_size
    )

    partial_proj = jnp.dot(attention_output, out_proj, preferred_element_type=jnp.float32)
    projected = jnp.sum(lax.all_gather(partial_proj, "tp", axis=0), axis=0)
    residual = hidden_full.astype(jnp.float32) + projected
    mean_square = jnp.mean(residual * residual, axis=1, keepdims=True)
    normed = (residual * lax.rsqrt(mean_square + norm_eps) * norm_gain[None, :]).astype(jnp.bfloat16)
    residual_own = lax.dynamic_slice_in_dim(residual, tp_index * own_width, own_width, 1)

    local_count = gate_up.shape[0]
    block_total = local_count * req_count
    split_count = max(1, block_total // EXPERTS)
    expert_range = jnp.arange(EXPERTS, dtype=jnp.int32)
    member = jnp.any(expert_ids[:, :, None] == expert_range[None, None, :], axis=1)
    member_int = member.astype(jnp.int32)
    slot_of = jnp.cumsum(member_int, axis=0, dtype=jnp.int32) - member_int
    slot_taken = jnp.take_along_axis(slot_of, expert_ids, axis=1)
    block_taken = (slot_taken % split_count) * EXPERTS + expert_ids
    block_range = jnp.arange(block_total, dtype=jnp.int32)
    block_weights = jnp.sum(
        jnp.where(block_taken[:, :, None] == block_range[None, None, :], router_weights[:, :, None], 0.0),
        axis=1,
    )

    def gather_req(value):
        if req_count > 8 or req_count % tp_count != 0:
            gathered = lax.all_gather(value, "req", axis=0, tiled=True)
            return gathered, jnp.arange(req_count, dtype=jnp.int32)
        per_tp = req_count // tp_count
        fetched = []
        for slot in range(per_tp):
            pairs = []
            for group in range(req_count):
                for part in range(tp_count):
                    shift = per_tp * part + slot + 1
                    source = ((group - shift) % req_count) * tp_count + part
                    pairs.append((source, group * tp_count + part))
            fetched.append(lax.ppermute(value, ("req", "tp"), pairs))
        shared = lax.all_gather(jnp.stack(fetched, axis=0), "tp", axis=0)
        shared = shared.reshape((req_count * value.shape[0],) + value.shape[1:])
        groups = (req_index - jnp.arange(req_count, dtype=jnp.int32) - 1) % req_count
        return shared, groups.astype(jnp.int32)

    weight_high = lax.reduce_precision(block_weights, exponent_bits=8, mantissa_bits=7)
    weight_rest = block_weights - weight_high
    weight_mid = lax.reduce_precision(weight_rest, exponent_bits=8, mantissa_bits=7)
    weight_low = weight_rest - weight_mid
    code = jnp.concatenate([weight_high, weight_mid, weight_low], axis=1).astype(jnp.bfloat16)
    code_lanes = -(-code.shape[1] // 128) * 128
    code = jnp.pad(code, ((0, 0), (0, code_lanes - code.shape[1])))
    message = jnp.concatenate([normed, code], axis=1)
    message_all, message_groups = gather_req(message)
    offset = (req_index * local_count).astype(jnp.int32).reshape(1)
    mixed = expert_mix(
        message_all, gate_up, down, offset, message_groups, model_width, block_total, row_count, tp_count
    )
    mixed = lax.all_to_all(mixed, ("req", "tp"), 0, 0, tiled=True)
    mixed = jnp.sum(mixed.astype(jnp.float32), axis=0)
    return (residual_own + mixed).astype(jnp.bfloat16)


def solution(mesh):
    placed = (
        P("req", "tp"),
        P("req", "tp"),
        P("req", None, None),
        P("req"),
        P("req", None),
        P(("req", "tp"), None, None, None),
        P("tp", None),
        P(),
        P("req", None),
        P("req", None),
        P("req", None, None, "tp"),
        P("req", "tp", None),
    )
    return jax.shard_map(
        per_device, mesh=mesh, in_specs=placed, out_specs=P("req", "tp"), check_vma=False
    )
```

```python
import functools
import math

import jax
import jax.numpy as jnp
from jax import lax
from jax.experimental import pallas as pl
from jax.experimental.pallas import tpu as pltpu
from jax.sharding import PartitionSpec as P

EXPERTS = 32


rope_base = 1000000.0
norm_eps = 1e-06
neg_floor = -1e30


def apply_rotary_heads(values, positions, head_size):
    half_size = head_size // 2
    exponents = jnp.arange(half_size, dtype=jnp.float32) * (2.0 / head_size)
    inverse_freq = jnp.power(jnp.float32(rope_base), -exponents)
    angles = positions.astype(jnp.float32)[:, None] * inverse_freq[None, :]
    cosine = jnp.cos(angles)[:, None, :]
    sine = jnp.sin(angles)[:, None, :]
    first_half = values[..., :half_size]
    second_half = values[..., half_size:]
    return jnp.concatenate(
        [first_half * cosine - second_half * sine, second_half * cosine + first_half * sine],
        axis=-1,
    )


def _expert_body(
    offset_ref, dest_ref, x_ref, gu_ref, dn_ref, o_ref, acc_ref, *, width, block_total, row_count, tp_count
):
    block = pl.program_id(1)

    @pl.when(block == 0)
    def _():
        acc_ref[...] = jnp.zeros_like(acc_ref)

    x = x_ref[:, :width]
    contract_rows = (((1,), (1,)), ((), ()))
    gate_part = lax.dot_general(x, gu_ref[0, 0], contract_rows, preferred_element_type=jnp.float32)
    up_part = lax.dot_general(x, gu_ref[0, 1], contract_rows, preferred_element_type=jnp.float32)
    activation = (jnp.maximum(gate_part, 0.0) * up_part).astype(jnp.bfloat16)
    produced = jnp.dot(activation, dn_ref[0], preferred_element_type=jnp.float32)
    produced = produced.astype(jnp.bfloat16).astype(jnp.float32)
    code = x_ref[:, width:].astype(jnp.float32)
    lanes = lax.broadcasted_iota(jnp.int32, code.shape, 1)
    column = offset_ref[0] + block
    chosen = jnp.sum(jnp.where(lanes == column, code, 0.0), axis=1, keepdims=True)
    chosen = chosen + jnp.sum(jnp.where(lanes == column + block_total, code, 0.0), axis=1, keepdims=True)
    chosen = chosen + jnp.sum(jnp.where(lanes == column + 2 * block_total, code, 0.0), axis=1, keepdims=True)
    acc_ref[...] += chosen * produced

    @pl.when(block == pl.num_programs(1) - 1)
    def _():
        own_width = o_ref.shape[2]
        tile_groups = x_ref.shape[0] // row_count
        for group in range(tile_groups):
            dest = dest_ref[pl.program_id(0) * tile_groups + group] - pl.program_id(0) * tile_groups
            for part in range(tp_count):
                o_ref[dest * tp_count + part] = acc_ref[
                    group * row_count : (group + 1) * row_count,
                    part * own_width : (part + 1) * own_width,
                ].astype(o_ref.dtype)


def expert_mix(rows, gate_up, down, offset, dest, width, block_total, row_count, tp_count):
    row_total, message_width = rows.shape
    local_count, _, _, hidden = gate_up.shape
    group_total = row_total // row_count
    tile_groups = math.gcd(group_total, 8)
    tile = tile_groups * row_count
    own_width = width // tp_count
    gate_up_t = jnp.swapaxes(gate_up, 2, 3)
    body = functools.partial(
        _expert_body, width=width, block_total=block_total, row_count=row_count, tp_count=tp_count
    )
    return pl.pallas_call(
        body,
        grid=(group_total // tile_groups, local_count),
        in_specs=[
            pl.BlockSpec(memory_space=pltpu.SMEM),
            pl.BlockSpec(memory_space=pltpu.SMEM),
            pl.BlockSpec((tile, message_width), lambda i, b: (i, 0)),
            pl.BlockSpec((1, 2, hidden, width), lambda i, b: (b, 0, 0, 0)),
            pl.BlockSpec((1, hidden, width), lambda i, b: (b, 0, 0)),
        ],
        out_specs=pl.BlockSpec((tile_groups * tp_count, row_count, own_width), lambda i, b: (i, 0, 0)),
        out_shape=jax.ShapeDtypeStruct((group_total * tp_count, row_count, own_width), jnp.bfloat16),
        scratch_shapes=[pltpu.VMEM((tile, width), jnp.float32)],
        compiler_params=pltpu.CompilerParams(dimension_semantics=("parallel", "arbitrary")),
    )(offset, dest, rows, gate_up_t, down)


def per_device(
    hidden_in,
    queries,
    fresh_key_value,
    positions,
    lengths,
    cache,
    out_proj,
    norm_gain,
    expert_ids,
    router_weights,
    gate_up,
    down,
):
    tp_count = lax.axis_size("tp")
    req_count = lax.axis_size("req")
    tp_index = lax.axis_index("tp")
    req_index = lax.axis_index("req")
    row_count = hidden_in.shape[0]
    head_size = cache.shape[3]
    kv_count = cache.shape[2]
    own_heads = queries.shape[1] // head_size
    head_count = own_heads * tp_count
    request_group_size = head_count // kv_count
    score_scaling = head_size ** (-0.5)
    model_width = norm_gain.shape[0]
    own_width = hidden_in.shape[1]
    first_head = tp_index * own_heads
    span_rows = cache.shape[0]

    q_local = apply_rotary_heads(
        queries.reshape(row_count, own_heads, head_size).astype(jnp.float32), positions, head_size
    ).astype(jnp.bfloat16)
    packed = jnp.stack([q_local.reshape(row_count, own_width), hidden_in], axis=0)
    arrivals = [packed] + [
        lax.ppermute(packed, "tp", [(i, (i + shift) % tp_count) for i in range(tp_count)])
        for shift in range(1, tp_count)
    ]
    arrivals = jnp.stack(arrivals, axis=0)
    order = (tp_index - jnp.arange(tp_count, dtype=jnp.int32)) % tp_count
    gathered = jnp.take(arrivals, order, axis=0, mode="clip")
    q_all = jnp.transpose(gathered[:, 0], (1, 0, 2)).reshape(
        row_count, kv_count, request_group_size, head_size
    )
    hidden_full = jnp.transpose(gathered[:, 1], (1, 0, 2)).reshape(row_count, model_width)

    k_new = apply_rotary_heads(
        fresh_key_value[:, 0].reshape(row_count, kv_count, head_size).astype(jnp.float32),
        positions,
        head_size,
    ).astype(jnp.bfloat16)
    value_fresh = fresh_key_value[:, 1].reshape(row_count, kv_count, head_size)
    own_score = (
        jnp.einsum("rcgd,rcd->rcg", q_all, k_new, preferred_element_type=jnp.float32)
        * score_scaling
    )

    segment_ends = jnp.cumsum(lengths[0], dtype=jnp.int32)
    segment_starts = segment_ends - lengths[0]
    cache_spots = tp_index * span_rows + jnp.arange(span_rows, dtype=jnp.int32)
    mask = (cache_spots[None, :] >= segment_starts[:, None]) & (
        cache_spots[None, :] < segment_ends[:, None]
    )
    mask = mask[:, None, None, :]
    keys = cache[:, 0]
    values = cache[:, 1]
    scores = (
        jnp.einsum("rcgd,jcd->rcgj", q_all, keys, preferred_element_type=jnp.float32)
        * score_scaling
    )
    scores = jnp.where(mask, scores, neg_floor)
    highest_local = jnp.max(scores, axis=3)
    weights = jnp.where(mask, jnp.exp(scores - highest_local[..., None]), 0.0)
    totals_local = jnp.sum(weights, axis=3)
    sums_local = jnp.einsum(
        "rcgj,jcd->rcgd",
        weights,
        values.astype(jnp.float32),
        precision=lax.Precision.HIGHEST,
        preferred_element_type=jnp.float32,
    )
    states = jnp.concatenate(
        [highest_local[..., None], totals_local[..., None], sums_local], axis=3
    ).reshape(row_count, tp_count, own_heads, head_size + 2)
    states = jnp.transpose(states, (1, 0, 2, 3))
    own_part_states = lax.dynamic_index_in_dim(states, tp_index, 0, keepdims=False)
    all_states = [own_part_states]
    for shift in range(1, tp_count):
        outgoing = lax.dynamic_index_in_dim(states, (tp_index + shift) % tp_count, 0, keepdims=False)
        all_states.append(
            lax.ppermute(outgoing, "tp", [(i, (i + shift) % tp_count) for i in range(tp_count)])
        )
    all_states = jnp.stack(all_states, axis=0)
    parts_highest = all_states[..., 0]
    parts_totals = all_states[..., 1]
    parts_sums = all_states[..., 2:]
    own_slice = lax.dynamic_slice_in_dim(own_score.reshape(row_count, head_count), first_head, own_heads, 1)
    top_score = jnp.maximum(jnp.max(parts_highest, axis=0), own_slice)
    factors = jnp.exp(parts_highest - top_score[None])
    own_part = jnp.exp(own_slice - top_score)
    if request_group_size % own_heads == 0:
        own_values = lax.dynamic_slice_in_dim(value_fresh, first_head // request_group_size, 1, 1)
        own_values = own_values.astype(jnp.float32)
    else:
        head_kv = (first_head + jnp.arange(own_heads, dtype=jnp.int32)) // request_group_size
        own_values = jnp.take(value_fresh, head_kv, axis=1).astype(jnp.float32)
    totals = jnp.sum(parts_totals * factors, axis=0) + own_part
    summed = jnp.sum(parts_sums * factors[..., None], axis=0) + own_values * own_part[..., None]
    attention_output = (summed / totals[..., None]).astype(jnp.bfloat16).reshape(
        row_count, own_heads * head_size
    )

    partial_proj = jnp.dot(attention_output, out_proj, preferred_element_type=jnp.float32)
    projected = jnp.sum(lax.all_gather(partial_proj, "tp", axis=0), axis=0)
    residual = hidden_full.astype(jnp.float32) + projected
    mean_square = jnp.mean(residual * residual, axis=1, keepdims=True)
    normed = (residual * lax.rsqrt(mean_square + norm_eps) * norm_gain[None, :]).astype(jnp.bfloat16)
    residual_own = lax.dynamic_slice_in_dim(residual, tp_index * own_width, own_width, 1)

    local_count = gate_up.shape[0]
    block_total = local_count * req_count
    split_count = max(1, block_total // EXPERTS)
    expert_range = jnp.arange(EXPERTS, dtype=jnp.int32)
    member = jnp.any(expert_ids[:, :, None] == expert_range[None, None, :], axis=1)
    member_int = member.astype(jnp.int32)
    slot_of = jnp.cumsum(member_int, axis=0, dtype=jnp.int32) - member_int
    slot_taken = jnp.take_along_axis(slot_of, expert_ids, axis=1)
    block_taken = (slot_taken % split_count) * EXPERTS + expert_ids
    block_range = jnp.arange(block_total, dtype=jnp.int32)
    block_weights = jnp.sum(
        jnp.where(block_taken[:, :, None] == block_range[None, None, :], router_weights[:, :, None], 0.0),
        axis=1,
    )

    def gather_req(value):
        if req_count > 8 or req_count % tp_count != 0:
            gathered = lax.all_gather(value, "req", axis=0, tiled=True)
            return gathered, jnp.arange(req_count, dtype=jnp.int32)
        per_tp = req_count // tp_count
        fetched = []
        for slot in range(per_tp):
            pairs = []
            for group in range(req_count):
                for part in range(tp_count):
                    shift = per_tp * part + slot + 1
                    source = ((group - shift) % req_count) * tp_count + part
                    pairs.append((source, group * tp_count + part))
            fetched.append(lax.ppermute(value, ("req", "tp"), pairs))
        shared = lax.all_gather(jnp.stack(fetched, axis=0), "tp", axis=0)
        shared = shared.reshape((req_count * value.shape[0],) + value.shape[1:])
        groups = (req_index - jnp.arange(req_count, dtype=jnp.int32) - 1) % req_count
        return shared, groups.astype(jnp.int32)

    weight_high = lax.reduce_precision(block_weights, exponent_bits=8, mantissa_bits=7)
    weight_rest = block_weights - weight_high
    weight_mid = lax.reduce_precision(weight_rest, exponent_bits=8, mantissa_bits=7)
    weight_low = weight_rest - weight_mid
    code = jnp.concatenate([weight_high, weight_mid, weight_low], axis=1).astype(jnp.bfloat16)
    code_lanes = -(-code.shape[1] // 128) * 128
    code = jnp.pad(code, ((0, 0), (0, code_lanes - code.shape[1])))
    message = jnp.concatenate([normed, code], axis=1)
    message_all, message_groups = gather_req(message)
    offset = (req_index * local_count).astype(jnp.int32).reshape(1)
    mixed = expert_mix(
        message_all, gate_up, down, offset, message_groups, model_width, block_total, row_count, tp_count
    )
    mixed = lax.all_to_all(mixed, ("req", "tp"), 0, 0, tiled=True)
    mixed = jnp.sum(mixed.astype(jnp.float32), axis=0)
    return (residual_own + mixed).astype(jnp.bfloat16)


def solution(mesh):
    placed = (
        P("req", "tp"),
        P("req", "tp"),
        P("req", None, None),
        P("req"),
        P("req", None),
        P(("req", "tp"), None, None, None),
        P("tp", None),
        P(),
        P("req", None),
        P("req", None),
        P("req", None, None, "tp"),
        P("req", "tp", None),
    )
    return jax.shard_map(
        per_device, mesh=mesh, in_specs=placed, out_specs=P("req", "tp"), check_vma=False
    )
```

```python
import functools
import math

import jax
import jax.numpy as jnp
from jax import lax
from jax.experimental import pallas as pl
from jax.experimental.pallas import tpu as pltpu
from jax.sharding import PartitionSpec as P

EXPERTS = 32


rope_base = 1000000.0
norm_eps = 1e-06
neg_floor = -1e30


def apply_rotary_heads(values, positions, head_size):
    half_size = head_size // 2
    exponents = jnp.arange(half_size, dtype=jnp.float32) * (2.0 / head_size)
    inverse_freq = jnp.power(jnp.float32(rope_base), -exponents)
    angles = positions.astype(jnp.float32)[:, None] * inverse_freq[None, :]
    cosine = jnp.cos(angles)[:, None, :]
    sine = jnp.sin(angles)[:, None, :]
    first_half = values[..., :half_size]
    second_half = values[..., half_size:]
    return jnp.concatenate(
        [first_half * cosine - second_half * sine, second_half * cosine + first_half * sine],
        axis=-1,
    )


def _expert_body(
    offset_ref, dest_ref, x_ref, gu_ref, dn_ref, o_ref, acc_ref, *, width, block_total, row_count, tp_count
):
    block = pl.program_id(1)

    @pl.when(block == 0)
    def _():
        acc_ref[...] = jnp.zeros_like(acc_ref)

    x = x_ref[:, :width]
    contract_rows = (((1,), (1,)), ((), ()))
    gate_part = lax.dot_general(x, gu_ref[0, 0], contract_rows, preferred_element_type=jnp.float32)
    up_part = lax.dot_general(x, gu_ref[0, 1], contract_rows, preferred_element_type=jnp.float32)
    activation = (jnp.maximum(gate_part, 0.0) * up_part).astype(jnp.bfloat16)
    produced = jnp.dot(activation, dn_ref[0], preferred_element_type=jnp.float32)
    produced = produced.astype(jnp.bfloat16).astype(jnp.float32)
    code = x_ref[:, width:].astype(jnp.float32)
    lanes = lax.broadcasted_iota(jnp.int32, code.shape, 1)
    column = offset_ref[0] + block
    chosen = jnp.sum(jnp.where(lanes == column, code, 0.0), axis=1, keepdims=True)
    chosen = chosen + jnp.sum(jnp.where(lanes == column + block_total, code, 0.0), axis=1, keepdims=True)
    chosen = chosen + jnp.sum(jnp.where(lanes == column + 2 * block_total, code, 0.0), axis=1, keepdims=True)
    acc_ref[...] += chosen * produced

    @pl.when(block == pl.num_programs(1) - 1)
    def _():
        own_width = o_ref.shape[2]
        tile_groups = x_ref.shape[0] // row_count
        for group in range(tile_groups):
            dest = dest_ref[pl.program_id(0) * tile_groups + group] - pl.program_id(0) * tile_groups
            for part in range(tp_count):
                o_ref[dest * tp_count + part] = acc_ref[
                    group * row_count : (group + 1) * row_count,
                    part * own_width : (part + 1) * own_width,
                ].astype(o_ref.dtype)


def expert_mix(rows, gate_up, down, offset, dest, width, block_total, row_count, tp_count):
    row_total, message_width = rows.shape
    local_count, _, _, hidden = gate_up.shape
    group_total = row_total // row_count
    tile_groups = math.gcd(group_total, 8)
    tile = tile_groups * row_count
    own_width = width // tp_count
    gate_up_t = jnp.swapaxes(gate_up, 2, 3)
    body = functools.partial(
        _expert_body, width=width, block_total=block_total, row_count=row_count, tp_count=tp_count
    )
    return pl.pallas_call(
        body,
        grid=(group_total // tile_groups, local_count),
        in_specs=[
            pl.BlockSpec(memory_space=pltpu.SMEM),
            pl.BlockSpec(memory_space=pltpu.SMEM),
            pl.BlockSpec((tile, message_width), lambda i, b: (i, 0)),
            pl.BlockSpec((1, 2, hidden, width), lambda i, b: (b, 0, 0, 0)),
            pl.BlockSpec((1, hidden, width), lambda i, b: (b, 0, 0)),
        ],
        out_specs=pl.BlockSpec((tile_groups * tp_count, row_count, own_width), lambda i, b: (i, 0, 0)),
        out_shape=jax.ShapeDtypeStruct((group_total * tp_count, row_count, own_width), jnp.bfloat16),
        scratch_shapes=[pltpu.VMEM((tile, width), jnp.float32)],
        compiler_params=pltpu.CompilerParams(dimension_semantics=("parallel", "arbitrary")),
    )(offset, dest, rows, gate_up_t, down)


def per_device(
    hidden_in,
    queries,
    fresh_key_value,
    positions,
    lengths,
    cache,
    out_proj,
    norm_gain,
    expert_ids,
    router_weights,
    gate_up,
    down,
):
    tp_count = lax.axis_size("tp")
    req_count = lax.axis_size("req")
    tp_index = lax.axis_index("tp")
    req_index = lax.axis_index("req")
    row_count = hidden_in.shape[0]
    head_size = cache.shape[3]
    kv_count = cache.shape[2]
    own_heads = queries.shape[1] // head_size
    head_count = own_heads * tp_count
    request_group_size = head_count // kv_count
    score_scaling = head_size ** (-0.5)
    model_width = norm_gain.shape[0]
    own_width = hidden_in.shape[1]
    first_head = tp_index * own_heads
    span_rows = cache.shape[0]

    q_local = apply_rotary_heads(
        queries.reshape(row_count, own_heads, head_size).astype(jnp.float32), positions, head_size
    ).astype(jnp.bfloat16)
    packed = jnp.stack([q_local.reshape(row_count, own_width), hidden_in], axis=0)
    gathered = lax.all_gather(packed, "tp", axis=0)
    q_all = jnp.transpose(gathered[:, 0], (1, 0, 2)).reshape(
        row_count, kv_count, request_group_size, head_size
    )
    hidden_full = jnp.transpose(gathered[:, 1], (1, 0, 2)).reshape(row_count, model_width)

    k_new = apply_rotary_heads(
        fresh_key_value[:, 0].reshape(row_count, kv_count, head_size).astype(jnp.float32),
        positions,
        head_size,
    ).astype(jnp.bfloat16)
    value_fresh = fresh_key_value[:, 1].reshape(row_count, kv_count, head_size)
    own_score = (
        jnp.einsum("rcgd,rcd->rcg", q_all, k_new, preferred_element_type=jnp.float32)
        * score_scaling
    )

    segment_ends = jnp.cumsum(lengths[0], dtype=jnp.int32)
    segment_starts = segment_ends - lengths[0]
    cache_spots = tp_index * span_rows + jnp.arange(span_rows, dtype=jnp.int32)
    mask = (cache_spots[None, :] >= segment_starts[:, None]) & (
        cache_spots[None, :] < segment_ends[:, None]
    )
    mask = mask[:, None, None, :]
    keys = cache[:, 0]
    values = cache[:, 1]
    scores = (
        jnp.einsum("rcgd,jcd->rcgj", q_all, keys, preferred_element_type=jnp.float32)
        * score_scaling
    )
    scores = jnp.where(mask, scores, neg_floor)
    highest_local = jnp.max(scores, axis=3)
    weights = jnp.where(mask, jnp.exp(scores - highest_local[..., None]), 0.0)
    totals_local = jnp.sum(weights, axis=3)
    sums_local = jnp.einsum(
        "rcgj,jcd->rcgd",
        weights,
        values.astype(jnp.float32),
        precision=lax.Precision.HIGHEST,
        preferred_element_type=jnp.float32,
    )
    states = jnp.concatenate(
        [highest_local[..., None], totals_local[..., None], sums_local], axis=3
    ).reshape(row_count, tp_count, own_heads, head_size + 2)
    states = jnp.transpose(states, (1, 0, 2, 3))
    own_part_states = lax.dynamic_index_in_dim(states, tp_index, 0, keepdims=False)
    all_states = [own_part_states]
    for shift in range(1, tp_count):
        outgoing = lax.dynamic_index_in_dim(states, (tp_index + shift) % tp_count, 0, keepdims=False)
        all_states.append(
            lax.ppermute(outgoing, "tp", [(i, (i + shift) % tp_count) for i in range(tp_count)])
        )
    all_states = jnp.stack(all_states, axis=0)
    parts_highest = all_states[..., 0]
    parts_totals = all_states[..., 1]
    parts_sums = all_states[..., 2:]
    own_slice = lax.dynamic_slice_in_dim(own_score.reshape(row_count, head_count), first_head, own_heads, 1)
    top_score = jnp.maximum(jnp.max(parts_highest, axis=0), own_slice)
    factors = jnp.exp(parts_highest - top_score[None])
    own_part = jnp.exp(own_slice - top_score)
    if request_group_size % own_heads == 0:
        own_values = lax.dynamic_slice_in_dim(value_fresh, first_head // request_group_size, 1, 1)
        own_values = own_values.astype(jnp.float32)
    else:
        head_kv = (first_head + jnp.arange(own_heads, dtype=jnp.int32)) // request_group_size
        own_values = jnp.take(value_fresh, head_kv, axis=1).astype(jnp.float32)
    totals = jnp.sum(parts_totals * factors, axis=0) + own_part
    summed = jnp.sum(parts_sums * factors[..., None], axis=0) + own_values * own_part[..., None]
    attention_output = (summed / totals[..., None]).astype(jnp.bfloat16).reshape(
        row_count, own_heads * head_size
    )

    partial_proj = jnp.dot(attention_output, out_proj, preferred_element_type=jnp.float32)
    projected = jnp.sum(
        lax.all_gather(partial_proj.astype(jnp.bfloat16), "tp", axis=0).astype(jnp.float32), axis=0
    )
    residual = hidden_full.astype(jnp.float32) + projected
    mean_square = jnp.mean(residual * residual, axis=1, keepdims=True)
    normed = (residual * lax.rsqrt(mean_square + norm_eps) * norm_gain[None, :]).astype(jnp.bfloat16)
    residual_own = lax.dynamic_slice_in_dim(residual, tp_index * own_width, own_width, 1)

    local_count = gate_up.shape[0]
    block_total = local_count * req_count
    split_count = max(1, block_total // EXPERTS)
    expert_range = jnp.arange(EXPERTS, dtype=jnp.int32)
    member = jnp.any(expert_ids[:, :, None] == expert_range[None, None, :], axis=1)
    member_int = member.astype(jnp.int32)
    slot_of = jnp.cumsum(member_int, axis=0, dtype=jnp.int32) - member_int
    slot_taken = jnp.take_along_axis(slot_of, expert_ids, axis=1)
    block_taken = (slot_taken % split_count) * EXPERTS + expert_ids
    block_range = jnp.arange(block_total, dtype=jnp.int32)
    block_weights = jnp.sum(
        jnp.where(block_taken[:, :, None] == block_range[None, None, :], router_weights[:, :, None], 0.0),
        axis=1,
    )

    def gather_req(value):
        if req_count > 8 or req_count % tp_count != 0:
            gathered = lax.all_gather(value, "req", axis=0, tiled=True)
            return gathered, jnp.arange(req_count, dtype=jnp.int32)
        per_tp = req_count // tp_count
        fetched = []
        for slot in range(per_tp):
            pairs = []
            for group in range(req_count):
                for part in range(tp_count):
                    shift = per_tp * part + slot + 1
                    source = ((group - shift) % req_count) * tp_count + part
                    pairs.append((source, group * tp_count + part))
            fetched.append(lax.ppermute(value, ("req", "tp"), pairs))
        shared = lax.all_gather(jnp.stack(fetched, axis=0), "tp", axis=0)
        shared = shared.reshape((req_count * value.shape[0],) + value.shape[1:])
        groups = (req_index - jnp.arange(req_count, dtype=jnp.int32) - 1) % req_count
        return shared, groups.astype(jnp.int32)

    weight_high = lax.reduce_precision(block_weights, exponent_bits=8, mantissa_bits=7)
    weight_rest = block_weights - weight_high
    weight_mid = lax.reduce_precision(weight_rest, exponent_bits=8, mantissa_bits=7)
    weight_low = weight_rest - weight_mid
    code = jnp.concatenate([weight_high, weight_mid, weight_low], axis=1).astype(jnp.bfloat16)
    code_lanes = -(-code.shape[1] // 128) * 128
    code = jnp.pad(code, ((0, 0), (0, code_lanes - code.shape[1])))
    message = jnp.concatenate([normed, code], axis=1)
    message_all, message_groups = gather_req(message)
    offset = (req_index * local_count).astype(jnp.int32).reshape(1)
    mixed = expert_mix(
        message_all, gate_up, down, offset, message_groups, model_width, block_total, row_count, tp_count
    )
    mixed = lax.all_to_all(mixed, ("req", "tp"), 0, 0, tiled=True)
    mixed = jnp.sum(mixed.astype(jnp.float32), axis=0)
    return (residual_own + mixed).astype(jnp.bfloat16)


def solution(mesh):
    placed = (
        P("req", "tp"),
        P("req", "tp"),
        P("req", None, None),
        P("req"),
        P("req", None),
        P(("req", "tp"), None, None, None),
        P("tp", None),
        P(),
        P("req", None),
        P("req", None),
        P("req", None, None, "tp"),
        P("req", "tp", None),
    )
    return jax.shard_map(
        per_device, mesh=mesh, in_specs=placed, out_specs=P("req", "tp"), check_vma=False
    )
```

```python
import functools
import math

import jax
import jax.numpy as jnp
from jax import lax
from jax.experimental import pallas as pl
from jax.experimental.pallas import tpu as pltpu
from jax.sharding import PartitionSpec as P

EXPERTS = 32


rope_base = 1000000.0
norm_eps = 1e-06
neg_floor = -1e30


def apply_rotary_heads(values, positions, head_size):
    half_size = head_size // 2
    exponents = jnp.arange(half_size, dtype=jnp.float32) * (2.0 / head_size)
    inverse_freq = jnp.power(jnp.float32(rope_base), -exponents)
    angles = positions.astype(jnp.float32)[:, None] * inverse_freq[None, :]
    cosine = jnp.cos(angles)[:, None, :]
    sine = jnp.sin(angles)[:, None, :]
    first_half = values[..., :half_size]
    second_half = values[..., half_size:]
    return jnp.concatenate(
        [first_half * cosine - second_half * sine, second_half * cosine + first_half * sine],
        axis=-1,
    )


def _expert_body(
    offset_ref, dest_ref, x_ref, gu_ref, dn_ref, o_ref, acc_ref, *, width, block_total, row_count, tp_count
):
    block = pl.program_id(1)

    @pl.when(block == 0)
    def _():
        acc_ref[...] = jnp.zeros_like(acc_ref)

    x = x_ref[:, :width]
    contract_rows = (((1,), (1,)), ((), ()))
    hidden = gu_ref.shape[2]
    both = gu_ref[0].reshape(2 * hidden, gu_ref.shape[3])
    both_part = lax.dot_general(x, both, contract_rows, preferred_element_type=jnp.float32)
    gate_part = both_part[:, :hidden]
    up_part = both_part[:, hidden:]
    activation = (jnp.maximum(gate_part, 0.0) * up_part).astype(jnp.bfloat16)
    produced = jnp.dot(activation, dn_ref[0], preferred_element_type=jnp.float32)
    produced = produced.astype(jnp.bfloat16).astype(jnp.float32)
    code = x_ref[:, width:].astype(jnp.float32)
    lanes = lax.broadcasted_iota(jnp.int32, code.shape, 1)
    column = offset_ref[0] + block
    chosen = jnp.sum(jnp.where(lanes == column, code, 0.0), axis=1, keepdims=True)
    chosen = chosen + jnp.sum(jnp.where(lanes == column + block_total, code, 0.0), axis=1, keepdims=True)
    chosen = chosen + jnp.sum(jnp.where(lanes == column + 2 * block_total, code, 0.0), axis=1, keepdims=True)
    acc_ref[...] += chosen * produced

    @pl.when(block == pl.num_programs(1) - 1)
    def _():
        own_width = o_ref.shape[2]
        tile_groups = x_ref.shape[0] // row_count
        for group in range(tile_groups):
            dest = dest_ref[pl.program_id(0) * tile_groups + group] - pl.program_id(0) * tile_groups
            for part in range(tp_count):
                o_ref[dest * tp_count + part] = acc_ref[
                    group * row_count : (group + 1) * row_count,
                    part * own_width : (part + 1) * own_width,
                ].astype(o_ref.dtype)


def expert_mix(rows, gate_up, down, offset, dest, width, block_total, row_count, tp_count):
    row_total, message_width = rows.shape
    local_count, _, _, hidden = gate_up.shape
    group_total = row_total // row_count
    tile_groups = math.gcd(group_total, 8)
    tile = tile_groups * row_count
    own_width = width // tp_count
    gate_up_t = jnp.swapaxes(gate_up, 2, 3)
    body = functools.partial(
        _expert_body, width=width, block_total=block_total, row_count=row_count, tp_count=tp_count
    )
    return pl.pallas_call(
        body,
        grid=(group_total // tile_groups, local_count),
        in_specs=[
            pl.BlockSpec(memory_space=pltpu.SMEM),
            pl.BlockSpec(memory_space=pltpu.SMEM),
            pl.BlockSpec((tile, message_width), lambda i, b: (i, 0)),
            pl.BlockSpec((1, 2, hidden, width), lambda i, b: (b, 0, 0, 0)),
            pl.BlockSpec((1, hidden, width), lambda i, b: (b, 0, 0)),
        ],
        out_specs=pl.BlockSpec((tile_groups * tp_count, row_count, own_width), lambda i, b: (i, 0, 0)),
        out_shape=jax.ShapeDtypeStruct((group_total * tp_count, row_count, own_width), jnp.bfloat16),
        scratch_shapes=[pltpu.VMEM((tile, width), jnp.float32)],
        compiler_params=pltpu.CompilerParams(dimension_semantics=("parallel", "arbitrary")),
    )(offset, dest, rows, gate_up_t, down)


def per_device(
    hidden_in,
    queries,
    fresh_key_value,
    positions,
    lengths,
    cache,
    out_proj,
    norm_gain,
    expert_ids,
    router_weights,
    gate_up,
    down,
):
    tp_count = lax.axis_size("tp")
    req_count = lax.axis_size("req")
    tp_index = lax.axis_index("tp")
    req_index = lax.axis_index("req")
    row_count = hidden_in.shape[0]
    head_size = cache.shape[3]
    kv_count = cache.shape[2]
    own_heads = queries.shape[1] // head_size
    head_count = own_heads * tp_count
    request_group_size = head_count // kv_count
    score_scaling = head_size ** (-0.5)
    model_width = norm_gain.shape[0]
    own_width = hidden_in.shape[1]
    first_head = tp_index * own_heads
    span_rows = cache.shape[0]

    q_local = apply_rotary_heads(
        queries.reshape(row_count, own_heads, head_size).astype(jnp.float32), positions, head_size
    ).astype(jnp.bfloat16)
    packed = jnp.stack([q_local.reshape(row_count, own_width), hidden_in], axis=0)
    gathered = lax.all_gather(packed, "tp", axis=0)
    q_all = jnp.transpose(gathered[:, 0], (1, 0, 2)).reshape(
        row_count, kv_count, request_group_size, head_size
    )
    hidden_full = jnp.transpose(gathered[:, 1], (1, 0, 2)).reshape(row_count, model_width)

    k_new = apply_rotary_heads(
        fresh_key_value[:, 0].reshape(row_count, kv_count, head_size).astype(jnp.float32),
        positions,
        head_size,
    ).astype(jnp.bfloat16)
    value_fresh = fresh_key_value[:, 1].reshape(row_count, kv_count, head_size)
    own_score = (
        jnp.einsum("rcgd,rcd->rcg", q_all, k_new, preferred_element_type=jnp.float32)
        * score_scaling
    )

    segment_ends = jnp.cumsum(lengths[0], dtype=jnp.int32)
    segment_starts = segment_ends - lengths[0]
    cache_spots = tp_index * span_rows + jnp.arange(span_rows, dtype=jnp.int32)
    mask = (cache_spots[None, :] >= segment_starts[:, None]) & (
        cache_spots[None, :] < segment_ends[:, None]
    )
    mask = mask[:, None, None, :]
    keys = cache[:, 0]
    values = cache[:, 1]
    scores = (
        jnp.einsum("rcgd,jcd->rcgj", q_all, keys, preferred_element_type=jnp.float32)
        * score_scaling
    )
    scores = jnp.where(mask, scores, neg_floor)
    highest_local = jnp.max(scores, axis=3)
    weights = jnp.where(mask, jnp.exp(scores - highest_local[..., None]), 0.0)
    totals_local = jnp.sum(weights, axis=3)
    sums_local = jnp.einsum(
        "rcgj,jcd->rcgd",
        weights,
        values.astype(jnp.float32),
        precision=lax.Precision.HIGHEST,
        preferred_element_type=jnp.float32,
    )
    states = jnp.concatenate(
        [highest_local[..., None], totals_local[..., None], sums_local], axis=3
    ).reshape(row_count, tp_count, own_heads, head_size + 2)
    states = jnp.transpose(states, (1, 0, 2, 3))
    own_part_states = lax.dynamic_index_in_dim(states, tp_index, 0, keepdims=False)
    all_states = [own_part_states]
    for shift in range(1, tp_count):
        outgoing = lax.dynamic_index_in_dim(states, (tp_index + shift) % tp_count, 0, keepdims=False)
        all_states.append(
            lax.ppermute(outgoing, "tp", [(i, (i + shift) % tp_count) for i in range(tp_count)])
        )
    all_states = jnp.stack(all_states, axis=0)
    parts_highest = all_states[..., 0]
    parts_totals = all_states[..., 1]
    parts_sums = all_states[..., 2:]
    own_slice = lax.dynamic_slice_in_dim(own_score.reshape(row_count, head_count), first_head, own_heads, 1)
    top_score = jnp.maximum(jnp.max(parts_highest, axis=0), own_slice)
    factors = jnp.exp(parts_highest - top_score[None])
    own_part = jnp.exp(own_slice - top_score)
    if request_group_size % own_heads == 0:
        own_values = lax.dynamic_slice_in_dim(value_fresh, first_head // request_group_size, 1, 1)
        own_values = own_values.astype(jnp.float32)
    else:
        head_kv = (first_head + jnp.arange(own_heads, dtype=jnp.int32)) // request_group_size
        own_values = jnp.take(value_fresh, head_kv, axis=1).astype(jnp.float32)
    totals = jnp.sum(parts_totals * factors, axis=0) + own_part
    summed = jnp.sum(parts_sums * factors[..., None], axis=0) + own_values * own_part[..., None]
    attention_output = (summed / totals[..., None]).astype(jnp.bfloat16).reshape(
        row_count, own_heads * head_size
    )

    partial_proj = jnp.dot(attention_output, out_proj, preferred_element_type=jnp.float32)
    projected = jnp.sum(
        lax.all_gather(partial_proj.astype(jnp.bfloat16), "tp", axis=0).astype(jnp.float32), axis=0
    )
    residual = hidden_full.astype(jnp.float32) + projected
    mean_square = jnp.mean(residual * residual, axis=1, keepdims=True)
    normed = (residual * lax.rsqrt(mean_square + norm_eps) * norm_gain[None, :]).astype(jnp.bfloat16)
    residual_own = lax.dynamic_slice_in_dim(residual, tp_index * own_width, own_width, 1)

    local_count = gate_up.shape[0]
    block_total = local_count * req_count
    split_count = max(1, block_total // EXPERTS)
    expert_range = jnp.arange(EXPERTS, dtype=jnp.int32)
    member = jnp.any(expert_ids[:, :, None] == expert_range[None, None, :], axis=1)
    member_int = member.astype(jnp.int32)
    slot_of = jnp.cumsum(member_int, axis=0, dtype=jnp.int32) - member_int
    slot_taken = jnp.take_along_axis(slot_of, expert_ids, axis=1)
    block_taken = (slot_taken % split_count) * EXPERTS + expert_ids
    block_range = jnp.arange(block_total, dtype=jnp.int32)
    block_weights = jnp.sum(
        jnp.where(block_taken[:, :, None] == block_range[None, None, :], router_weights[:, :, None], 0.0),
        axis=1,
    )

    def gather_req(value):
        if req_count > 8 or req_count % tp_count != 0:
            gathered = lax.all_gather(value, "req", axis=0, tiled=True)
            return gathered, jnp.arange(req_count, dtype=jnp.int32)
        per_tp = req_count // tp_count
        fetched = []
        for slot in range(per_tp):
            pairs = []
            for group in range(req_count):
                for part in range(tp_count):
                    shift = per_tp * part + slot + 1
                    source = ((group - shift) % req_count) * tp_count + part
                    pairs.append((source, group * tp_count + part))
            fetched.append(lax.ppermute(value, ("req", "tp"), pairs))
        shared = lax.all_gather(jnp.stack(fetched, axis=0), "tp", axis=0)
        shared = shared.reshape((req_count * value.shape[0],) + value.shape[1:])
        groups = (req_index - jnp.arange(req_count, dtype=jnp.int32) - 1) % req_count
        return shared, groups.astype(jnp.int32)

    weight_high = lax.reduce_precision(block_weights, exponent_bits=8, mantissa_bits=7)
    weight_rest = block_weights - weight_high
    weight_mid = lax.reduce_precision(weight_rest, exponent_bits=8, mantissa_bits=7)
    weight_low = weight_rest - weight_mid
    code = jnp.concatenate([weight_high, weight_mid, weight_low], axis=1).astype(jnp.bfloat16)
    code_lanes = -(-code.shape[1] // 128) * 128
    code = jnp.pad(code, ((0, 0), (0, code_lanes - code.shape[1])))
    message = jnp.concatenate([normed, code], axis=1)
    message_all, message_groups = gather_req(message)
    offset = (req_index * local_count).astype(jnp.int32).reshape(1)
    mixed = expert_mix(
        message_all, gate_up, down, offset, message_groups, model_width, block_total, row_count, tp_count
    )
    mixed = lax.all_to_all(mixed, ("req", "tp"), 0, 0, tiled=True)
    mixed = jnp.sum(mixed.astype(jnp.float32), axis=0)
    return (residual_own + mixed).astype(jnp.bfloat16)


def solution(mesh):
    placed = (
        P("req", "tp"),
        P("req", "tp"),
        P("req", None, None),
        P("req"),
        P("req", None),
        P(("req", "tp"), None, None, None),
        P("tp", None),
        P(),
        P("req", None),
        P("req", None),
        P("req", None, None, "tp"),
        P("req", "tp", None),
    )
    return jax.shard_map(
        per_device, mesh=mesh, in_specs=placed, out_specs=P("req", "tp"), check_vma=False
    )
```

```python
import functools
import math

import jax
import jax.numpy as jnp
from jax import lax
from jax.experimental import pallas as pl
from jax.experimental.pallas import tpu as pltpu
from jax.sharding import PartitionSpec as P

EXPERTS = 32


rope_base = 1000000.0
norm_eps = 1e-06
neg_floor = -1e30


def apply_rotary_heads(values, positions, head_size):
    half_size = head_size // 2
    exponents = jnp.arange(half_size, dtype=jnp.float32) * (2.0 / head_size)
    inverse_freq = jnp.power(jnp.float32(rope_base), -exponents)
    angles = positions.astype(jnp.float32)[:, None] * inverse_freq[None, :]
    cosine = jnp.cos(angles)[:, None, :]
    sine = jnp.sin(angles)[:, None, :]
    first_half = values[..., :half_size]
    second_half = values[..., half_size:]
    return jnp.concatenate(
        [first_half * cosine - second_half * sine, second_half * cosine + first_half * sine],
        axis=-1,
    )


def _expert_body(
    offset_ref, dest_ref, x_ref, gu_ref, dn_ref, o_ref, acc_ref, *, width, block_total, row_count, tp_count
):
    block = pl.program_id(1)

    @pl.when(block == 0)
    def _():
        acc_ref[...] = jnp.zeros_like(acc_ref)

    x = x_ref[:, :width]
    contract_rows = (((1,), (1,)), ((), ()))
    gate_part = lax.dot_general(x, gu_ref[0, 0], contract_rows, preferred_element_type=jnp.float32)
    up_part = lax.dot_general(x, gu_ref[0, 1], contract_rows, preferred_element_type=jnp.float32)
    activation = (jnp.maximum(gate_part, 0.0) * up_part).astype(jnp.bfloat16)
    produced = jnp.dot(activation, dn_ref[0], preferred_element_type=jnp.float32)
    produced = produced.astype(jnp.bfloat16).astype(jnp.float32)
    code = x_ref[:, width:].astype(jnp.float32)
    lanes = lax.broadcasted_iota(jnp.int32, code.shape, 1)
    column = offset_ref[0] + block
    chosen = jnp.sum(jnp.where(lanes == column, code, 0.0), axis=1, keepdims=True)
    chosen = chosen + jnp.sum(jnp.where(lanes == column + block_total, code, 0.0), axis=1, keepdims=True)
    chosen = chosen + jnp.sum(jnp.where(lanes == column + 2 * block_total, code, 0.0), axis=1, keepdims=True)
    acc_ref[...] += chosen * produced

    @pl.when(block == pl.num_programs(1) - 1)
    def _():
        own_width = o_ref.shape[2]
        tile_groups = x_ref.shape[0] // row_count
        for group in range(tile_groups):
            dest = dest_ref[pl.program_id(0) * tile_groups + group] - pl.program_id(0) * tile_groups
            for part in range(tp_count):
                o_ref[dest * tp_count + part] = acc_ref[
                    group * row_count : (group + 1) * row_count,
                    part * own_width : (part + 1) * own_width,
                ].astype(o_ref.dtype)


def expert_mix(rows, gate_up, down, offset, dest, width, block_total, row_count, tp_count):
    row_total, message_width = rows.shape
    local_count, _, _, hidden = gate_up.shape
    group_total = row_total // row_count
    tile_groups = math.gcd(group_total, 8)
    tile = tile_groups * row_count
    own_width = width // tp_count
    gate_up_t = jnp.swapaxes(gate_up, 2, 3)
    body = functools.partial(
        _expert_body, width=width, block_total=block_total, row_count=row_count, tp_count=tp_count
    )
    return pl.pallas_call(
        body,
        grid=(group_total // tile_groups, local_count),
        in_specs=[
            pl.BlockSpec(memory_space=pltpu.SMEM),
            pl.BlockSpec(memory_space=pltpu.SMEM),
            pl.BlockSpec((tile, message_width), lambda i, b: (i, 0)),
            pl.BlockSpec((1, 2, hidden, width), lambda i, b: (b, 0, 0, 0)),
            pl.BlockSpec((1, hidden, width), lambda i, b: (b, 0, 0)),
        ],
        out_specs=pl.BlockSpec((tile_groups * tp_count, row_count, own_width), lambda i, b: (i, 0, 0)),
        out_shape=jax.ShapeDtypeStruct((group_total * tp_count, row_count, own_width), jnp.bfloat16),
        scratch_shapes=[pltpu.VMEM((tile, width), jnp.float32)],
        compiler_params=pltpu.CompilerParams(dimension_semantics=("parallel", "arbitrary")),
    )(offset, dest, rows, gate_up_t, down)


def per_device(
    hidden_in,
    queries,
    fresh_key_value,
    positions,
    lengths,
    cache,
    out_proj,
    norm_gain,
    expert_ids,
    router_weights,
    gate_up,
    down,
):
    tp_count = lax.axis_size("tp")
    req_count = lax.axis_size("req")
    tp_index = lax.axis_index("tp")
    req_index = lax.axis_index("req")
    row_count = hidden_in.shape[0]
    head_size = cache.shape[3]
    kv_count = cache.shape[2]
    own_heads = queries.shape[1] // head_size
    head_count = own_heads * tp_count
    request_group_size = head_count // kv_count
    score_scaling = head_size ** (-0.5)
    model_width = norm_gain.shape[0]
    own_width = hidden_in.shape[1]
    first_head = tp_index * own_heads
    span_rows = cache.shape[0]

    packed = jnp.stack([queries, hidden_in], axis=0)
    gathered = lax.all_gather(packed, "tp", axis=0)
    q_raw = jnp.transpose(gathered[:, 0], (1, 0, 2)).reshape(row_count, head_count, head_size)
    q_all = apply_rotary_heads(q_raw.astype(jnp.float32), positions, head_size).astype(jnp.bfloat16)
    q_all = q_all.reshape(row_count, kv_count, request_group_size, head_size)
    hidden_full = jnp.transpose(gathered[:, 1], (1, 0, 2)).reshape(row_count, model_width)

    k_new = apply_rotary_heads(
        fresh_key_value[:, 0].reshape(row_count, kv_count, head_size).astype(jnp.float32),
        positions,
        head_size,
    ).astype(jnp.bfloat16)
    value_fresh = fresh_key_value[:, 1].reshape(row_count, kv_count, head_size)
    own_score = (
        jnp.einsum("rcgd,rcd->rcg", q_all, k_new, preferred_element_type=jnp.float32)
        * score_scaling
    )

    segment_ends = jnp.cumsum(lengths[0], dtype=jnp.int32)
    segment_starts = segment_ends - lengths[0]
    cache_spots = tp_index * span_rows + jnp.arange(span_rows, dtype=jnp.int32)
    mask = (cache_spots[None, :] >= segment_starts[:, None]) & (
        cache_spots[None, :] < segment_ends[:, None]
    )
    mask = mask[:, None, None, :]
    keys = cache[:, 0]
    values = cache[:, 1]
    scores = (
        jnp.einsum("rcgd,jcd->rcgj", q_all, keys, preferred_element_type=jnp.float32)
        * score_scaling
    )
    scores = jnp.where(mask, scores, neg_floor)
    highest_local = jnp.max(scores, axis=3)
    weights = jnp.where(mask, jnp.exp(scores - highest_local[..., None]), 0.0)
    totals_local = jnp.sum(weights, axis=3)
    sums_local = jnp.einsum(
        "rcgj,jcd->rcgd",
        weights,
        values.astype(jnp.float32),
        precision=lax.Precision.HIGHEST,
        preferred_element_type=jnp.float32,
    )
    states = jnp.concatenate(
        [highest_local[..., None], totals_local[..., None], sums_local], axis=3
    ).reshape(row_count, tp_count, own_heads, head_size + 2)
    states = jnp.transpose(states, (1, 0, 2, 3))
    own_part_states = lax.dynamic_index_in_dim(states, tp_index, 0, keepdims=False)
    all_states = [own_part_states]
    for shift in range(1, tp_count):
        outgoing = lax.dynamic_index_in_dim(states, (tp_index + shift) % tp_count, 0, keepdims=False)
        all_states.append(
            lax.ppermute(outgoing, "tp", [(i, (i + shift) % tp_count) for i in range(tp_count)])
        )
    all_states = jnp.stack(all_states, axis=0)
    parts_highest = all_states[..., 0]
    parts_totals = all_states[..., 1]
    parts_sums = all_states[..., 2:]
    own_slice = lax.dynamic_slice_in_dim(own_score.reshape(row_count, head_count), first_head, own_heads, 1)
    top_score = jnp.maximum(jnp.max(parts_highest, axis=0), own_slice)
    factors = jnp.exp(parts_highest - top_score[None])
    own_part = jnp.exp(own_slice - top_score)
    if request_group_size % own_heads == 0:
        own_values = lax.dynamic_slice_in_dim(value_fresh, first_head // request_group_size, 1, 1)
        own_values = own_values.astype(jnp.float32)
    else:
        head_kv = (first_head + jnp.arange(own_heads, dtype=jnp.int32)) // request_group_size
        own_values = jnp.take(value_fresh, head_kv, axis=1).astype(jnp.float32)
    totals = jnp.sum(parts_totals * factors, axis=0) + own_part
    summed = jnp.sum(parts_sums * factors[..., None], axis=0) + own_values * own_part[..., None]
    attention_output = (summed / totals[..., None]).astype(jnp.bfloat16).reshape(
        row_count, own_heads * head_size
    )

    partial_proj = jnp.dot(attention_output, out_proj, preferred_element_type=jnp.float32)
    projected = jnp.sum(
        lax.all_gather(partial_proj.astype(jnp.bfloat16), "tp", axis=0).astype(jnp.float32), axis=0
    )
    residual = hidden_full.astype(jnp.float32) + projected
    mean_square = jnp.mean(residual * residual, axis=1, keepdims=True)
    normed = (residual * lax.rsqrt(mean_square + norm_eps) * norm_gain[None, :]).astype(jnp.bfloat16)
    residual_own = lax.dynamic_slice_in_dim(residual, tp_index * own_width, own_width, 1)

    local_count = gate_up.shape[0]
    block_total = local_count * req_count
    split_count = max(1, block_total // EXPERTS)
    expert_range = jnp.arange(EXPERTS, dtype=jnp.int32)
    member = jnp.any(expert_ids[:, :, None] == expert_range[None, None, :], axis=1)
    member_int = member.astype(jnp.int32)
    slot_of = jnp.cumsum(member_int, axis=0, dtype=jnp.int32) - member_int
    slot_taken = jnp.take_along_axis(slot_of, expert_ids, axis=1)
    block_taken = (slot_taken % split_count) * EXPERTS + expert_ids
    block_range = jnp.arange(block_total, dtype=jnp.int32)
    block_weights = jnp.sum(
        jnp.where(block_taken[:, :, None] == block_range[None, None, :], router_weights[:, :, None], 0.0),
        axis=1,
    )

    def gather_req(value):
        if req_count > 8 or req_count % tp_count != 0:
            gathered = lax.all_gather(value, "req", axis=0, tiled=True)
            return gathered, jnp.arange(req_count, dtype=jnp.int32)
        per_tp = req_count // tp_count
        fetched = []
        for slot in range(per_tp):
            pairs = []
            for group in range(req_count):
                for part in range(tp_count):
                    shift = per_tp * part + slot + 1
                    source = ((group - shift) % req_count) * tp_count + part
                    pairs.append((source, group * tp_count + part))
            fetched.append(lax.ppermute(value, ("req", "tp"), pairs))
        shared = lax.all_gather(jnp.stack(fetched, axis=0), "tp", axis=0)
        shared = shared.reshape((req_count * value.shape[0],) + value.shape[1:])
        groups = (req_index - jnp.arange(req_count, dtype=jnp.int32) - 1) % req_count
        return shared, groups.astype(jnp.int32)

    weight_high = lax.reduce_precision(block_weights, exponent_bits=8, mantissa_bits=7)
    weight_rest = block_weights - weight_high
    weight_mid = lax.reduce_precision(weight_rest, exponent_bits=8, mantissa_bits=7)
    weight_low = weight_rest - weight_mid
    code = jnp.concatenate([weight_high, weight_mid, weight_low], axis=1).astype(jnp.bfloat16)
    code_lanes = -(-code.shape[1] // 128) * 128
    code = jnp.pad(code, ((0, 0), (0, code_lanes - code.shape[1])))
    message = jnp.concatenate([normed, code], axis=1)
    message_all, message_groups = gather_req(message)
    offset = (req_index * local_count).astype(jnp.int32).reshape(1)
    mixed = expert_mix(
        message_all, gate_up, down, offset, message_groups, model_width, block_total, row_count, tp_count
    )
    mixed = lax.all_to_all(mixed, ("req", "tp"), 0, 0, tiled=True)
    mixed = jnp.sum(mixed.astype(jnp.float32), axis=0)
    return (residual_own + mixed).astype(jnp.bfloat16)


def solution(mesh):
    placed = (
        P("req", "tp"),
        P("req", "tp"),
        P("req", None, None),
        P("req"),
        P("req", None),
        P(("req", "tp"), None, None, None),
        P("tp", None),
        P(),
        P("req", None),
        P("req", None),
        P("req", None, None, "tp"),
        P("req", "tp", None),
    )
    return jax.shard_map(
        per_device, mesh=mesh, in_specs=placed, out_specs=P("req", "tp"), check_vma=False
    )
```

```python
import functools
import math

import jax
import jax.numpy as jnp
from jax import lax
from jax.experimental import pallas as pl
from jax.experimental.pallas import tpu as pltpu
from jax.sharding import PartitionSpec as P

EXPERTS = 32


rope_base = 1000000.0
norm_eps = 1e-06
neg_floor = -1e30


def apply_rotary_heads(values, positions, head_size):
    half_size = head_size // 2
    exponents = jnp.arange(half_size, dtype=jnp.float32) * (2.0 / head_size)
    inverse_freq = jnp.power(jnp.float32(rope_base), -exponents)
    angles = positions.astype(jnp.float32)[:, None] * inverse_freq[None, :]
    cosine = jnp.cos(angles)[:, None, :]
    sine = jnp.sin(angles)[:, None, :]
    first_half = values[..., :half_size]
    second_half = values[..., half_size:]
    return jnp.concatenate(
        [first_half * cosine - second_half * sine, second_half * cosine + first_half * sine],
        axis=-1,
    )


def _expert_body(
    index_ref, x_ref, gu_ref, dn_ref, o_ref, acc_ref, *, width, block_total, row_count, tp_count, arrival_order
):
    block = pl.program_id(1)

    @pl.when(block == 0)
    def _():
        acc_ref[...] = jnp.zeros_like(acc_ref)

    x = x_ref[:, :width]
    contract_rows = (((1,), (1,)), ((), ()))
    gate_part = lax.dot_general(x, gu_ref[0, 0], contract_rows, preferred_element_type=jnp.float32)
    up_part = lax.dot_general(x, gu_ref[0, 1], contract_rows, preferred_element_type=jnp.float32)
    activation = (jnp.maximum(gate_part, 0.0) * up_part).astype(jnp.bfloat16)
    produced = jnp.dot(activation, dn_ref[0], preferred_element_type=jnp.float32)
    produced = produced.astype(jnp.bfloat16).astype(jnp.float32)
    code = x_ref[:, width:].astype(jnp.float32)
    lanes = lax.broadcasted_iota(jnp.int32, code.shape, 1)
    local_count = pl.num_programs(1)
    column = index_ref[0] * local_count + block
    chosen = jnp.sum(jnp.where(lanes == column, code, 0.0), axis=1, keepdims=True)
    chosen = chosen + jnp.sum(jnp.where(lanes == column + block_total, code, 0.0), axis=1, keepdims=True)
    chosen = chosen + jnp.sum(jnp.where(lanes == column + 2 * block_total, code, 0.0), axis=1, keepdims=True)
    acc_ref[...] += chosen * produced

    @pl.when(block == pl.num_programs(1) - 1)
    def _():
        own_width = o_ref.shape[2]
        tile_groups = x_ref.shape[0] // row_count
        for group in range(tile_groups):
            if arrival_order:
                group_total = o_ref.shape[0] // tp_count
                dest = (index_ref[0] + 2 * group_total - group - 1) % group_total
            else:
                dest = group
            for part in range(tp_count):
                o_ref[dest * tp_count + part] = acc_ref[
                    group * row_count : (group + 1) * row_count,
                    part * own_width : (part + 1) * own_width,
                ].astype(o_ref.dtype)


def expert_mix(rows, gate_up, down, req_index, arrival_order, width, block_total, row_count, tp_count):
    row_total, message_width = rows.shape
    local_count, _, _, hidden = gate_up.shape
    group_total = row_total // row_count
    tile_groups = math.gcd(group_total, 8)
    tile = tile_groups * row_count
    own_width = width // tp_count
    gate_up_t = jnp.swapaxes(gate_up, 2, 3)
    body = functools.partial(
        _expert_body,
        width=width,
        block_total=block_total,
        row_count=row_count,
        tp_count=tp_count,
        arrival_order=arrival_order,
    )
    return pl.pallas_call(
        body,
        grid=(group_total // tile_groups, local_count),
        in_specs=[
            pl.BlockSpec(memory_space=pltpu.SMEM),
            pl.BlockSpec((tile, message_width), lambda i, b: (i, 0)),
            pl.BlockSpec((1, 2, hidden, width), lambda i, b: (b, 0, 0, 0)),
            pl.BlockSpec((1, hidden, width), lambda i, b: (b, 0, 0)),
        ],
        out_specs=pl.BlockSpec((tile_groups * tp_count, row_count, own_width), lambda i, b: (i, 0, 0)),
        out_shape=jax.ShapeDtypeStruct((group_total * tp_count, row_count, own_width), jnp.bfloat16),
        scratch_shapes=[pltpu.VMEM((tile, width), jnp.float32)],
        compiler_params=pltpu.CompilerParams(dimension_semantics=("parallel", "arbitrary")),
    )(req_index, rows, gate_up_t, down)


def per_device(
    hidden_in,
    queries,
    fresh_key_value,
    positions,
    lengths,
    cache,
    out_proj,
    norm_gain,
    expert_ids,
    router_weights,
    gate_up,
    down,
):
    tp_count = lax.axis_size("tp")
    req_count = lax.axis_size("req")
    tp_index = lax.axis_index("tp")
    req_index = lax.axis_index("req")
    row_count = hidden_in.shape[0]
    head_size = cache.shape[3]
    kv_count = cache.shape[2]
    own_heads = queries.shape[1] // head_size
    head_count = own_heads * tp_count
    request_group_size = head_count // kv_count
    score_scaling = head_size ** (-0.5)
    model_width = norm_gain.shape[0]
    own_width = hidden_in.shape[1]
    first_head = tp_index * own_heads
    span_rows = cache.shape[0]

    gathered = lax.all_gather(queries, "tp", axis=0)
    q_raw = jnp.transpose(gathered, (1, 0, 2)).reshape(row_count, head_count, head_size)
    q_all = apply_rotary_heads(q_raw.astype(jnp.float32), positions, head_size).astype(jnp.bfloat16)
    q_all = q_all.reshape(row_count, kv_count, request_group_size, head_size)

    k_new = apply_rotary_heads(
        fresh_key_value[:, 0].reshape(row_count, kv_count, head_size).astype(jnp.float32),
        positions,
        head_size,
    ).astype(jnp.bfloat16)
    value_fresh = fresh_key_value[:, 1].reshape(row_count, kv_count, head_size)
    own_score = (
        jnp.einsum("rcgd,rcd->rcg", q_all, k_new, preferred_element_type=jnp.float32)
        * score_scaling
    )

    segment_ends = jnp.cumsum(lengths[0], dtype=jnp.int32)
    segment_starts = segment_ends - lengths[0]
    cache_spots = tp_index * span_rows + jnp.arange(span_rows, dtype=jnp.int32)
    mask = (cache_spots[None, :] >= segment_starts[:, None]) & (
        cache_spots[None, :] < segment_ends[:, None]
    )
    mask = mask[:, None, None, :]
    keys = cache[:, 0]
    values = cache[:, 1]
    scores = (
        jnp.einsum("rcgd,jcd->rcgj", q_all, keys, preferred_element_type=jnp.float32)
        * score_scaling
    )
    scores = jnp.where(mask, scores, neg_floor)
    highest_local = jnp.max(scores, axis=3)
    weights = jnp.where(mask, jnp.exp(scores - highest_local[..., None]), 0.0)
    totals_local = jnp.sum(weights, axis=3)
    sums_local = jnp.einsum(
        "rcgj,jcd->rcgd",
        weights,
        values.astype(jnp.float32),
        precision=lax.Precision.HIGHEST,
        preferred_element_type=jnp.float32,
    )
    states = jnp.concatenate(
        [highest_local[..., None], totals_local[..., None], sums_local], axis=3
    ).reshape(row_count, tp_count, own_heads, head_size + 2)
    states = jnp.transpose(states, (1, 0, 2, 3))
    own_part_states = lax.dynamic_index_in_dim(states, tp_index, 0, keepdims=False)
    all_states = [own_part_states]
    for shift in range(1, tp_count):
        outgoing = lax.dynamic_index_in_dim(states, (tp_index + shift) % tp_count, 0, keepdims=False)
        all_states.append(
            lax.ppermute(outgoing, "tp", [(i, (i + shift) % tp_count) for i in range(tp_count)])
        )
    all_states = jnp.stack(all_states, axis=0)
    parts_highest = all_states[..., 0]
    parts_totals = all_states[..., 1]
    parts_sums = all_states[..., 2:]
    own_slice = lax.dynamic_slice_in_dim(own_score.reshape(row_count, head_count), first_head, own_heads, 1)
    top_score = jnp.maximum(jnp.max(parts_highest, axis=0), own_slice)
    factors = jnp.exp(parts_highest - top_score[None])
    own_part = jnp.exp(own_slice - top_score)
    if request_group_size % own_heads == 0:
        own_values = lax.dynamic_slice_in_dim(value_fresh, first_head // request_group_size, 1, 1)
        own_values = own_values.astype(jnp.float32)
    else:
        head_kv = (first_head + jnp.arange(own_heads, dtype=jnp.int32)) // request_group_size
        own_values = jnp.take(value_fresh, head_kv, axis=1).astype(jnp.float32)
    totals = jnp.sum(parts_totals * factors, axis=0) + own_part
    summed = jnp.sum(parts_sums * factors[..., None], axis=0) + own_values * own_part[..., None]
    attention_output = (summed / totals[..., None]).astype(jnp.bfloat16).reshape(
        row_count, own_heads * head_size
    )

    partial_proj = jnp.dot(attention_output, out_proj, preferred_element_type=jnp.float32)
    proj_message = jnp.concatenate([partial_proj.astype(jnp.bfloat16), hidden_in], axis=1)
    proj_all = lax.all_gather(proj_message, "tp", axis=0)
    projected = jnp.sum(proj_all[:, :, :model_width].astype(jnp.float32), axis=0)
    hidden_full = jnp.transpose(proj_all[:, :, model_width:], (1, 0, 2)).reshape(row_count, model_width)
    residual = hidden_full.astype(jnp.float32) + projected
    mean_square = jnp.mean(residual * residual, axis=1, keepdims=True)
    normed = (residual * lax.rsqrt(mean_square + norm_eps) * norm_gain[None, :]).astype(jnp.bfloat16)
    residual_own = lax.dynamic_slice_in_dim(residual, tp_index * own_width, own_width, 1)

    local_count = gate_up.shape[0]
    block_total = local_count * req_count
    split_count = max(1, block_total // EXPERTS)
    expert_range = jnp.arange(EXPERTS, dtype=jnp.int32)
    member = jnp.any(expert_ids[:, :, None] == expert_range[None, None, :], axis=1)
    member_int = member.astype(jnp.int32)
    slot_of = jnp.cumsum(member_int, axis=0, dtype=jnp.int32) - member_int
    slot_taken = jnp.take_along_axis(slot_of, expert_ids, axis=1)
    block_taken = (slot_taken % split_count) * EXPERTS + expert_ids
    block_range = jnp.arange(block_total, dtype=jnp.int32)
    block_weights = jnp.sum(
        jnp.where(block_taken[:, :, None] == block_range[None, None, :], router_weights[:, :, None], 0.0),
        axis=1,
    )

    def gather_req(value):
        if req_count > 8 or 8 % req_count != 0 or req_count % tp_count != 0:
            return lax.all_gather(value, "req", axis=0, tiled=True), False
        per_tp = req_count // tp_count
        fetched = []
        for slot in range(per_tp):
            pairs = []
            for group in range(req_count):
                for part in range(tp_count):
                    shift = per_tp * part + slot + 1
                    source = ((group - shift) % req_count) * tp_count + part
                    pairs.append((source, group * tp_count + part))
            fetched.append(lax.ppermute(value, ("req", "tp"), pairs))
        shared = lax.all_gather(jnp.stack(fetched, axis=0), "tp", axis=0)
        shared = shared.reshape((req_count * value.shape[0],) + value.shape[1:])
        return shared, True

    weight_high = lax.reduce_precision(block_weights, exponent_bits=8, mantissa_bits=7)
    weight_rest = block_weights - weight_high
    weight_mid = lax.reduce_precision(weight_rest, exponent_bits=8, mantissa_bits=7)
    weight_low = weight_rest - weight_mid
    code = jnp.concatenate([weight_high, weight_mid, weight_low], axis=1).astype(jnp.bfloat16)
    code_lanes = -(-code.shape[1] // 128) * 128
    code = jnp.pad(code, ((0, 0), (0, code_lanes - code.shape[1])))
    message = jnp.concatenate([normed, code], axis=1)
    message_all, arrival_order = gather_req(message)
    index_scalar = req_index.astype(jnp.int32).reshape(1)
    mixed = expert_mix(
        message_all, gate_up, down, index_scalar, arrival_order, model_width, block_total, row_count, tp_count
    )
    mixed = lax.all_to_all(mixed, ("req", "tp"), 0, 0, tiled=True)
    mixed = jnp.sum(mixed.astype(jnp.float32), axis=0)
    return (residual_own + mixed).astype(jnp.bfloat16)


def solution(mesh):
    placed = (
        P("req", "tp"),
        P("req", "tp"),
        P("req", None, None),
        P("req"),
        P("req", None),
        P(("req", "tp"), None, None, None),
        P("tp", None),
        P(),
        P("req", None),
        P("req", None),
        P("req", None, None, "tp"),
        P("req", "tp", None),
    )
    return jax.shard_map(
        per_device, mesh=mesh, in_specs=placed, out_specs=P("req", "tp"), check_vma=False
    )
```

```python
import functools
import math

import jax
import jax.numpy as jnp
from jax import lax
from jax.experimental import pallas as pl
from jax.experimental.pallas import tpu as pltpu
from jax.sharding import PartitionSpec as P

EXPERTS = 32


rope_base = 1000000.0
norm_eps = 1e-06
neg_floor = -1e30


def apply_rotary_heads(values, positions, head_size):
    half_size = head_size // 2
    exponents = jnp.arange(half_size, dtype=jnp.float32) * (2.0 / head_size)
    inverse_freq = jnp.power(jnp.float32(rope_base), -exponents)
    angles = positions.astype(jnp.float32)[:, None] * inverse_freq[None, :]
    cosine = jnp.cos(angles)[:, None, :]
    sine = jnp.sin(angles)[:, None, :]
    first_half = values[..., :half_size]
    second_half = values[..., half_size:]
    return jnp.concatenate(
        [first_half * cosine - second_half * sine, second_half * cosine + first_half * sine],
        axis=-1,
    )


def _expert_body(
    index_ref, x_ref, gu_ref, dn_ref, o_ref, acc_ref, *, width, block_total, row_count, tp_count, arrival_order
):
    block = pl.program_id(1)

    @pl.when(block == 0)
    def _():
        acc_ref[...] = jnp.zeros_like(acc_ref)

    x = x_ref[:, :width]
    contract_rows = (((1,), (1,)), ((), ()))
    gate_part = lax.dot_general(x, gu_ref[0, 0], contract_rows, preferred_element_type=jnp.float32)
    up_part = lax.dot_general(x, gu_ref[0, 1], contract_rows, preferred_element_type=jnp.float32)
    activation = (jnp.maximum(gate_part, 0.0) * up_part).astype(jnp.bfloat16)
    produced = jnp.dot(activation, dn_ref[0], preferred_element_type=jnp.float32)
    produced = produced.astype(jnp.bfloat16).astype(jnp.float32)
    code = x_ref[:, width:].astype(jnp.float32)
    lanes = lax.broadcasted_iota(jnp.int32, code.shape, 1)
    local_count = pl.num_programs(1)
    column = index_ref[0] * local_count + block
    chosen = jnp.sum(jnp.where(lanes == column, code, 0.0), axis=1, keepdims=True)
    chosen = chosen + jnp.sum(jnp.where(lanes == column + block_total, code, 0.0), axis=1, keepdims=True)
    chosen = chosen + jnp.sum(jnp.where(lanes == column + 2 * block_total, code, 0.0), axis=1, keepdims=True)
    acc_ref[...] += chosen * produced

    @pl.when(block == pl.num_programs(1) - 1)
    def _():
        own_width = o_ref.shape[2]
        tile_groups = x_ref.shape[0] // row_count
        for group in range(tile_groups):
            if arrival_order:
                group_total = o_ref.shape[0] // tp_count
                dest = (index_ref[0] + 2 * group_total - group - 1) % group_total
            else:
                dest = group
            for part in range(tp_count):
                o_ref[dest * tp_count + part] = acc_ref[
                    group * row_count : (group + 1) * row_count,
                    part * own_width : (part + 1) * own_width,
                ].astype(o_ref.dtype)


def expert_mix(rows, gate_up, down, req_index, arrival_order, width, block_total, row_count, tp_count):
    row_total, message_width = rows.shape
    local_count, _, _, hidden = gate_up.shape
    group_total = row_total // row_count
    tile_groups = math.gcd(group_total, 8)
    tile = tile_groups * row_count
    own_width = width // tp_count
    gate_up_t = jnp.swapaxes(gate_up, 2, 3)
    body = functools.partial(
        _expert_body,
        width=width,
        block_total=block_total,
        row_count=row_count,
        tp_count=tp_count,
        arrival_order=arrival_order,
    )
    return pl.pallas_call(
        body,
        grid=(group_total // tile_groups, local_count),
        in_specs=[
            pl.BlockSpec(memory_space=pltpu.SMEM),
            pl.BlockSpec((tile, message_width), lambda i, b: (i, 0)),
            pl.BlockSpec((1, 2, hidden, width), lambda i, b: (b, 0, 0, 0)),
            pl.BlockSpec((1, hidden, width), lambda i, b: (b, 0, 0)),
        ],
        out_specs=pl.BlockSpec((tile_groups * tp_count, row_count, own_width), lambda i, b: (i, 0, 0)),
        out_shape=jax.ShapeDtypeStruct((group_total * tp_count, row_count, own_width), jnp.bfloat16),
        scratch_shapes=[pltpu.VMEM((tile, width), jnp.float32)],
        compiler_params=pltpu.CompilerParams(dimension_semantics=("parallel", "arbitrary")),
    )(req_index, rows, gate_up_t, down)


def per_device(
    hidden_in,
    queries,
    fresh_key_value,
    positions,
    lengths,
    cache,
    out_proj,
    norm_gain,
    expert_ids,
    router_weights,
    gate_up,
    down,
):
    tp_count = lax.axis_size("tp")
    req_count = lax.axis_size("req")
    tp_index = lax.axis_index("tp")
    req_index = lax.axis_index("req")
    row_count = hidden_in.shape[0]
    head_size = cache.shape[3]
    kv_count = cache.shape[2]
    own_heads = queries.shape[1] // head_size
    head_count = own_heads * tp_count
    request_group_size = head_count // kv_count
    score_scaling = head_size ** (-0.5)
    model_width = norm_gain.shape[0]
    own_width = hidden_in.shape[1]
    first_head = tp_index * own_heads
    span_rows = cache.shape[0]

    packed = jnp.stack([queries, hidden_in], axis=0)
    gathered = lax.all_gather(packed, "tp", axis=0)
    q_raw = jnp.transpose(gathered[:, 0], (1, 0, 2)).reshape(row_count, head_count, head_size)
    q_all = apply_rotary_heads(q_raw.astype(jnp.float32), positions, head_size).astype(jnp.bfloat16)
    q_all = q_all.reshape(row_count, kv_count, request_group_size, head_size)
    hidden_full = jnp.transpose(gathered[:, 1], (1, 0, 2)).reshape(row_count, model_width)

    k_new = apply_rotary_heads(
        fresh_key_value[:, 0].reshape(row_count, kv_count, head_size).astype(jnp.float32),
        positions,
        head_size,
    ).astype(jnp.bfloat16)
    value_fresh = fresh_key_value[:, 1].reshape(row_count, kv_count, head_size)
    own_score = (
        jnp.einsum("rcgd,rcd->rcg", q_all, k_new, preferred_element_type=jnp.float32)
        * score_scaling
    )

    segment_ends = jnp.cumsum(lengths[0], dtype=jnp.int32)
    segment_starts = segment_ends - lengths[0]
    cache_spots = tp_index * span_rows + jnp.arange(span_rows, dtype=jnp.int32)
    mask = (cache_spots[None, :] >= segment_starts[:, None]) & (
        cache_spots[None, :] < segment_ends[:, None]
    )
    mask = mask[:, None, None, :]
    keys = cache[:, 0]
    values = cache[:, 1]
    scores = (
        jnp.einsum("rcgd,jcd->rcgj", q_all, keys, preferred_element_type=jnp.float32)
        * score_scaling
    )
    scores = jnp.where(mask, scores, neg_floor)
    highest_local = jnp.max(scores, axis=3)
    weights = jnp.where(mask, jnp.exp(scores - highest_local[..., None]), 0.0)
    totals_local = jnp.sum(weights, axis=3)
    sums_local = jnp.einsum(
        "rcgj,jcd->rcgd",
        weights,
        values.astype(jnp.float32),
        precision=lax.Precision.HIGHEST,
        preferred_element_type=jnp.float32,
    )
    states = jnp.concatenate(
        [highest_local[..., None], totals_local[..., None], sums_local], axis=3
    ).reshape(row_count, tp_count, own_heads, head_size + 2)
    states = jnp.transpose(states, (1, 0, 2, 3))
    own_part_states = lax.dynamic_index_in_dim(states, tp_index, 0, keepdims=False)
    all_states = [own_part_states]
    for shift in range(1, tp_count):
        outgoing = lax.dynamic_index_in_dim(states, (tp_index + shift) % tp_count, 0, keepdims=False)
        all_states.append(
            lax.ppermute(outgoing, "tp", [(i, (i + shift) % tp_count) for i in range(tp_count)])
        )
    all_states = jnp.stack(all_states, axis=0)
    parts_highest = all_states[..., 0]
    parts_totals = all_states[..., 1]
    parts_sums = all_states[..., 2:]
    own_slice = lax.dynamic_slice_in_dim(own_score.reshape(row_count, head_count), first_head, own_heads, 1)
    top_score = jnp.maximum(jnp.max(parts_highest, axis=0), own_slice)
    factors = jnp.exp(parts_highest - top_score[None])
    own_part = jnp.exp(own_slice - top_score)
    if request_group_size % own_heads == 0:
        own_values = lax.dynamic_slice_in_dim(value_fresh, first_head // request_group_size, 1, 1)
        own_values = own_values.astype(jnp.float32)
    else:
        head_kv = (first_head + jnp.arange(own_heads, dtype=jnp.int32)) // request_group_size
        own_values = jnp.take(value_fresh, head_kv, axis=1).astype(jnp.float32)
    totals = jnp.sum(parts_totals * factors, axis=0) + own_part
    summed = jnp.sum(parts_sums * factors[..., None], axis=0) + own_values * own_part[..., None]
    attention_output = (summed / totals[..., None]).astype(jnp.bfloat16).reshape(
        row_count, own_heads * head_size
    )

    partial_proj = jnp.dot(attention_output, out_proj, preferred_element_type=jnp.float32)
    projected = jnp.sum(
        lax.all_gather(partial_proj.astype(jnp.bfloat16), "tp", axis=0).astype(jnp.float32), axis=0
    )
    residual = hidden_full.astype(jnp.float32) + projected
    mean_square = jnp.mean(residual * residual, axis=1, keepdims=True)
    normed = (residual * lax.rsqrt(mean_square + norm_eps) * norm_gain[None, :]).astype(jnp.bfloat16)
    residual_own = lax.dynamic_slice_in_dim(residual, tp_index * own_width, own_width, 1)

    local_count = gate_up.shape[0]
    block_total = local_count * req_count
    split_count = max(1, block_total // EXPERTS)
    expert_range = jnp.arange(EXPERTS, dtype=jnp.int32)
    member = jnp.any(expert_ids[:, :, None] == expert_range[None, None, :], axis=1)
    member_int = member.astype(jnp.int32)
    slot_of = jnp.cumsum(member_int, axis=0, dtype=jnp.int32) - member_int
    slot_taken = jnp.take_along_axis(slot_of, expert_ids, axis=1)
    block_taken = (slot_taken % split_count) * EXPERTS + expert_ids
    block_range = jnp.arange(block_total, dtype=jnp.int32)
    block_weights = jnp.sum(
        jnp.where(block_taken[:, :, None] == block_range[None, None, :], router_weights[:, :, None], 0.0),
        axis=1,
    )

    def gather_req(value):
        if req_count > 8 or 8 % req_count != 0 or req_count % tp_count != 0:
            return lax.all_gather(value, "req", axis=0, tiled=True), False
        per_tp = req_count // tp_count
        fetched = []
        for slot in range(per_tp):
            pairs = []
            for group in range(req_count):
                for part in range(tp_count):
                    shift = per_tp * part + slot + 1
                    source = ((group - shift) % req_count) * tp_count + part
                    pairs.append((source, group * tp_count + part))
            fetched.append(lax.ppermute(value, ("req", "tp"), pairs))
        shared = lax.all_gather(jnp.stack(fetched, axis=0), "tp", axis=0)
        shared = shared.reshape((req_count * value.shape[0],) + value.shape[1:])
        return shared, True

    weight_high = lax.reduce_precision(block_weights, exponent_bits=8, mantissa_bits=7)
    weight_rest = block_weights - weight_high
    weight_mid = lax.reduce_precision(weight_rest, exponent_bits=8, mantissa_bits=7)
    weight_low = weight_rest - weight_mid
    code = jnp.concatenate([weight_high, weight_mid, weight_low], axis=1).astype(jnp.bfloat16)
    code_lanes = -(-code.shape[1] // 128) * 128
    code = jnp.pad(code, ((0, 0), (0, code_lanes - code.shape[1])))
    message = jnp.concatenate([normed, code], axis=1)
    message_all, arrival_order = gather_req(message)
    index_scalar = req_index.astype(jnp.int32).reshape(1)
    mixed = expert_mix(
        message_all, gate_up, down, index_scalar, arrival_order, model_width, block_total, row_count, tp_count
    )
    mixed = lax.all_to_all(mixed, ("req", "tp"), 0, 0, tiled=True)
    mixed = jnp.sum(mixed.astype(jnp.float32), axis=0)
    return (residual_own + mixed).astype(jnp.bfloat16)


def solution(mesh):
    placed = (
        P("req", "tp"),
        P("req", "tp"),
        P("req", None, None),
        P("req"),
        P("req", None),
        P(("req", "tp"), None, None, None),
        P("tp", None),
        P(),
        P("req", None),
        P("req", None),
        P("req", None, None, "tp"),
        P("req", "tp", None),
    )
    return jax.shard_map(
        per_device, mesh=mesh, in_specs=placed, out_specs=P("req", "tp"), check_vma=False
    )
```

```python
import functools
import math

import jax
import jax.numpy as jnp
from jax import lax
from jax.experimental import pallas as pl
from jax.experimental.pallas import tpu as pltpu
from jax.sharding import PartitionSpec as P

EXPERTS = 32


rope_base = 1000000.0
norm_eps = 1e-06
neg_floor = -1e30


def apply_rotary_heads(values, positions, head_size):
    half_size = head_size // 2
    exponents = jnp.arange(half_size, dtype=jnp.float32) * (2.0 / head_size)
    inverse_freq = jnp.power(jnp.float32(rope_base), -exponents)
    angles = positions.astype(jnp.float32)[:, None] * inverse_freq[None, :]
    cosine = jnp.cos(angles)[:, None, :]
    sine = jnp.sin(angles)[:, None, :]
    first_half = values[..., :half_size]
    second_half = values[..., half_size:]
    return jnp.concatenate(
        [first_half * cosine - second_half * sine, second_half * cosine + first_half * sine],
        axis=-1,
    )


def _expert_body(
    index_ref, x_ref, gu_ref, dn_ref, o_ref, acc_ref, *, width, block_total, row_count, tp_count, arrival_order
):
    block = pl.program_id(1)

    @pl.when(block == 0)
    def _():
        acc_ref[...] = jnp.zeros_like(acc_ref)

    x = x_ref[:, :width]
    contract_rows = (((1,), (1,)), ((), ()))
    gate_part = lax.dot_general(x, gu_ref[0, 0], contract_rows, preferred_element_type=jnp.float32)
    up_part = lax.dot_general(x, gu_ref[0, 1], contract_rows, preferred_element_type=jnp.float32)
    activation = (jnp.maximum(gate_part, 0.0) * up_part).astype(jnp.bfloat16)
    produced = jnp.dot(activation, dn_ref[0], preferred_element_type=jnp.float32)
    produced = produced.astype(jnp.bfloat16).astype(jnp.float32)
    code = x_ref[:, width:].astype(jnp.float32)
    lanes = lax.broadcasted_iota(jnp.int32, code.shape, 1)
    local_count = pl.num_programs(1)
    column = index_ref[0] * local_count + block
    chosen = jnp.sum(jnp.where(lanes == column, code, 0.0), axis=1, keepdims=True)
    chosen = chosen + jnp.sum(jnp.where(lanes == column + block_total, code, 0.0), axis=1, keepdims=True)
    chosen = chosen + jnp.sum(jnp.where(lanes == column + 2 * block_total, code, 0.0), axis=1, keepdims=True)
    acc_ref[...] += chosen * produced

    @pl.when(block == pl.num_programs(1) - 1)
    def _():
        own_width = o_ref.shape[2]
        tile_groups = x_ref.shape[0] // row_count
        for group in range(tile_groups):
            if arrival_order:
                group_total = o_ref.shape[0] // tp_count
                dest = (index_ref[0] + 2 * group_total - group - 1) % group_total
            else:
                dest = group
            for part in range(tp_count):
                o_ref[dest * tp_count + part] = acc_ref[
                    group * row_count : (group + 1) * row_count,
                    part * own_width : (part + 1) * own_width,
                ].astype(o_ref.dtype)


def expert_mix(rows, gate_up, down, req_index, arrival_order, width, block_total, row_count, tp_count):
    row_total, message_width = rows.shape
    local_count, _, _, hidden = gate_up.shape
    group_total = row_total // row_count
    tile_groups = math.gcd(group_total, 8)
    tile = tile_groups * row_count
    own_width = width // tp_count
    gate_up_t = jnp.swapaxes(gate_up, 2, 3)
    body = functools.partial(
        _expert_body,
        width=width,
        block_total=block_total,
        row_count=row_count,
        tp_count=tp_count,
        arrival_order=arrival_order,
    )
    return pl.pallas_call(
        body,
        grid=(group_total // tile_groups, local_count),
        in_specs=[
            pl.BlockSpec(memory_space=pltpu.SMEM),
            pl.BlockSpec((tile, message_width), lambda i, b: (i, 0)),
            pl.BlockSpec((1, 2, hidden, width), lambda i, b: (b, 0, 0, 0)),
            pl.BlockSpec((1, hidden, width), lambda i, b: (b, 0, 0)),
        ],
        out_specs=pl.BlockSpec((tile_groups * tp_count, row_count, own_width), lambda i, b: (i, 0, 0)),
        out_shape=jax.ShapeDtypeStruct((group_total * tp_count, row_count, own_width), jnp.bfloat16),
        scratch_shapes=[pltpu.VMEM((tile, width), jnp.float32)],
        compiler_params=pltpu.CompilerParams(dimension_semantics=("parallel", "arbitrary")),
    )(req_index, rows, gate_up_t, down)


def per_device(
    hidden_in,
    queries,
    fresh_key_value,
    positions,
    lengths,
    cache,
    out_proj,
    norm_gain,
    expert_ids,
    router_weights,
    gate_up,
    down,
):
    tp_count = lax.axis_size("tp")
    req_count = lax.axis_size("req")
    tp_index = lax.axis_index("tp")
    req_index = lax.axis_index("req")
    row_count = hidden_in.shape[0]
    head_size = cache.shape[3]
    kv_count = cache.shape[2]
    own_heads = queries.shape[1] // head_size
    head_count = own_heads * tp_count
    request_group_size = head_count // kv_count
    score_scaling = head_size ** (-0.5)
    model_width = norm_gain.shape[0]
    own_width = hidden_in.shape[1]
    first_head = tp_index * own_heads
    span_rows = cache.shape[0]

    packed = jnp.stack([queries, hidden_in], axis=0)
    gathered = lax.all_gather(packed, "tp", axis=0)
    q_raw = jnp.transpose(gathered[:, 0], (1, 0, 2)).reshape(row_count, head_count, head_size)
    q_all = apply_rotary_heads(q_raw.astype(jnp.float32), positions, head_size).astype(jnp.bfloat16)
    q_all = q_all.reshape(row_count, kv_count, request_group_size, head_size)
    hidden_full = jnp.transpose(gathered[:, 1], (1, 0, 2)).reshape(row_count, model_width)

    k_new = apply_rotary_heads(
        fresh_key_value[:, 0].reshape(row_count, kv_count, head_size).astype(jnp.float32),
        positions,
        head_size,
    ).astype(jnp.bfloat16)
    value_fresh = fresh_key_value[:, 1].reshape(row_count, kv_count, head_size)
    own_score = (
        jnp.einsum("rcgd,rcd->rcg", q_all, k_new, preferred_element_type=jnp.float32)
        * score_scaling
    )

    segment_ends = jnp.cumsum(lengths[0], dtype=jnp.int32)
    segment_starts = segment_ends - lengths[0]
    cache_spots = tp_index * span_rows + jnp.arange(span_rows, dtype=jnp.int32)
    mask = (cache_spots[None, :] >= segment_starts[:, None]) & (
        cache_spots[None, :] < segment_ends[:, None]
    )
    mask = mask[:, None, None, :]
    keys = cache[:, 0]
    values = cache[:, 1]
    scores = (
        jnp.einsum("rcgd,jcd->rcgj", q_all, keys, preferred_element_type=jnp.float32)
        * score_scaling
    )
    scores = jnp.where(mask, scores, neg_floor)
    highest_local = jnp.max(scores, axis=3)
    weights = jnp.where(mask, jnp.exp(scores - highest_local[..., None]), 0.0)
    totals_local = jnp.sum(weights, axis=3)
    sums_local = jnp.einsum(
        "rcgj,jcd->rcgd",
        weights,
        values.astype(jnp.float32),
        precision=lax.Precision.HIGHEST,
        preferred_element_type=jnp.float32,
    )
    sums_heads = sums_local.reshape(row_count, tp_count, own_heads * head_size)
    stats = jnp.concatenate(
        [
            highest_local.reshape(row_count, tp_count, own_heads),
            totals_local.reshape(row_count, tp_count, own_heads),
        ],
        axis=2,
    )
    stats_lanes = -(-stats.shape[2] // 128) * 128
    stats = jnp.pad(stats, ((0, 0), (0, 0), (0, stats_lanes - stats.shape[2])))
    states = jnp.transpose(jnp.concatenate([sums_heads, stats], axis=2), (1, 0, 2))
    own_part_states = lax.dynamic_index_in_dim(states, tp_index, 0, keepdims=False)
    all_states = [own_part_states]
    for shift in range(1, tp_count):
        outgoing = lax.dynamic_index_in_dim(states, (tp_index + shift) % tp_count, 0, keepdims=False)
        all_states.append(
            lax.ppermute(outgoing, "tp", [(i, (i + shift) % tp_count) for i in range(tp_count)])
        )
    all_states = jnp.stack(all_states, axis=0)
    sums_width = own_heads * head_size
    parts_sums = all_states[:, :, :sums_width].reshape(tp_count, row_count, own_heads, head_size)
    parts_highest = all_states[:, :, sums_width : sums_width + own_heads]
    parts_totals = all_states[:, :, sums_width + own_heads : sums_width + 2 * own_heads]
    own_slice = lax.dynamic_slice_in_dim(own_score.reshape(row_count, head_count), first_head, own_heads, 1)
    top_score = jnp.maximum(jnp.max(parts_highest, axis=0), own_slice)
    factors = jnp.exp(parts_highest - top_score[None])
    own_part = jnp.exp(own_slice - top_score)
    if request_group_size % own_heads == 0:
        own_values = lax.dynamic_slice_in_dim(value_fresh, first_head // request_group_size, 1, 1)
        own_values = own_values.astype(jnp.float32)
    else:
        head_kv = (first_head + jnp.arange(own_heads, dtype=jnp.int32)) // request_group_size
        own_values = jnp.take(value_fresh, head_kv, axis=1).astype(jnp.float32)
    totals = jnp.sum(parts_totals * factors, axis=0) + own_part
    summed = jnp.sum(parts_sums * factors[..., None], axis=0) + own_values * own_part[..., None]
    attention_output = (summed / totals[..., None]).astype(jnp.bfloat16).reshape(
        row_count, own_heads * head_size
    )

    partial_proj = jnp.dot(attention_output, out_proj, preferred_element_type=jnp.float32)
    projected = jnp.sum(
        lax.all_gather(partial_proj.astype(jnp.bfloat16), "tp", axis=0).astype(jnp.float32), axis=0
    )
    residual = hidden_full.astype(jnp.float32) + projected
    mean_square = jnp.mean(residual * residual, axis=1, keepdims=True)
    normed = (residual * lax.rsqrt(mean_square + norm_eps) * norm_gain[None, :]).astype(jnp.bfloat16)
    residual_own = lax.dynamic_slice_in_dim(residual, tp_index * own_width, own_width, 1)

    local_count = gate_up.shape[0]
    block_total = local_count * req_count
    split_count = max(1, block_total // EXPERTS)
    expert_range = jnp.arange(EXPERTS, dtype=jnp.int32)
    member = jnp.any(expert_ids[:, :, None] == expert_range[None, None, :], axis=1)
    member_int = member.astype(jnp.int32)
    slot_of = jnp.cumsum(member_int, axis=0, dtype=jnp.int32) - member_int
    slot_taken = jnp.take_along_axis(slot_of, expert_ids, axis=1)
    block_taken = (slot_taken % split_count) * EXPERTS + expert_ids
    block_range = jnp.arange(block_total, dtype=jnp.int32)
    block_weights = jnp.sum(
        jnp.where(block_taken[:, :, None] == block_range[None, None, :], router_weights[:, :, None], 0.0),
        axis=1,
    )

    def gather_req(value):
        if req_count > 8 or 8 % req_count != 0 or req_count % tp_count != 0:
            return lax.all_gather(value, "req", axis=0, tiled=True), False
        per_tp = req_count // tp_count
        fetched = []
        for slot in range(per_tp):
            pairs = []
            for group in range(req_count):
                for part in range(tp_count):
                    shift = per_tp * part + slot + 1
                    source = ((group - shift) % req_count) * tp_count + part
                    pairs.append((source, group * tp_count + part))
            fetched.append(lax.ppermute(value, ("req", "tp"), pairs))
        shared = lax.all_gather(jnp.stack(fetched, axis=0), "tp", axis=0)
        shared = shared.reshape((req_count * value.shape[0],) + value.shape[1:])
        return shared, True

    weight_high = lax.reduce_precision(block_weights, exponent_bits=8, mantissa_bits=7)
    weight_rest = block_weights - weight_high
    weight_mid = lax.reduce_precision(weight_rest, exponent_bits=8, mantissa_bits=7)
    weight_low = weight_rest - weight_mid
    code = jnp.concatenate([weight_high, weight_mid, weight_low], axis=1).astype(jnp.bfloat16)
    code_lanes = -(-code.shape[1] // 128) * 128
    code = jnp.pad(code, ((0, 0), (0, code_lanes - code.shape[1])))
    message = jnp.concatenate([normed, code], axis=1)
    message_all, arrival_order = gather_req(message)
    index_scalar = req_index.astype(jnp.int32).reshape(1)
    mixed = expert_mix(
        message_all, gate_up, down, index_scalar, arrival_order, model_width, block_total, row_count, tp_count
    )
    mixed = lax.all_to_all(mixed, ("req", "tp"), 0, 0, tiled=True)
    mixed = jnp.sum(mixed.astype(jnp.float32), axis=0)
    return (residual_own + mixed).astype(jnp.bfloat16)


def solution(mesh):
    placed = (
        P("req", "tp"),
        P("req", "tp"),
        P("req", None, None),
        P("req"),
        P("req", None),
        P(("req", "tp"), None, None, None),
        P("tp", None),
        P(),
        P("req", None),
        P("req", None),
        P("req", None, None, "tp"),
        P("req", "tp", None),
    )
    return jax.shard_map(
        per_device, mesh=mesh, in_specs=placed, out_specs=P("req", "tp"), check_vma=False
    )
```

```python
import functools
import math

import jax
import jax.numpy as jnp
from jax import lax
from jax.experimental import pallas as pl
from jax.experimental.pallas import tpu as pltpu
from jax.sharding import PartitionSpec as P

EXPERTS = 32


rope_base = 1000000.0
norm_eps = 1e-06
neg_floor = -1e30


def apply_rotary_heads(values, positions, head_size):
    half_size = head_size // 2
    exponents = jnp.arange(half_size, dtype=jnp.float32) * (2.0 / head_size)
    inverse_freq = jnp.power(jnp.float32(rope_base), -exponents)
    angles = positions.astype(jnp.float32)[:, None] * inverse_freq[None, :]
    cosine = jnp.cos(angles)[:, None, :]
    sine = jnp.sin(angles)[:, None, :]
    first_half = values[..., :half_size]
    second_half = values[..., half_size:]
    return jnp.concatenate(
        [first_half * cosine - second_half * sine, second_half * cosine + first_half * sine],
        axis=-1,
    )


def _expert_body(
    index_ref, x_ref, gu_ref, dn_ref, o_ref, acc_ref, *, width, block_total, row_count, tp_count, arrival_order
):
    block = pl.program_id(1)

    @pl.when(block == 0)
    def _():
        acc_ref[...] = jnp.zeros_like(acc_ref)

    x = x_ref[:, :width]
    contract_rows = (((1,), (1,)), ((), ()))
    gate_part = lax.dot_general(x, gu_ref[0, 0], contract_rows, preferred_element_type=jnp.float32)
    up_part = lax.dot_general(x, gu_ref[0, 1], contract_rows, preferred_element_type=jnp.float32)
    activation = (jnp.maximum(gate_part, 0.0) * up_part).astype(jnp.bfloat16)
    produced = jnp.dot(activation, dn_ref[0], preferred_element_type=jnp.float32)
    produced = produced.astype(jnp.bfloat16).astype(jnp.float32)
    code = x_ref[:, width:].astype(jnp.float32)
    lanes = lax.broadcasted_iota(jnp.int32, code.shape, 1)
    local_count = pl.num_programs(1)
    column = index_ref[0] * local_count + block
    chosen = jnp.sum(jnp.where(lanes == column, code, 0.0), axis=1, keepdims=True)
    chosen = chosen + jnp.sum(jnp.where(lanes == column + block_total, code, 0.0), axis=1, keepdims=True)
    chosen = chosen + jnp.sum(jnp.where(lanes == column + 2 * block_total, code, 0.0), axis=1, keepdims=True)
    acc_ref[...] += chosen * produced

    @pl.when(block == pl.num_programs(1) - 1)
    def _():
        own_width = o_ref.shape[2]
        tile_groups = x_ref.shape[0] // row_count
        for group in range(tile_groups):
            if arrival_order:
                group_total = o_ref.shape[0] // tp_count
                per_tp = group_total // tp_count
                source_tp = (index_ref[1] + tp_count - group // per_tp) % tp_count
                message = source_tp * per_tp + group % per_tp
                dest = (index_ref[0] + 2 * group_total - message - 1) % group_total
            else:
                dest = group
            for part in range(tp_count):
                o_ref[dest * tp_count + part] = acc_ref[
                    group * row_count : (group + 1) * row_count,
                    part * own_width : (part + 1) * own_width,
                ].astype(o_ref.dtype)


def expert_mix(rows, gate_up, down, req_index, arrival_order, width, block_total, row_count, tp_count):
    row_total, message_width = rows.shape
    local_count, _, _, hidden = gate_up.shape
    group_total = row_total // row_count
    tile_groups = math.gcd(group_total, 8)
    tile = tile_groups * row_count
    own_width = width // tp_count
    gate_up_t = jnp.swapaxes(gate_up, 2, 3)
    body = functools.partial(
        _expert_body,
        width=width,
        block_total=block_total,
        row_count=row_count,
        tp_count=tp_count,
        arrival_order=arrival_order,
    )
    return pl.pallas_call(
        body,
        grid=(group_total // tile_groups, local_count),
        in_specs=[
            pl.BlockSpec(memory_space=pltpu.SMEM),
            pl.BlockSpec((tile, message_width), lambda i, b: (i, 0)),
            pl.BlockSpec((1, 2, hidden, width), lambda i, b: (b, 0, 0, 0)),
            pl.BlockSpec((1, hidden, width), lambda i, b: (b, 0, 0)),
        ],
        out_specs=pl.BlockSpec((tile_groups * tp_count, row_count, own_width), lambda i, b: (i, 0, 0)),
        out_shape=jax.ShapeDtypeStruct((group_total * tp_count, row_count, own_width), jnp.bfloat16),
        scratch_shapes=[pltpu.VMEM((tile, width), jnp.float32)],
        compiler_params=pltpu.CompilerParams(dimension_semantics=("parallel", "arbitrary")),
    )(req_index, rows, gate_up_t, down)


def per_device(
    hidden_in,
    queries,
    fresh_key_value,
    positions,
    lengths,
    cache,
    out_proj,
    norm_gain,
    expert_ids,
    router_weights,
    gate_up,
    down,
):
    tp_count = lax.axis_size("tp")
    req_count = lax.axis_size("req")
    tp_index = lax.axis_index("tp")
    req_index = lax.axis_index("req")
    row_count = hidden_in.shape[0]
    head_size = cache.shape[3]
    kv_count = cache.shape[2]
    own_heads = queries.shape[1] // head_size
    head_count = own_heads * tp_count
    request_group_size = head_count // kv_count
    score_scaling = head_size ** (-0.5)
    model_width = norm_gain.shape[0]
    own_width = hidden_in.shape[1]
    first_head = tp_index * own_heads
    span_rows = cache.shape[0]

    packed = jnp.stack([queries, hidden_in], axis=0)
    gathered = lax.all_gather(packed, "tp", axis=0)
    q_raw = jnp.transpose(gathered[:, 0], (1, 0, 2)).reshape(row_count, head_count, head_size)
    q_all = apply_rotary_heads(q_raw.astype(jnp.float32), positions, head_size).astype(jnp.bfloat16)
    q_all = q_all.reshape(row_count, kv_count, request_group_size, head_size)
    hidden_full = jnp.transpose(gathered[:, 1], (1, 0, 2)).reshape(row_count, model_width)

    k_new = apply_rotary_heads(
        fresh_key_value[:, 0].reshape(row_count, kv_count, head_size).astype(jnp.float32),
        positions,
        head_size,
    ).astype(jnp.bfloat16)
    value_fresh = fresh_key_value[:, 1].reshape(row_count, kv_count, head_size)
    own_score = (
        jnp.einsum("rcgd,rcd->rcg", q_all, k_new, preferred_element_type=jnp.float32)
        * score_scaling
    )

    segment_ends = jnp.cumsum(lengths[0], dtype=jnp.int32)
    segment_starts = segment_ends - lengths[0]
    cache_spots = tp_index * span_rows + jnp.arange(span_rows, dtype=jnp.int32)
    mask = (cache_spots[None, :] >= segment_starts[:, None]) & (
        cache_spots[None, :] < segment_ends[:, None]
    )
    mask = mask[:, None, None, :]
    keys = cache[:, 0]
    values = cache[:, 1]
    scores = (
        jnp.einsum("rcgd,jcd->rcgj", q_all, keys, preferred_element_type=jnp.float32)
        * score_scaling
    )
    scores = jnp.where(mask, scores, neg_floor)
    highest_local = jnp.max(scores, axis=3)
    weights = jnp.where(mask, jnp.exp(scores - highest_local[..., None]), 0.0)
    totals_local = jnp.sum(weights, axis=3)
    sums_local = jnp.einsum(
        "rcgj,jcd->rcgd",
        weights,
        values.astype(jnp.float32),
        precision=lax.Precision.HIGHEST,
        preferred_element_type=jnp.float32,
    )
    sums_heads = sums_local.reshape(row_count, tp_count, own_heads * head_size)
    stats = jnp.concatenate(
        [
            highest_local.reshape(row_count, tp_count, own_heads),
            totals_local.reshape(row_count, tp_count, own_heads),
        ],
        axis=2,
    )
    stats_lanes = -(-stats.shape[2] // 128) * 128
    stats = jnp.pad(stats, ((0, 0), (0, 0), (0, stats_lanes - stats.shape[2])))
    states = jnp.transpose(jnp.concatenate([sums_heads, stats], axis=2), (1, 0, 2))
    own_part_states = lax.dynamic_index_in_dim(states, tp_index, 0, keepdims=False)
    all_states = [own_part_states]
    for shift in range(1, tp_count):
        outgoing = lax.dynamic_index_in_dim(states, (tp_index + shift) % tp_count, 0, keepdims=False)
        all_states.append(
            lax.ppermute(outgoing, "tp", [(i, (i + shift) % tp_count) for i in range(tp_count)])
        )
    all_states = jnp.stack(all_states, axis=0)
    sums_width = own_heads * head_size
    parts_sums = all_states[:, :, :sums_width].reshape(tp_count, row_count, own_heads, head_size)
    parts_highest = all_states[:, :, sums_width : sums_width + own_heads]
    parts_totals = all_states[:, :, sums_width + own_heads : sums_width + 2 * own_heads]
    own_slice = lax.dynamic_slice_in_dim(own_score.reshape(row_count, head_count), first_head, own_heads, 1)
    top_score = jnp.maximum(jnp.max(parts_highest, axis=0), own_slice)
    factors = jnp.exp(parts_highest - top_score[None])
    own_part = jnp.exp(own_slice - top_score)
    if request_group_size % own_heads == 0:
        own_values = lax.dynamic_slice_in_dim(value_fresh, first_head // request_group_size, 1, 1)
        own_values = own_values.astype(jnp.float32)
    else:
        head_kv = (first_head + jnp.arange(own_heads, dtype=jnp.int32)) // request_group_size
        own_values = jnp.take(value_fresh, head_kv, axis=1).astype(jnp.float32)
    totals = jnp.sum(parts_totals * factors, axis=0) + own_part
    summed = jnp.sum(parts_sums * factors[..., None], axis=0) + own_values * own_part[..., None]
    attention_output = (summed / totals[..., None]).astype(jnp.bfloat16).reshape(
        row_count, own_heads * head_size
    )

    partial_proj = jnp.dot(attention_output, out_proj, preferred_element_type=jnp.float32)
    projected = jnp.sum(
        lax.all_gather(partial_proj.astype(jnp.bfloat16), "tp", axis=0).astype(jnp.float32), axis=0
    )
    residual = hidden_full.astype(jnp.float32) + projected
    mean_square = jnp.mean(residual * residual, axis=1, keepdims=True)
    normed = (residual * lax.rsqrt(mean_square + norm_eps) * norm_gain[None, :]).astype(jnp.bfloat16)
    residual_own = lax.dynamic_slice_in_dim(residual, tp_index * own_width, own_width, 1)

    local_count = gate_up.shape[0]
    block_total = local_count * req_count
    split_count = max(1, block_total // EXPERTS)
    expert_range = jnp.arange(EXPERTS, dtype=jnp.int32)
    member = jnp.any(expert_ids[:, :, None] == expert_range[None, None, :], axis=1)
    member_int = member.astype(jnp.int32)
    slot_of = jnp.cumsum(member_int, axis=0, dtype=jnp.int32) - member_int
    slot_taken = jnp.take_along_axis(slot_of, expert_ids, axis=1)
    block_taken = (slot_taken % split_count) * EXPERTS + expert_ids
    block_range = jnp.arange(block_total, dtype=jnp.int32)
    block_weights = jnp.sum(
        jnp.where(block_taken[:, :, None] == block_range[None, None, :], router_weights[:, :, None], 0.0),
        axis=1,
    )

    def gather_req(value):
        if req_count > 8 or 8 % req_count != 0 or req_count % tp_count != 0:
            return lax.all_gather(value, "req", axis=0, tiled=True), False
        per_tp = req_count // tp_count
        fetched = []
        for slot in range(per_tp):
            pairs = []
            for group in range(req_count):
                for part in range(tp_count):
                    shift = per_tp * part + slot + 1
                    source = ((group - shift) % req_count) * tp_count + part
                    pairs.append((source, group * tp_count + part))
            fetched.append(lax.ppermute(value, ("req", "tp"), pairs))
        fetched = jnp.stack(fetched, axis=0)
        shared = [fetched] + [
            lax.ppermute(fetched, "tp", [(i, (i + shift) % tp_count) for i in range(tp_count)])
            for shift in range(1, tp_count)
        ]
        shared = jnp.stack(shared, axis=0)
        shared = shared.reshape((req_count * value.shape[0],) + value.shape[1:])
        return shared, True

    weight_high = lax.reduce_precision(block_weights, exponent_bits=8, mantissa_bits=7)
    weight_rest = block_weights - weight_high
    weight_mid = lax.reduce_precision(weight_rest, exponent_bits=8, mantissa_bits=7)
    weight_low = weight_rest - weight_mid
    code = jnp.concatenate([weight_high, weight_mid, weight_low], axis=1).astype(jnp.bfloat16)
    code_lanes = -(-code.shape[1] // 128) * 128
    code = jnp.pad(code, ((0, 0), (0, code_lanes - code.shape[1])))
    message = jnp.concatenate([normed, code], axis=1)
    message_all, arrival_order = gather_req(message)
    index_scalar = jnp.stack([req_index, tp_index]).astype(jnp.int32)
    mixed = expert_mix(
        message_all, gate_up, down, index_scalar, arrival_order, model_width, block_total, row_count, tp_count
    )
    mixed = lax.all_to_all(mixed, ("req", "tp"), 0, 0, tiled=True)
    mixed = jnp.sum(mixed.astype(jnp.float32), axis=0)
    return (residual_own + mixed).astype(jnp.bfloat16)


def solution(mesh):
    placed = (
        P("req", "tp"),
        P("req", "tp"),
        P("req", None, None),
        P("req"),
        P("req", None),
        P(("req", "tp"), None, None, None),
        P("tp", None),
        P(),
        P("req", None),
        P("req", None),
        P("req", None, None, "tp"),
        P("req", "tp", None),
    )
    return jax.shard_map(
        per_device, mesh=mesh, in_specs=placed, out_specs=P("req", "tp"), check_vma=False
    )
```

```python
import functools
import math

import jax
import jax.numpy as jnp
from jax import lax
from jax.experimental import pallas as pl
from jax.experimental.pallas import tpu as pltpu
from jax.sharding import PartitionSpec as P

EXPERTS = 32


rope_base = 1000000.0
norm_eps = 1e-06
neg_floor = -1e30


def apply_rotary_heads(values, positions, head_size):
    half_size = head_size // 2
    exponents = jnp.arange(half_size, dtype=jnp.float32) * (2.0 / head_size)
    inverse_freq = jnp.power(jnp.float32(rope_base), -exponents)
    angles = positions.astype(jnp.float32)[:, None] * inverse_freq[None, :]
    cosine = jnp.cos(angles)[:, None, :]
    sine = jnp.sin(angles)[:, None, :]
    first_half = values[..., :half_size]
    second_half = values[..., half_size:]
    return jnp.concatenate(
        [first_half * cosine - second_half * sine, second_half * cosine + first_half * sine],
        axis=-1,
    )


def _expert_body(
    index_ref, x_ref, gu_ref, dn_ref, o_ref, acc_ref, *, width, block_total, row_count, tp_count, arrival_order
):
    block = pl.program_id(1)

    @pl.when(block == 0)
    def _():
        acc_ref[...] = jnp.zeros_like(acc_ref)

    x = x_ref[:, :width]
    contract_rows = (((1,), (1,)), ((), ()))
    gate_part = lax.dot_general(x, gu_ref[0, 0], contract_rows, preferred_element_type=jnp.float32)
    up_part = lax.dot_general(x, gu_ref[0, 1], contract_rows, preferred_element_type=jnp.float32)
    activation = (jnp.maximum(gate_part, 0.0) * up_part).astype(jnp.bfloat16)
    produced = jnp.dot(activation, dn_ref[0], preferred_element_type=jnp.float32)
    produced = produced.astype(jnp.bfloat16).astype(jnp.float32)
    code = x_ref[:, width:].astype(jnp.float32)
    lanes = lax.broadcasted_iota(jnp.int32, code.shape, 1)
    local_count = pl.num_programs(1)
    column = index_ref[0] * local_count + block
    chosen = jnp.sum(jnp.where(lanes == column, code, 0.0), axis=1, keepdims=True)
    chosen = chosen + jnp.sum(jnp.where(lanes == column + block_total, code, 0.0), axis=1, keepdims=True)
    chosen = chosen + jnp.sum(jnp.where(lanes == column + 2 * block_total, code, 0.0), axis=1, keepdims=True)
    acc_ref[...] += chosen * produced

    @pl.when(block == pl.num_programs(1) - 1)
    def _():
        own_width = o_ref.shape[2]
        tile_groups = x_ref.shape[0] // row_count
        for group in range(tile_groups):
            if arrival_order:
                group_total = o_ref.shape[0] // tp_count
                per_tp = group_total // tp_count
                shift = (group % per_tp) * tp_count + group // per_tp + 1
                dest = (index_ref[0] + 2 * group_total - shift) % group_total
            else:
                dest = group
            for part in range(tp_count):
                o_ref[dest * tp_count + part] = acc_ref[
                    group * row_count : (group + 1) * row_count,
                    part * own_width : (part + 1) * own_width,
                ].astype(o_ref.dtype)


def expert_mix(rows, gate_up, down, req_index, arrival_order, width, block_total, row_count, tp_count):
    row_total, message_width = rows.shape
    local_count, _, _, hidden = gate_up.shape
    group_total = row_total // row_count
    tile_groups = math.gcd(group_total, 8)
    tile = tile_groups * row_count
    own_width = width // tp_count
    gate_up_t = jnp.swapaxes(gate_up, 2, 3)
    body = functools.partial(
        _expert_body,
        width=width,
        block_total=block_total,
        row_count=row_count,
        tp_count=tp_count,
        arrival_order=arrival_order,
    )
    return pl.pallas_call(
        body,
        grid=(group_total // tile_groups, local_count),
        in_specs=[
            pl.BlockSpec(memory_space=pltpu.SMEM),
            pl.BlockSpec((tile, message_width), lambda i, b: (i, 0)),
            pl.BlockSpec((1, 2, hidden, width), lambda i, b: (b, 0, 0, 0)),
            pl.BlockSpec((1, hidden, width), lambda i, b: (b, 0, 0)),
        ],
        out_specs=pl.BlockSpec((tile_groups * tp_count, row_count, own_width), lambda i, b: (i, 0, 0)),
        out_shape=jax.ShapeDtypeStruct((group_total * tp_count, row_count, own_width), jnp.bfloat16),
        scratch_shapes=[pltpu.VMEM((tile, width), jnp.float32)],
        compiler_params=pltpu.CompilerParams(dimension_semantics=("parallel", "arbitrary")),
    )(req_index, rows, gate_up_t, down)


def per_device(
    hidden_in,
    queries,
    fresh_key_value,
    positions,
    lengths,
    cache,
    out_proj,
    norm_gain,
    expert_ids,
    router_weights,
    gate_up,
    down,
):
    tp_count = lax.axis_size("tp")
    req_count = lax.axis_size("req")
    tp_index = lax.axis_index("tp")
    req_index = lax.axis_index("req")
    row_count = hidden_in.shape[0]
    head_size = cache.shape[3]
    kv_count = cache.shape[2]
    own_heads = queries.shape[1] // head_size
    head_count = own_heads * tp_count
    request_group_size = head_count // kv_count
    score_scaling = head_size ** (-0.5)
    model_width = norm_gain.shape[0]
    own_width = hidden_in.shape[1]
    first_head = tp_index * own_heads
    span_rows = cache.shape[0]

    packed = jnp.stack([queries, hidden_in], axis=0)
    gathered = lax.all_gather(packed, "tp", axis=0)
    q_raw = jnp.transpose(gathered[:, 0], (1, 0, 2)).reshape(row_count, head_count, head_size)
    q_all = apply_rotary_heads(q_raw.astype(jnp.float32), positions, head_size).astype(jnp.bfloat16)
    q_all = q_all.reshape(row_count, kv_count, request_group_size, head_size)
    hidden_full = jnp.transpose(gathered[:, 1], (1, 0, 2)).reshape(row_count, model_width)

    k_new = apply_rotary_heads(
        fresh_key_value[:, 0].reshape(row_count, kv_count, head_size).astype(jnp.float32),
        positions,
        head_size,
    ).astype(jnp.bfloat16)
    value_fresh = fresh_key_value[:, 1].reshape(row_count, kv_count, head_size)
    own_score = (
        jnp.einsum("rcgd,rcd->rcg", q_all, k_new, preferred_element_type=jnp.float32)
        * score_scaling
    )

    segment_ends = jnp.cumsum(lengths[0], dtype=jnp.int32)
    segment_starts = segment_ends - lengths[0]
    cache_spots = tp_index * span_rows + jnp.arange(span_rows, dtype=jnp.int32)
    mask = (cache_spots[None, :] >= segment_starts[:, None]) & (
        cache_spots[None, :] < segment_ends[:, None]
    )
    mask = mask[:, None, None, :]
    keys = cache[:, 0]
    values = cache[:, 1]
    scores = (
        jnp.einsum("rcgd,jcd->rcgj", q_all, keys, preferred_element_type=jnp.float32)
        * score_scaling
    )
    scores = jnp.where(mask, scores, neg_floor)
    highest_local = jnp.max(scores, axis=3)
    weights = jnp.where(mask, jnp.exp(scores - highest_local[..., None]), 0.0)
    totals_local = jnp.sum(weights, axis=3)
    sums_local = jnp.einsum(
        "rcgj,jcd->rcgd",
        weights,
        values.astype(jnp.float32),
        precision=lax.Precision.HIGHEST,
        preferred_element_type=jnp.float32,
    )
    sums_heads = sums_local.reshape(row_count, tp_count, own_heads * head_size)
    stats = jnp.concatenate(
        [
            highest_local.reshape(row_count, tp_count, own_heads),
            totals_local.reshape(row_count, tp_count, own_heads),
        ],
        axis=2,
    )
    stats_lanes = -(-stats.shape[2] // 128) * 128
    stats = jnp.pad(stats, ((0, 0), (0, 0), (0, stats_lanes - stats.shape[2])))
    states = jnp.transpose(jnp.concatenate([sums_heads, stats], axis=2), (1, 0, 2))
    own_part_states = lax.dynamic_index_in_dim(states, tp_index, 0, keepdims=False)
    all_states = [own_part_states]
    for shift in range(1, tp_count):
        outgoing = lax.dynamic_index_in_dim(states, (tp_index + shift) % tp_count, 0, keepdims=False)
        all_states.append(
            lax.ppermute(outgoing, "tp", [(i, (i + shift) % tp_count) for i in range(tp_count)])
        )
    all_states = jnp.stack(all_states, axis=0)
    sums_width = own_heads * head_size
    parts_sums = all_states[:, :, :sums_width].reshape(tp_count, row_count, own_heads, head_size)
    parts_highest = all_states[:, :, sums_width : sums_width + own_heads]
    parts_totals = all_states[:, :, sums_width + own_heads : sums_width + 2 * own_heads]
    own_slice = lax.dynamic_slice_in_dim(own_score.reshape(row_count, head_count), first_head, own_heads, 1)
    top_score = jnp.maximum(jnp.max(parts_highest, axis=0), own_slice)
    factors = jnp.exp(parts_highest - top_score[None])
    own_part = jnp.exp(own_slice - top_score)
    if request_group_size % own_heads == 0:
        own_values = lax.dynamic_slice_in_dim(value_fresh, first_head // request_group_size, 1, 1)
        own_values = own_values.astype(jnp.float32)
    else:
        head_kv = (first_head + jnp.arange(own_heads, dtype=jnp.int32)) // request_group_size
        own_values = jnp.take(value_fresh, head_kv, axis=1).astype(jnp.float32)
    totals = jnp.sum(parts_totals * factors, axis=0) + own_part
    summed = jnp.sum(parts_sums * factors[..., None], axis=0) + own_values * own_part[..., None]
    attention_output = (summed / totals[..., None]).astype(jnp.bfloat16).reshape(
        row_count, own_heads * head_size
    )

    partial_proj = jnp.dot(attention_output, out_proj, preferred_element_type=jnp.float32)
    projected = jnp.sum(
        lax.all_gather(partial_proj.astype(jnp.bfloat16), "tp", axis=0).astype(jnp.float32), axis=0
    )
    residual = hidden_full.astype(jnp.float32) + projected
    mean_square = jnp.mean(residual * residual, axis=1, keepdims=True)
    normed = (residual * lax.rsqrt(mean_square + norm_eps) * norm_gain[None, :]).astype(jnp.bfloat16)
    residual_own = lax.dynamic_slice_in_dim(residual, tp_index * own_width, own_width, 1)

    local_count = gate_up.shape[0]
    block_total = local_count * req_count
    split_count = max(1, block_total // EXPERTS)
    expert_range = jnp.arange(EXPERTS, dtype=jnp.int32)
    member = jnp.any(expert_ids[:, :, None] == expert_range[None, None, :], axis=1)
    member_int = member.astype(jnp.int32)
    slot_of = jnp.cumsum(member_int, axis=0, dtype=jnp.int32) - member_int
    slot_taken = jnp.take_along_axis(slot_of, expert_ids, axis=1)
    block_taken = (slot_taken % split_count) * EXPERTS + expert_ids
    block_range = jnp.arange(block_total, dtype=jnp.int32)
    block_weights = jnp.sum(
        jnp.where(block_taken[:, :, None] == block_range[None, None, :], router_weights[:, :, None], 0.0),
        axis=1,
    )

    def gather_req(value):
        if req_count > 8 or 8 % req_count != 0 or req_count % tp_count != 0:
            return lax.all_gather(value, "req", axis=0, tiled=True), False
        per_tp = req_count // tp_count
        fetched = []
        for slot in range(per_tp):
            pairs = []
            for group in range(req_count):
                for part in range(tp_count):
                    shift = slot * tp_count + part + 1
                    source = ((group - shift) % req_count) * tp_count + part
                    pairs.append((source, group * tp_count + part))
            fetched.append(lax.ppermute(value, ("req", "tp"), pairs))
        shared = lax.all_gather(jnp.stack(fetched, axis=0), "tp", axis=0)
        shared = shared.reshape((req_count * value.shape[0],) + value.shape[1:])
        return shared, True

    weight_high = lax.reduce_precision(block_weights, exponent_bits=8, mantissa_bits=7)
    weight_rest = block_weights - weight_high
    weight_mid = lax.reduce_precision(weight_rest, exponent_bits=8, mantissa_bits=7)
    weight_low = weight_rest - weight_mid
    code = jnp.concatenate([weight_high, weight_mid, weight_low], axis=1).astype(jnp.bfloat16)
    code_lanes = -(-code.shape[1] // 128) * 128
    code = jnp.pad(code, ((0, 0), (0, code_lanes - code.shape[1])))
    message = jnp.concatenate([normed, code], axis=1)
    message_all, arrival_order = gather_req(message)
    index_scalar = req_index.astype(jnp.int32).reshape(1)
    mixed = expert_mix(
        message_all, gate_up, down, index_scalar, arrival_order, model_width, block_total, row_count, tp_count
    )
    mixed = lax.all_to_all(mixed, ("req", "tp"), 0, 0, tiled=True)
    mixed = jnp.sum(mixed.astype(jnp.float32), axis=0)
    return (residual_own + mixed).astype(jnp.bfloat16)


def solution(mesh):
    placed = (
        P("req", "tp"),
        P("req", "tp"),
        P("req", None, None),
        P("req"),
        P("req", None),
        P(("req", "tp"), None, None, None),
        P("tp", None),
        P(),
        P("req", None),
        P("req", None),
        P("req", None, None, "tp"),
        P("req", "tp", None),
    )
    return jax.shard_map(
        per_device, mesh=mesh, in_specs=placed, out_specs=P("req", "tp"), check_vma=False
    )
```
